32 devices in a mesh: groups: 2 (over x), seq: 8 (over z, y), exp: 2 (over core).
Axes of the slice: x: 2, y: 2, z: 4, core: 2. Of those that a mesh axis runs over, the one named last changes fastest.
Arguments:
- queries: bfloat16 [4096, 2048], P(('groups', 'seq'), 'exp'), parts along dimension 0, may hold values from -400 to 400
- key_rows: bfloat16 [4096, 256], P(('groups', 'seq'), 'exp'), parts along dimension 0, may hold values from -4 to 4
- values: bfloat16 [4096, 256], P(('groups', 'seq'), 'exp'), parts along dimension 0, may hold values from -4 to 4
- cached_rows: bfloat16 [2, 256, 256], P(None, 'groups', 'exp'), parts along dimension 1, may hold values from -4 to 4
- sink_logits: float32 [32], P('exp'), may hold values from 1 to 5
- out_weight: bfloat16 [2048, 1536], P('exp'), may hold values from -0.375 to 0.375
- residual: bfloat16 [4096, 1536], P(('groups', 'seq')), parts along dimension 0, may hold values from -45 to 45
- norm_gain: float32 [1536], replicated, may hold values from 0.5 to 1.5
- expert_in: bfloat16 [8, 2, 1536, 1536], P('seq', None, None, 'exp'), may hold values from -0.15625 to 0.15625
- expert_out: bfloat16 [8, 1536, 1536], P('seq', 'exp'), may hold values from -0.15625 to 0.15625
- routes: int32 [4096, 4], P(('groups', 'seq')), parts along dimension 0, may hold values from 0 to 7, all different within a row; in each aligned block of 256 rows (0 to 255, 256 to 511, ...) at most 192 rows name the same one
- route_gates: float32 [4096, 4], P(('groups', 'seq')), parts along dimension 0, may hold values from 0.1 to 1
Outputs:
- layer_out: bfloat16 [4096, 1536], P(('groups', 'seq')), parts along dimension 0
The draws below stay inside these ranges and needn't reach their ends.
There are 2 independent parts, one for each index of `groups`. The reference program is written for one: setup_inputs(seed, part) draws one part's arguments, and reference() takes and returns one part's arrays. A program takes and returns all parts, laid end to end along the dimension named above; an argument that names none is the same for every part. Nothing has to cross between parts.
Inputs may be any that keep to these rules, and one draw needn't show every extreme that they name: `routes`: within the rows of one index of seq, each expert is named by at most 192 rows, and in every draw some expert is named by exactly 192 rows of some such block.
All inputs are finite; a program needn't handle non-finite values.
Results may differ from the reference program's by a relative error of at most 0.008.
Values may be sent and summed in bfloat16 or wider, within the bound.
No kernel may reach another device: no remote copies, remote signals or barrier semaphores. Data moves between devices by JAX's collectives and lax.ppermute only.
A program may use at most 128 MiB of HBM per device.

```python
import math
import jax
import jax.numpy as jnp
import numpy as np
from jax import lax

TOK_DEV = 256
D = 1536
FF = 1536
HEADS = 32
KV_HEADS = 4
HEAD_DIM = 64
WINDOW = 128
TOP = 4
EXPERTS = 8
CAP = 192
TOKENS = 2048
N_SEQ = 8
N_EXP = 2


def key_field(key):
    base = jax.random.normal(jax.random.fold_in(key, 17), (TOKENS, KV_HEADS * HEAD_DIM), jnp.float32)
    return jnp.clip(base, -4.0, 4.0)


def draw_key_rows(key, part):
    field = key_field(key)
    return field.astype(jnp.bfloat16)


def draw_queries(key, part):
    base = jnp.clip(jax.random.normal(jax.random.fold_in(key, 23), (TOKENS, HEADS * HEAD_DIM), jnp.float32), -4.0, 4.0)
    return base.astype(jnp.bfloat16)


def draw_residual(key, part):
    row_scale = 0.3 * jnp.exp(jax.random.uniform(jax.random.fold_in(key, 31), (TOKENS, 1), jnp.float32, 0.0, 2.302585))
    column_scale = 0.3 * jnp.exp(jax.random.uniform(jax.random.fold_in(key, 37), (1, D), jnp.float32, 0.0, 2.302585))
    base = jnp.clip(jax.random.normal(jax.random.fold_in(key, 43), (TOKENS, D), jnp.float32), -4.0, 4.0)
    return (base * row_scale * column_scale).astype(jnp.bfloat16)


def level_of(rng, extent, pieces, low, top_value):
    def one(dim, blocks):
        steps = jax.random.uniform(jax.random.fold_in(jax.random.fold_in(rng, 6), dim), (blocks,), jnp.float32, low / len(pieces), top_value / len(pieces))
        return jnp.repeat(jnp.exp(steps), extent[dim] // blocks).reshape((-1,) + (1,) * (len(extent) - dim - 1))

    loudness = one(*pieces[0])
    for cut in pieces[1:]:
        loudness = loudness * one(*cut)
    return loudness


def shared_out(stream_key, own, number, rows, count, top, most, lean):
    sequence = jax.random.permutation(stream_key, count)
    heavy_load, usual = load_shares(count, rows * top, most, lean, True), load_shares(count, rows * top, most, lean, False)
    places = jnp.arange(count)

    def named(lengths, offset_by):
        used = int((lengths > 0).sum())
        fixed = max(1, used // 4)
        moved = fixed + (places - fixed + offset_by * (used - fixed)) % max(1, count - fixed)
        return jnp.zeros((count,), jnp.int32).at[sequence[jnp.where(places < fixed, places, moved)]].set(jnp.asarray(lengths, jnp.int32))

    lengths = jnp.where(number % 4 == 0, named(heavy_load, number // 4), named(usual, number - number // 4 - 1))
    mixed = jax.random.permutation(jax.random.fold_in(own, 3), count)
    donor, taker = mixed[0:count // 2 * 2:2], mixed[1:count // 2 * 2:2]
    margin = jnp.minimum(lengths[donor] - 1, most - lengths[taker]) // 2
    margin = jnp.where((donor == sequence[0]) | (taker == sequence[0]) | (lengths[taker] == 0), 0, jnp.maximum(margin, 0))
    moved = jax.random.randint(jax.random.fold_in(own, 4), (count // 2,), 0, 1 << 20) % (margin + 1)
    lengths = lengths.at[donor].add(-moved).at[taker].add(moved)
    members = jnp.searchsorted(jnp.cumsum(lengths), jnp.arange(rows * top), side="right").astype(jnp.int32)
    grid = members.reshape(top, rows).T
    grid = grid[jax.random.permutation(jax.random.fold_in(own, 1), rows)]
    offset_by = jax.random.randint(jax.random.fold_in(own, 2), (rows, 1), 0, top)
    return jnp.take_along_axis(grid, (jnp.arange(top)[None, :] + offset_by) % top, axis=1)


def load_shares(count, total, reach, skew, full):
    weights = [(1 << 20) // math.isqrt(grade ** skew) + 1 for grade in range(1, count + 1)]
    largest = reach if full else min(reach, max(-(-total // count), total * weights[0] // sum(weights)))
    least = 1 if total - largest >= count - 1 else 0
    counts, spare = [largest] + [least] * (count - 1), total - largest - least * (count - 1)
    while spare > 0:
        free = [i for i in range(1, count) if counts[i] < largest] or [i for i in range(1, count) if counts[i] < reach]
        mass, budget = sum([weights[i] for i in free]), spare
        for i in free:
            extra = min(reach - counts[i], max(1, budget * weights[i] // mass), spare)
            counts[i] = counts[i] + extra
            spare = spare - extra
    return np.array(counts)


def scatter_about(key, extent, scale, limit, split=(), kind=jnp.bfloat16):
    factor_of = level_of(key, extent, split, -0.22, 0.18) if split else 1.0
    array = jax.random.normal(key, extent, jnp.float32) * scale * factor_of
    return jnp.minimum(jnp.maximum(array, -limit), limit).astype(kind)


def setup_inputs(seed: int = 0, part: int = 0) -> dict:
    streams_of = jax.random.split(jax.random.key(seed), 13)
    own_keys = jax.random.split(jax.random.fold_in(streams_of[12], part), 13)
    queries = draw_queries(jax.random.fold_in(jax.random.fold_in(streams_of[12], part), 71), part)
    key_rows = draw_key_rows(jax.random.fold_in(jax.random.fold_in(streams_of[12], part), 71), part)
    values = scatter_about(own_keys[2], (TOKENS, KV_HEADS * HEAD_DIM), 1.0, 4.0, ((0, 8), (1, 2)))
    cached_rows = scatter_about(own_keys[3], (2, WINDOW, KV_HEADS * HEAD_DIM), 1.0, 4.0, ((2, 2),))
    sink_logits = jnp.clip(1.0 + 4.0 * jax.random.uniform(streams_of[4], (HEADS,), jnp.float32) ** level_of(streams_of[4], (HEADS,), ((0, 2),), -0.2, 0.2), 1.0, 5.0)
    out_weight = scatter_about(streams_of[5], (HEADS * HEAD_DIM, D), (HEADS * HEAD_DIM // 8) ** -0.5, 0.375, ((0, 2),))
    residual = draw_residual(jax.random.fold_in(jax.random.fold_in(streams_of[12], part), 71), part)
    norm_gain = jnp.clip(1.0 + 0.1 * jax.random.normal(streams_of[7], (D,), jnp.float32), 0.5, 1.5)
    expert_in = scatter_about(streams_of[8], (EXPERTS, 2, D, FF), D ** -0.5, 0.15625, ((0, 8), (3, 2)))
    expert_out = scatter_about(streams_of[9], (EXPERTS, FF, D), FF ** -0.5, 0.15625, ((0, 8), (1, 2)))
    routes_keys = jax.random.split(jax.random.fold_in(own_keys[10], 1), TOKENS // TOK_DEV)
    routes_turns = jax.random.permutation(jax.random.fold_in(own_keys[10], 3), TOKENS // TOK_DEV)
    routes = jax.vmap(lambda own, number: shared_out(jax.random.fold_in(own_keys[10], 2), own, number, TOK_DEV, EXPERTS, TOP, CAP, 2))(routes_keys, routes_turns).reshape((TOKENS, TOP))
    route_gates = jnp.clip(jnp.exp(math.log(1.0) - 2.3025851 * jax.random.uniform(own_keys[11], (TOKENS, TOP), jnp.float32) ** level_of(own_keys[11], (TOKENS, TOP), ((0, 8),), -0.2, 0.2)), 0.1, 1.0)
    return {"queries": queries, "key_rows": key_rows, "values": values, "cached_rows": cached_rows, "sink_logits": sink_logits, "out_weight": out_weight, "residual": residual, "norm_gain": norm_gain, "expert_in": expert_in, "expert_out": expert_out, "routes": routes, "route_gates": route_gates}


GLU_ALPHA = 1.702
EPSILON = 1e-05

def rms_normalize(mixed_rows, norm_gain):
    mean_square = lax.optimization_barrier(jnp.mean(mixed_rows * mixed_rows, axis=-1, keepdims=True))
    return (mixed_rows * lax.rsqrt(mean_square + EPSILON) * norm_gain).astype(jnp.bfloat16)

def reference(queries, key_rows, values, cached_rows, sink_logits, out_weight, residual, norm_gain, expert_in, expert_out, routes, route_gates):
    group = HEADS // KV_HEADS
    keys_all = jnp.concatenate([cached_rows[0], key_rows], axis=0)
    values_all = jnp.concatenate([cached_rows[1], values], axis=0)
    block_count = TOKENS // WINDOW
    query_blocks = queries.reshape(block_count, WINDOW, KV_HEADS, group, HEAD_DIM)
    sink_table = sink_logits.reshape(KV_HEADS, group)[:, :, None]
    query_pos = jnp.arange(WINDOW)[:, None]
    key_pos = jnp.arange(2 * WINDOW)[None, :]
    allowed = (key_pos > query_pos) & (key_pos <= query_pos + WINDOW)

    def attend(block_id):
        first_key = (block_id * WINDOW).astype(jnp.int32)
        key_block = lax.dynamic_slice_in_dim(keys_all, first_key, 2 * WINDOW, 0).reshape(2 * WINDOW, KV_HEADS, HEAD_DIM)
        value_block = lax.dynamic_slice_in_dim(values_all, first_key, 2 * WINDOW, 0).reshape(2 * WINDOW, KV_HEADS, HEAD_DIM)
        query_block = lax.dynamic_index_in_dim(query_blocks, block_id, 0, keepdims=False)
        scores = jnp.einsum('qhgd,khd->hgqk', query_block.astype(jnp.float32), key_block.astype(jnp.float32)) * HEAD_DIM ** (-0.5)
        scores = jnp.where(allowed, scores, -jnp.inf)
        largest = jnp.maximum(lax.optimization_barrier(jnp.max(scores, axis=-1)), sink_table)
        weights_exp = jnp.exp(scores - largest[..., None])
        denominator = jnp.exp(sink_table - largest) + lax.optimization_barrier(jnp.sum(weights_exp, axis=-1))
        probs = (weights_exp / denominator[..., None]).astype(jnp.bfloat16)
        heads_out = jnp.einsum('hgqk,khd->qhgd', probs.astype(jnp.float32), value_block.astype(jnp.float32))
        return heads_out.astype(jnp.bfloat16).reshape(WINDOW, HEADS * HEAD_DIM)
    attended = lax.map(attend, jnp.arange(block_count, dtype=jnp.int32)).reshape(TOKENS, HEADS * HEAD_DIM)
    mixed_rows = residual.astype(jnp.float32) + jnp.dot(attended, out_weight, preferred_element_type=jnp.float32)
    normed = rms_normalize(mixed_rows, norm_gain)
    assigned = TOKENS * TOP
    flat_experts = routes.reshape(-1).astype(jnp.int32)
    token_index = (jnp.arange(assigned, dtype=jnp.int32) // TOP).astype(jnp.int32)
    block_index = (token_index // TOK_DEV).astype(jnp.int32)
    expert_hits = (flat_experts[:, None] == jnp.arange(EXPERTS, dtype=jnp.int32)[None, :]).astype(jnp.int32)
    running = jnp.cumsum(expert_hits.reshape(N_SEQ, TOK_DEV * TOP, EXPERTS), axis=1).reshape(assigned, EXPERTS)
    slot_rank = lax.optimization_barrier(jnp.sum(expert_hits * (running - 1), axis=1)).astype(jnp.int32)
    slot_index = (block_index * CAP + slot_rank).astype(jnp.int32)
    table = jnp.full((EXPERTS, N_SEQ * CAP), TOKENS, jnp.int32).at[flat_experts, slot_index].set(token_index)
    gate_table = jnp.zeros((EXPERTS, N_SEQ * CAP), jnp.float32).at[flat_experts, slot_index].set(route_gates.reshape(-1))
    normed_padded = jnp.concatenate([normed, jnp.zeros((1, D), jnp.bfloat16)], axis=0)
    half_units = FF // N_EXP

    def serve(accumulated, expert_id):
        slot_tokens = table[expert_id]
        slot_rows = normed_padded[slot_tokens]
        gate_up = jnp.einsum('rd,kdf->krf', slot_rows.astype(jnp.float32), expert_in[expert_id].astype(jnp.float32))
        gate_val = gate_up[0]
        up_val = gate_up[1]
        activation = ((up_val + 1.0) * gate_val * jax.nn.sigmoid(GLU_ALPHA * gate_val)).astype(jnp.bfloat16)
        expert_result = jnp.zeros((N_SEQ * CAP, D), jnp.float32)
        for core_half in range(N_EXP):
            part_sum = jnp.dot(activation[:, core_half * half_units:(core_half + 1) * half_units], expert_out[expert_id, core_half * half_units:(core_half + 1) * half_units], preferred_element_type=jnp.float32)
            expert_result = expert_result + lax.optimization_barrier(part_sum.astype(jnp.bfloat16)).astype(jnp.float32)
        accumulated = accumulated.at[slot_tokens].add(gate_table[expert_id][:, None] * expert_result)
        return (accumulated, None)
    moe_sum, unused = lax.scan(serve, jnp.zeros((TOKENS + 1, D), jnp.float32), jnp.arange(EXPERTS, dtype=jnp.int32))
    return (mixed_rows + moe_sum[:TOKENS]).astype(jnp.bfloat16)
```

```python
import jax
import jax.numpy as jnp
from jax import lax
from jax.sharding import PartitionSpec as P

HEAD_DIM = 64
WINDOW = 128
TOP = 4


GLU_ALPHA = 1.702
EPSILON = 1e-05


def shifted(shard, axis, by):
    size = lax.axis_size(axis)
    pairs = [(i, i + by) for i in range(size) if 0 <= i + by < size]
    return lax.ppermute(shard, axis, pairs)


def swap_exp(x):
    size = lax.axis_size("exp")
    return lax.ppermute(x, "exp", [(i, (i + 1) % size) for i in range(size)])


def rms_normalize(mixed_rows, norm_gain):
    mean_square = jnp.mean(mixed_rows * mixed_rows, axis=-1, keepdims=True)
    return (mixed_rows * lax.rsqrt(mean_square + EPSILON) * norm_gain).astype(jnp.bfloat16)


def attend_block(queries, keys_all, values_all, sink_logits, block_rows, window_rows):
    kv_count = keys_all.shape[1] // HEAD_DIM
    group = queries.shape[1] // HEAD_DIM // kv_count
    query_block = queries.reshape(block_rows, kv_count, group, HEAD_DIM)
    key_block = keys_all.reshape(block_rows + window_rows, kv_count, HEAD_DIM)
    value_block = values_all.reshape(block_rows + window_rows, kv_count, HEAD_DIM)
    scores = jnp.einsum(
        "qhgd,khd->hgqk", query_block, key_block, preferred_element_type=jnp.float32
    ) * HEAD_DIM ** (-0.5)
    query_pos = jnp.arange(block_rows)[:, None]
    key_pos = jnp.arange(block_rows + window_rows)[None, :]
    allowed = (key_pos > query_pos) & (key_pos <= query_pos + window_rows)
    scores = jnp.where(allowed, scores, -jnp.inf)
    sink_table = sink_logits.reshape(kv_count, group)[:, :, None]
    largest = jnp.maximum(jnp.max(scores, axis=-1), sink_table)
    weights_exp = jnp.exp(scores - largest[..., None])
    denominator = jnp.exp(sink_table - largest) + jnp.sum(weights_exp, axis=-1)
    probs = (weights_exp / denominator[..., None]).astype(jnp.bfloat16)
    heads_out = jnp.einsum("hgqk,khd->qhgd", probs, value_block, preferred_element_type=jnp.float32)
    return heads_out.astype(jnp.bfloat16).reshape(block_rows, queries.shape[1])


def on_device(
    queries,
    key_rows,
    values,
    cached_rows,
    sink_logits,
    out_weight,
    residual,
    norm_gain,
    expert_in,
    expert_out,
    routes,
    route_gates,
):
    tok_rows = queries.shape[0]
    window_rows = WINDOW
    rim_rows = jnp.stack([key_rows[tok_rows - window_rows :], values[tok_rows - window_rows :]])
    received = shifted(rim_rows, "seq", 1)
    prior = jnp.where(lax.axis_index("seq") == 0, cached_rows, received)
    keys_all = jnp.concatenate([prior[0], key_rows], axis=0)
    values_all = jnp.concatenate([prior[1], values], axis=0)
    block_rows = min(tok_rows, 512)
    pieces = attend_block(queries, keys_all, values_all, sink_logits, block_rows, window_rows)
    partial_rows = jnp.dot(pieces, out_weight, preferred_element_type=jnp.float32)
    mixed_rows = residual.astype(jnp.float32) + (partial_rows + swap_exp(partial_rows))
    normed = rms_normalize(mixed_rows, norm_gain)

    experts = lax.axis_size("seq")
    width = normed.shape[1]
    capacity = 3 * tok_rows * TOP // (2 * experts)
    half = -(-capacity // 2)
    slots = experts * half
    core = lax.axis_index("exp")
    flat_experts = routes.reshape(-1)
    expert_hits = (flat_experts[:, None] == jnp.arange(experts, dtype=jnp.int32)[None, :]).astype(
        jnp.int32
    )
    slot_rank = jnp.sum(expert_hits * (jnp.cumsum(expert_hits, axis=0) - 1), axis=1)
    local_rank = slot_rank - core * half
    mine = (local_rank >= 0) & (local_rank < half)
    slot_id = jnp.where(mine, flat_experts * half + local_rank, -1)
    slot_iota = jnp.arange(slots, dtype=jnp.int32)
    pick = (slot_id[:, None] == slot_iota[None, :]).astype(jnp.bfloat16)
    select = jnp.max(pick.reshape(tok_rows, TOP, slots), axis=1).T
    outgoing = (
        jnp.dot(select, normed, preferred_element_type=jnp.float32)
        .astype(jnp.bfloat16)
        .reshape(experts, half, width)
    )
    slot_rows = lax.all_to_all(outgoing, "seq", split_axis=0, concat_axis=0, tiled=True)
    both_rows = jnp.concatenate([slot_rows, swap_exp(slot_rows)], axis=1)
    flat_rows = both_rows.reshape(-1, width)
    gate_up = jnp.einsum("rd,kdf->krf", flat_rows, expert_in[0], preferred_element_type=jnp.float32)
    gate_val = gate_up[0]
    up_val = gate_up[1]
    activation = ((up_val + 1.0) * gate_val * jax.nn.sigmoid(GLU_ALPHA * gate_val)).astype(
        jnp.bfloat16
    )
    out_part = (
        jnp.dot(activation, expert_out[0], preferred_element_type=jnp.float32)
        .astype(jnp.bfloat16)
        .reshape(experts, 2 * half, width)
    )
    own_part = out_part[:, :half]
    their_part = swap_exp(out_part[:, half:])
    result = (own_part.astype(jnp.float32) + their_part.astype(jnp.float32)).astype(jnp.bfloat16)
    returned = lax.all_to_all(result, "seq", split_axis=0, concat_axis=0, tiled=True)
    picked = jnp.dot(pick, returned.reshape(slots, width), preferred_element_type=jnp.float32)
    weighted = jnp.sum(picked.reshape(tok_rows, TOP, width) * route_gates[:, :, None], axis=1)
    moe = weighted + swap_exp(weighted)
    return (mixed_rows + moe).astype(jnp.bfloat16)


def solution(mesh):
    placed = (
        P(("groups", "seq"), "exp"),
        P(("groups", "seq"), "exp"),
        P(("groups", "seq"), "exp"),
        P(None, "groups", "exp"),
        P("exp"),
        P("exp", None),
        P(("groups", "seq"), None),
        P(),
        P("seq", None, None, "exp"),
        P("seq", "exp", None),
        P(("groups", "seq"), None),
        P(("groups", "seq"), None),
    )
    return jax.shard_map(
        on_device, mesh=mesh, in_specs=placed, out_specs=P(("groups", "seq"), None), check_vma=False
    )
```

```python
import jax
import jax.numpy as jnp
from jax import lax
from jax.sharding import PartitionSpec as P

HEAD_DIM = 64
WINDOW = 128
TOP = 4


GLU_ALPHA = 1.702
EPSILON = 1e-05


def shifted(shard, axis, by):
    size = lax.axis_size(axis)
    pairs = [(i, i + by) for i in range(size) if 0 <= i + by < size]
    return lax.ppermute(shard, axis, pairs)


def swap_exp(x):
    size = lax.axis_size("exp")
    return lax.ppermute(x, "exp", [(i, (i + 1) % size) for i in range(size)])


def rms_normalize(mixed_rows, norm_gain):
    mean_square = jnp.mean(mixed_rows * mixed_rows, axis=-1, keepdims=True)
    return (mixed_rows * lax.rsqrt(mean_square + EPSILON) * norm_gain).astype(jnp.bfloat16)


def attend_block(queries, keys_all, values_all, sink_logits, block_rows, window_rows):
    kv_count = keys_all.shape[1] // HEAD_DIM
    group = queries.shape[1] // HEAD_DIM // kv_count
    query_block = queries.reshape(block_rows, kv_count, group, HEAD_DIM)
    key_block = keys_all.reshape(block_rows + window_rows, kv_count, HEAD_DIM)
    value_block = values_all.reshape(block_rows + window_rows, kv_count, HEAD_DIM)
    scores = jnp.einsum(
        "qhgd,khd->hgqk", query_block, key_block, preferred_element_type=jnp.float32
    ) * HEAD_DIM ** (-0.5)
    query_pos = jnp.arange(block_rows)[:, None]
    key_pos = jnp.arange(block_rows + window_rows)[None, :]
    allowed = (key_pos > query_pos) & (key_pos <= query_pos + window_rows)
    scores = jnp.where(allowed, scores, -jnp.inf)
    sink_table = sink_logits.reshape(kv_count, group)[:, :, None]
    largest = jnp.maximum(jnp.max(scores, axis=-1), sink_table)
    weights_exp = jnp.exp(scores - largest[..., None])
    denominator = jnp.exp(sink_table - largest) + jnp.sum(weights_exp, axis=-1)
    probs = (weights_exp / denominator[..., None]).astype(jnp.bfloat16)
    heads_out = jnp.einsum("hgqk,khd->qhgd", probs, value_block, preferred_element_type=jnp.float32)
    return heads_out.astype(jnp.bfloat16).reshape(block_rows, queries.shape[1])


def gathered_slots(normed, routes, core, half, experts):
    tok_rows, width = normed.shape
    cores = lax.axis_size("exp")
    share = tok_rows // cores
    own_rows = lax.dynamic_slice_in_dim(normed, core * share, share, 0)
    tokens = lax.all_gather(own_rows, ("seq", "exp"), axis=0, tiled=True).reshape(
        experts, tok_rows, width
    )
    all_routes = lax.all_gather(routes, "seq", axis=0, tiled=False)
    expert = lax.axis_index("seq")
    has = jnp.any(all_routes == expert, axis=-1)
    rank = jnp.cumsum(has.astype(jnp.int32), axis=1) - 1
    rank_order = (jnp.arange(2 * half, dtype=jnp.int32) + core * half) % (2 * half)
    select = (has[:, None, :] & (rank[:, None, :] == rank_order[None, :, None])).astype(jnp.bfloat16)
    return jnp.einsum(
        "bst,btd->bsd", select, tokens, preferred_element_type=jnp.float32
    ).astype(jnp.bfloat16)


def on_device(
    queries,
    key_rows,
    values,
    cached_rows,
    sink_logits,
    out_weight,
    residual,
    norm_gain,
    expert_in,
    expert_out,
    routes,
    route_gates,
):
    tok_rows = queries.shape[0]
    window_rows = WINDOW
    rim_rows = jnp.stack([key_rows[tok_rows - window_rows :], values[tok_rows - window_rows :]])
    received = shifted(rim_rows, "seq", 1)
    prior = jnp.where(lax.axis_index("seq") == 0, cached_rows, received)
    keys_all = jnp.concatenate([prior[0], key_rows], axis=0)
    values_all = jnp.concatenate([prior[1], values], axis=0)
    block_rows = min(tok_rows, 512)
    pieces = attend_block(queries, keys_all, values_all, sink_logits, block_rows, window_rows)
    partial_rows = jnp.dot(pieces, out_weight, preferred_element_type=jnp.float32)
    mixed_rows = residual.astype(jnp.float32) + (partial_rows + swap_exp(partial_rows))
    normed = rms_normalize(mixed_rows, norm_gain)

    experts = lax.axis_size("seq")
    width = normed.shape[1]
    capacity = 3 * tok_rows * TOP // (2 * experts)
    half = -(-capacity // 2)
    slots = experts * half
    core = lax.axis_index("exp")
    flat_experts = routes.reshape(-1)
    expert_hits = (flat_experts[:, None] == jnp.arange(experts, dtype=jnp.int32)[None, :]).astype(
        jnp.int32
    )
    slot_rank = jnp.sum(expert_hits * (jnp.cumsum(expert_hits, axis=0) - 1), axis=1)
    local_rank = slot_rank - core * half
    mine = (local_rank >= 0) & (local_rank < half)
    slot_id = jnp.where(mine, flat_experts * half + local_rank, -1)
    slot_iota = jnp.arange(slots, dtype=jnp.int32)
    pick = (slot_id[:, None] == slot_iota[None, :]).astype(jnp.bfloat16)
    if tok_rows <= 2 * capacity:
        both_rows = gathered_slots(normed, routes, core, half, experts)
    else:
        select = jnp.max(pick.reshape(tok_rows, TOP, slots), axis=1).T
        outgoing = (
            jnp.dot(select, normed, preferred_element_type=jnp.float32)
            .astype(jnp.bfloat16)
            .reshape(experts, half, width)
        )
        slot_rows = lax.all_to_all(outgoing, "seq", split_axis=0, concat_axis=0, tiled=True)
        both_rows = jnp.concatenate([slot_rows, swap_exp(slot_rows)], axis=1)
    flat_rows = both_rows.reshape(-1, width)
    gate_up = jnp.einsum("rd,kdf->krf", flat_rows, expert_in[0], preferred_element_type=jnp.float32)
    gate_val = gate_up[0]
    up_val = gate_up[1]
    activation = ((up_val + 1.0) * gate_val * jax.nn.sigmoid(GLU_ALPHA * gate_val)).astype(
        jnp.bfloat16
    )
    out_part = (
        jnp.dot(activation, expert_out[0], preferred_element_type=jnp.float32)
        .astype(jnp.bfloat16)
        .reshape(experts, 2 * half, width)
    )
    own_part = out_part[:, :half]
    their_part = swap_exp(out_part[:, half:])
    result = (own_part.astype(jnp.float32) + their_part.astype(jnp.float32)).astype(jnp.bfloat16)
    returned = lax.all_to_all(result, "seq", split_axis=0, concat_axis=0, tiled=True)
    picked = jnp.dot(pick, returned.reshape(slots, width), preferred_element_type=jnp.float32)
    weighted = jnp.sum(picked.reshape(tok_rows, TOP, width) * route_gates[:, :, None], axis=1)
    moe = weighted + swap_exp(weighted)
    return (mixed_rows + moe).astype(jnp.bfloat16)


def solution(mesh):
    placed = (
        P(("groups", "seq"), "exp"),
        P(("groups", "seq"), "exp"),
        P(("groups", "seq"), "exp"),
        P(None, "groups", "exp"),
        P("exp"),
        P("exp", None),
        P(("groups", "seq"), None),
        P(),
        P("seq", None, None, "exp"),
        P("seq", "exp", None),
        P(("groups", "seq"), None),
        P(("groups", "seq"), None),
    )
    return jax.shard_map(
        on_device, mesh=mesh, in_specs=placed, out_specs=P(("groups", "seq"), None), check_vma=False
    )
```

```python
import jax
import jax.numpy as jnp
from jax import lax
from jax.sharding import PartitionSpec as P

HEAD_DIM = 64
WINDOW = 128
TOP = 4


GLU_ALPHA = 1.702
EPSILON = 1e-05


def shifted(shard, axis, by):
    size = lax.axis_size(axis)
    pairs = [(i, i + by) for i in range(size) if 0 <= i + by < size]
    return lax.ppermute(shard, axis, pairs)


def swap_exp(x):
    size = lax.axis_size("exp")
    return lax.ppermute(x, "exp", [(i, (i + 1) % size) for i in range(size)])


def rms_normalize(mixed_rows, norm_gain):
    mean_square = jnp.mean(mixed_rows * mixed_rows, axis=-1, keepdims=True)
    return (mixed_rows * lax.rsqrt(mean_square + EPSILON) * norm_gain).astype(jnp.bfloat16)


def attend_block(queries, keys_all, values_all, sink_logits, block_rows, window_rows):
    kv_count = keys_all.shape[1] // HEAD_DIM
    group = queries.shape[1] // HEAD_DIM // kv_count
    query_block = queries.reshape(block_rows, kv_count, group, HEAD_DIM)
    key_block = keys_all.reshape(block_rows + window_rows, kv_count, HEAD_DIM)
    value_block = values_all.reshape(block_rows + window_rows, kv_count, HEAD_DIM)
    scores = jnp.einsum(
        "qhgd,khd->hgqk", query_block, key_block, preferred_element_type=jnp.float32
    ) * HEAD_DIM ** (-0.5)
    query_pos = jnp.arange(block_rows)[:, None]
    key_pos = jnp.arange(block_rows + window_rows)[None, :]
    allowed = (key_pos > query_pos) & (key_pos <= query_pos + window_rows)
    scores = jnp.where(allowed, scores, -jnp.inf)
    sink_table = sink_logits.reshape(kv_count, group)[:, :, None]
    largest = jnp.maximum(jnp.max(scores, axis=-1), sink_table)
    weights_exp = jnp.exp(scores - largest[..., None])
    denominator = jnp.exp(sink_table - largest) + jnp.sum(weights_exp, axis=-1)
    probs = (weights_exp / denominator[..., None]).astype(jnp.bfloat16)
    heads_out = jnp.einsum("hgqk,khd->qhgd", probs, value_block, preferred_element_type=jnp.float32)
    return heads_out.astype(jnp.bfloat16).reshape(block_rows, queries.shape[1])


def expert_hidden(rows, expert_in):
    gate_up = jnp.einsum("rd,kdf->krf", rows, expert_in, preferred_element_type=jnp.float32)
    gate_val = gate_up[0]
    up_val = gate_up[1]
    return ((up_val + 1.0) * gate_val * jax.nn.sigmoid(GLU_ALPHA * gate_val)).astype(jnp.bfloat16)


def on_device(
    queries,
    key_rows,
    values,
    cached_rows,
    sink_logits,
    out_weight,
    residual,
    norm_gain,
    expert_in,
    expert_out,
    routes,
    route_gates,
):
    tok_rows = queries.shape[0]
    window_rows = WINDOW
    rim_rows = jnp.stack([key_rows[tok_rows - window_rows :], values[tok_rows - window_rows :]])
    received = shifted(rim_rows, "seq", 1)
    prior = jnp.where(lax.axis_index("seq") == 0, cached_rows, received)
    keys_all = jnp.concatenate([prior[0], key_rows], axis=0)
    values_all = jnp.concatenate([prior[1], values], axis=0)
    block_rows = min(tok_rows, 512)
    pieces = attend_block(queries, keys_all, values_all, sink_logits, block_rows, window_rows)
    partial_rows = jnp.dot(pieces, out_weight, preferred_element_type=jnp.float32)
    mixed_rows = residual.astype(jnp.float32) + (partial_rows + swap_exp(partial_rows))
    normed = rms_normalize(mixed_rows, norm_gain)

    experts = lax.axis_size("seq")
    width = normed.shape[1]
    capacity = 3 * tok_rows * TOP // (2 * experts)
    half = -(-capacity // 2)
    slots = experts * half
    core = lax.axis_index("exp")
    flat_experts = routes.reshape(-1)
    expert_hits = (flat_experts[:, None] == jnp.arange(experts, dtype=jnp.int32)[None, :]).astype(
        jnp.int32
    )
    slot_rank = jnp.sum(expert_hits * (jnp.cumsum(expert_hits, axis=0) - 1), axis=1)
    local_rank = slot_rank - core * half
    mine = (local_rank >= 0) & (local_rank < half)
    slot_id = jnp.where(mine, flat_experts * half + local_rank, -1)
    slot_iota = jnp.arange(slots, dtype=jnp.int32)
    pick = (slot_id[:, None] == slot_iota[None, :]).astype(jnp.bfloat16)
    select = jnp.max(pick.reshape(tok_rows, TOP, slots), axis=1).T
    outgoing = (
        jnp.dot(select, normed, preferred_element_type=jnp.float32)
        .astype(jnp.bfloat16)
        .reshape(experts, half, width)
    )
    slot_rows = lax.all_to_all(outgoing, "seq", split_axis=0, concat_axis=0, tiled=True)
    other_rows = swap_exp(slot_rows)
    own_hidden = expert_hidden(slot_rows.reshape(-1, width), expert_in[0])
    own_hidden, other_rows = lax.optimization_barrier((own_hidden, other_rows))
    other_hidden = expert_hidden(other_rows.reshape(-1, width), expert_in[0])
    their_part = swap_exp(
        jnp.dot(other_hidden, expert_out[0], preferred_element_type=jnp.float32)
        .astype(jnp.bfloat16)
        .reshape(experts, half, width)
    )
    own_part = (
        jnp.dot(own_hidden, expert_out[0], preferred_element_type=jnp.float32)
        .astype(jnp.bfloat16)
        .reshape(experts, half, width)
    )
    result = (own_part.astype(jnp.float32) + their_part.astype(jnp.float32)).astype(jnp.bfloat16)
    returned = lax.all_to_all(result, "seq", split_axis=0, concat_axis=0, tiled=True)
    picked = jnp.dot(pick, returned.reshape(slots, width), preferred_element_type=jnp.float32)
    weighted = jnp.sum(picked.reshape(tok_rows, TOP, width) * route_gates[:, :, None], axis=1)
    moe = weighted + swap_exp(weighted)
    return (mixed_rows + moe).astype(jnp.bfloat16)


def solution(mesh):
    placed = (
        P(("groups", "seq"), "exp"),
        P(("groups", "seq"), "exp"),
        P(("groups", "seq"), "exp"),
        P(None, "groups", "exp"),
        P("exp"),
        P("exp", None),
        P(("groups", "seq"), None),
        P(),
        P("seq", None, None, "exp"),
        P("seq", "exp", None),
        P(("groups", "seq"), None),
        P(("groups", "seq"), None),
    )
    return jax.shard_map(
        on_device, mesh=mesh, in_specs=placed, out_specs=P(("groups", "seq"), None), check_vma=False
    )
```

```python
import jax
import jax.numpy as jnp
from jax import lax
from jax.sharding import PartitionSpec as P

HEAD_DIM = 64
WINDOW = 128
TOP = 4
CHUNKS = 2


GLU_ALPHA = 1.702
EPSILON = 1e-05


def shifted(shard, axis, by):
    size = lax.axis_size(axis)
    pairs = [(i, i + by) for i in range(size) if 0 <= i + by < size]
    return lax.ppermute(shard, axis, pairs)


def swap_exp(x):
    size = lax.axis_size("exp")
    return lax.ppermute(x, "exp", [(i, (i + 1) % size) for i in range(size)])


def rms_normalize(mixed_rows, norm_gain):
    mean_square = jnp.mean(mixed_rows * mixed_rows, axis=-1, keepdims=True)
    return (mixed_rows * lax.rsqrt(mean_square + EPSILON) * norm_gain).astype(jnp.bfloat16)


def attend_block(queries, keys_all, values_all, sink_logits, block_rows, window_rows):
    kv_count = keys_all.shape[1] // HEAD_DIM
    group = queries.shape[1] // HEAD_DIM // kv_count
    query_block = queries.reshape(block_rows, kv_count, group, HEAD_DIM)
    key_block = keys_all.reshape(block_rows + window_rows, kv_count, HEAD_DIM)
    value_block = values_all.reshape(block_rows + window_rows, kv_count, HEAD_DIM)
    scores = jnp.einsum(
        "qhgd,khd->hgqk", query_block, key_block, preferred_element_type=jnp.float32
    ) * HEAD_DIM ** (-0.5)
    query_pos = jnp.arange(block_rows)[:, None]
    key_pos = jnp.arange(block_rows + window_rows)[None, :]
    allowed = (key_pos > query_pos) & (key_pos <= query_pos + window_rows)
    scores = jnp.where(allowed, scores, -jnp.inf)
    sink_table = sink_logits.reshape(kv_count, group)[:, :, None]
    largest = jnp.maximum(jnp.max(scores, axis=-1), sink_table)
    weights_exp = jnp.exp(scores - largest[..., None])
    denominator = jnp.exp(sink_table - largest) + jnp.sum(weights_exp, axis=-1)
    probs = (weights_exp / denominator[..., None]).astype(jnp.bfloat16)
    heads_out = jnp.einsum("hgqk,khd->qhgd", probs, value_block, preferred_element_type=jnp.float32)
    return heads_out.astype(jnp.bfloat16).reshape(block_rows, queries.shape[1])


def expert_hidden(rows, expert_in):
    gate_up = jnp.einsum("rd,kdf->krf", rows, expert_in, preferred_element_type=jnp.float32)
    gate_val = gate_up[0]
    up_val = gate_up[1]
    return ((up_val + 1.0) * gate_val * jax.nn.sigmoid(GLU_ALPHA * gate_val)).astype(jnp.bfloat16)


def serve_rows(slot_rows, expert_in, expert_out):
    blocks, piece, width = slot_rows.shape
    other_rows = swap_exp(slot_rows)
    own_hidden = expert_hidden(slot_rows.reshape(-1, width), expert_in)
    own_hidden, other_rows = lax.optimization_barrier((own_hidden, other_rows))
    other_hidden = expert_hidden(other_rows.reshape(-1, width), expert_in)
    their_part = swap_exp(
        jnp.dot(other_hidden, expert_out, preferred_element_type=jnp.float32)
        .astype(jnp.bfloat16)
        .reshape(blocks, piece, width)
    )
    own_part = (
        jnp.dot(own_hidden, expert_out, preferred_element_type=jnp.float32)
        .astype(jnp.bfloat16)
        .reshape(blocks, piece, width)
    )
    return (own_part.astype(jnp.float32) + their_part.astype(jnp.float32)).astype(jnp.bfloat16)


def on_device(
    queries,
    key_rows,
    values,
    cached_rows,
    sink_logits,
    out_weight,
    residual,
    norm_gain,
    expert_in,
    expert_out,
    routes,
    route_gates,
):
    tok_rows = queries.shape[0]
    window_rows = WINDOW
    rim_rows = jnp.stack([key_rows[tok_rows - window_rows :], values[tok_rows - window_rows :]])
    received = shifted(rim_rows, "seq", 1)
    prior = jnp.where(lax.axis_index("seq") == 0, cached_rows, received)
    keys_all = jnp.concatenate([prior[0], key_rows], axis=0)
    values_all = jnp.concatenate([prior[1], values], axis=0)
    block_rows = min(tok_rows, 512)
    pieces = attend_block(queries, keys_all, values_all, sink_logits, block_rows, window_rows)
    partial_rows = jnp.dot(pieces, out_weight, preferred_element_type=jnp.float32)
    mixed_rows = residual.astype(jnp.float32) + (partial_rows + swap_exp(partial_rows))
    normed = rms_normalize(mixed_rows, norm_gain)

    experts = lax.axis_size("seq")
    width = normed.shape[1]
    capacity = 3 * tok_rows * TOP // (2 * experts)
    half = -(-capacity // 2)
    slots = experts * half
    core = lax.axis_index("exp")
    flat_experts = routes.reshape(-1)
    expert_hits = (flat_experts[:, None] == jnp.arange(experts, dtype=jnp.int32)[None, :]).astype(
        jnp.int32
    )
    slot_rank = jnp.sum(expert_hits * (jnp.cumsum(expert_hits, axis=0) - 1), axis=1)
    local_rank = slot_rank - core * half
    mine = (local_rank >= 0) & (local_rank < half)
    slot_id = jnp.where(mine, flat_experts * half + local_rank, -1)
    slot_iota = jnp.arange(slots, dtype=jnp.int32)
    pick = (slot_id[:, None] == slot_iota[None, :]).astype(jnp.bfloat16)
    select = jnp.max(pick.reshape(tok_rows, TOP, slots), axis=1).T
    outgoing = (
        jnp.dot(select, normed, preferred_element_type=jnp.float32)
        .astype(jnp.bfloat16)
        .reshape(experts, half, width)
    )
    chunks = CHUNKS if half % CHUNKS == 0 else 1
    piece = half // CHUNKS if chunks == CHUNKS else half
    arrived = [
        lax.all_to_all(
            outgoing[:, q * piece : (q + 1) * piece], "seq", split_axis=0, concat_axis=0, tiled=True
        )
        for q in range(chunks)
    ]
    results = []
    served = None
    for q in range(chunks):
        slot_rows = arrived[q]
        if served is not None:
            slot_rows, served = lax.optimization_barrier((slot_rows, served))
        served = serve_rows(slot_rows, expert_in[0], expert_out[0])
        results.append(lax.all_to_all(served, "seq", split_axis=0, concat_axis=0, tiled=True))
    returned = jnp.concatenate(results, axis=1)
    picked = jnp.dot(pick, returned.reshape(slots, width), preferred_element_type=jnp.float32)
    weighted = jnp.sum(picked.reshape(tok_rows, TOP, width) * route_gates[:, :, None], axis=1)
    moe = weighted + swap_exp(weighted)
    return (mixed_rows + moe).astype(jnp.bfloat16)


def solution(mesh):
    placed = (
        P(("groups", "seq"), "exp"),
        P(("groups", "seq"), "exp"),
        P(("groups", "seq"), "exp"),
        P(None, "groups", "exp"),
        P("exp"),
        P("exp", None),
        P(("groups", "seq"), None),
        P(),
        P("seq", None, None, "exp"),
        P("seq", "exp", None),
        P(("groups", "seq"), None),
        P(("groups", "seq"), None),
    )
    return jax.shard_map(
        on_device, mesh=mesh, in_specs=placed, out_specs=P(("groups", "seq"), None), check_vma=False
    )
```

```python
import jax
import jax.numpy as jnp
from jax import lax
from jax.experimental import pallas as pl
from jax.experimental.pallas import tpu as pltpu
from jax.sharding import PartitionSpec as P

HEAD_DIM = 64
WINDOW = 128
TOP = 4


GLU_ALPHA = 1.702
EPSILON = 1e-05


def shifted(shard, axis, by):
    size = lax.axis_size(axis)
    pairs = [(i, i + by) for i in range(size) if 0 <= i + by < size]
    return lax.ppermute(shard, axis, pairs)


def swap_exp(x):
    size = lax.axis_size("exp")
    return lax.ppermute(x, "exp", [(i, (i + 1) % size) for i in range(size)])


def rms_normalize(mixed_rows, norm_gain):
    mean_square = jnp.mean(mixed_rows * mixed_rows, axis=-1, keepdims=True)
    return (mixed_rows * lax.rsqrt(mean_square + EPSILON) * norm_gain).astype(jnp.bfloat16)


def attend_block(queries, keys_all, values_all, sink_logits, block_rows, window_rows):
    kv_count = keys_all.shape[1] // HEAD_DIM
    group = queries.shape[1] // HEAD_DIM // kv_count
    query_block = queries.reshape(block_rows, kv_count, group, HEAD_DIM)
    key_block = keys_all.reshape(block_rows + window_rows, kv_count, HEAD_DIM)
    value_block = values_all.reshape(block_rows + window_rows, kv_count, HEAD_DIM)
    scores = jnp.einsum(
        "qhgd,khd->hgqk", query_block, key_block, preferred_element_type=jnp.float32
    ) * HEAD_DIM ** (-0.5)
    query_pos = jnp.arange(block_rows)[:, None]
    key_pos = jnp.arange(block_rows + window_rows)[None, :]
    allowed = (key_pos > query_pos) & (key_pos <= query_pos + window_rows)
    scores = jnp.where(allowed, scores, -jnp.inf)
    sink_table = sink_logits.reshape(kv_count, group)[:, :, None]
    largest = jnp.maximum(jnp.max(scores, axis=-1), sink_table)
    weights_exp = jnp.exp(scores - largest[..., None])
    denominator = jnp.exp(sink_table - largest) + jnp.sum(weights_exp, axis=-1)
    probs = (weights_exp / denominator[..., None]).astype(jnp.bfloat16)
    heads_out = jnp.einsum("hgqk,khd->qhgd", probs, value_block, preferred_element_type=jnp.float32)
    return heads_out.astype(jnp.bfloat16).reshape(block_rows, queries.shape[1])


def expert_hidden(rows, expert_in):
    gate_up = jnp.einsum("rd,kdf->krf", rows, expert_in, preferred_element_type=jnp.float32)
    gate_val = gate_up[0]
    up_val = gate_up[1]
    return ((up_val + 1.0) * gate_val * jax.nn.sigmoid(GLU_ALPHA * gate_val)).astype(jnp.bfloat16)


def attention_kernel(sink_ref, q_ref, k_ref, v_ref, o_ref):
    rows = q_ref.shape[0]
    keys = k_ref.shape[2]
    pair_cols = 2 * HEAD_DIM
    pairs = q_ref.shape[1] // pair_cols
    per_kv = pairs // k_ref.shape[0]
    q_pos = lax.broadcasted_iota(jnp.int32, (rows, keys), 0)
    k_pos = lax.broadcasted_iota(jnp.int32, (rows, keys), 1)
    allowed = (k_pos > q_pos) & (k_pos <= q_pos + WINDOW)
    for j in range(pairs):
        kv = j // per_kv
        q_pair = q_ref[:, j * pair_cols : (j + 1) * pair_cols]
        total = None
        for a in range(2):
            scores = lax.dot_general(
                q_pair, k_ref[kv, a], (((1,), (1,)), ((), ())), preferred_element_type=jnp.float32
            ) * HEAD_DIM ** (-0.5)
            scores = jnp.where(allowed, scores, -jnp.inf)
            sink = sink_ref[2 * j + a]
            largest = jnp.maximum(jnp.max(scores, axis=-1, keepdims=True), sink)
            weights_exp = jnp.exp(scores - largest)
            denominator = jnp.exp(sink - largest) + jnp.sum(weights_exp, axis=-1, keepdims=True)
            probs = (weights_exp / denominator).astype(jnp.bfloat16)
            out = jnp.dot(probs, v_ref[kv, a], preferred_element_type=jnp.float32)
            total = out if total is None else total + out
        o_ref[:, j * pair_cols : (j + 1) * pair_cols] = total.astype(o_ref.dtype)


def placed_heads(rows_all):
    keys, cols = rows_all.shape
    kv_count = cols // HEAD_DIM
    zeros = jnp.zeros((keys, HEAD_DIM), rows_all.dtype)
    out = []
    for kv in range(kv_count):
        head = rows_all[:, kv * HEAD_DIM : (kv + 1) * HEAD_DIM]
        out.append(jnp.stack([jnp.concatenate([head, zeros], 1), jnp.concatenate([zeros, head], 1)]))
    return jnp.stack(out)


def attend_kernel(queries, keys_all, values_all, sink_logits):
    rows, cols = queries.shape
    keys = keys_all.shape[0]
    heads = cols // HEAD_DIM
    cost = pl.CostEstimate(
        flops=4 * 2 * rows * keys * 2 * HEAD_DIM * heads,
        transcendentals=rows * keys * heads,
        bytes_accessed=2 * rows * cols * 2 + 2 * 2 * keys_all.size * 2 * 2,
    )
    return pl.pallas_call(
        attention_kernel,
        out_shape=jax.ShapeDtypeStruct((rows, cols), jnp.bfloat16),
        in_specs=[
            pl.BlockSpec(memory_space=pltpu.SMEM),
            pl.BlockSpec(memory_space=pltpu.VMEM),
            pl.BlockSpec(memory_space=pltpu.VMEM),
            pl.BlockSpec(memory_space=pltpu.VMEM),
        ],
        out_specs=pl.BlockSpec(memory_space=pltpu.VMEM),
        cost_estimate=cost,
    )(sink_logits, queries, placed_heads(keys_all), placed_heads(values_all))


def on_device(
    queries,
    key_rows,
    values,
    cached_rows,
    sink_logits,
    out_weight,
    residual,
    norm_gain,
    expert_in,
    expert_out,
    routes,
    route_gates,
):
    tok_rows = queries.shape[0]
    window_rows = WINDOW
    rim_rows = jnp.stack([key_rows[tok_rows - window_rows :], values[tok_rows - window_rows :]])
    received = shifted(rim_rows, "seq", 1)
    prior = jnp.where(lax.axis_index("seq") == 0, cached_rows, received)
    keys_all = jnp.concatenate([prior[0], key_rows], axis=0)
    values_all = jnp.concatenate([prior[1], values], axis=0)
    pieces = attend_kernel(queries, keys_all, values_all, sink_logits)
    partial_rows = jnp.dot(pieces, out_weight, preferred_element_type=jnp.float32)
    mixed_rows = residual.astype(jnp.float32) + (partial_rows + swap_exp(partial_rows))
    normed = rms_normalize(mixed_rows, norm_gain)

    experts = lax.axis_size("seq")
    width = normed.shape[1]
    capacity = 3 * tok_rows * TOP // (2 * experts)
    half = -(-capacity // 2)
    slots = experts * half
    core = lax.axis_index("exp")
    flat_experts = routes.reshape(-1)
    expert_hits = (flat_experts[:, None] == jnp.arange(experts, dtype=jnp.int32)[None, :]).astype(
        jnp.int32
    )
    slot_rank = jnp.sum(expert_hits * (jnp.cumsum(expert_hits, axis=0) - 1), axis=1)
    local_rank = slot_rank - core * half
    mine = (local_rank >= 0) & (local_rank < half)
    slot_id = jnp.where(mine, flat_experts * half + local_rank, -1)
    slot_iota = jnp.arange(slots, dtype=jnp.int32)
    pick = (slot_id[:, None] == slot_iota[None, :]).astype(jnp.bfloat16)
    select = jnp.max(pick.reshape(tok_rows, TOP, slots), axis=1).T
    outgoing = (
        jnp.dot(select, normed, preferred_element_type=jnp.float32)
        .astype(jnp.bfloat16)
        .reshape(experts, half, width)
    )
    slot_rows = lax.all_to_all(outgoing, "seq", split_axis=0, concat_axis=0, tiled=True)
    other_rows = swap_exp(slot_rows)
    own_hidden = expert_hidden(slot_rows.reshape(-1, width), expert_in[0])
    own_hidden, other_rows = lax.optimization_barrier((own_hidden, other_rows))
    other_hidden = expert_hidden(other_rows.reshape(-1, width), expert_in[0])
    their_part = swap_exp(
        jnp.dot(other_hidden, expert_out[0], preferred_element_type=jnp.float32)
        .astype(jnp.bfloat16)
        .reshape(experts, half, width)
    )
    own_part = (
        jnp.dot(own_hidden, expert_out[0], preferred_element_type=jnp.float32)
        .astype(jnp.bfloat16)
        .reshape(experts, half, width)
    )
    result = (own_part.astype(jnp.float32) + their_part.astype(jnp.float32)).astype(jnp.bfloat16)
    returned = lax.all_to_all(result, "seq", split_axis=0, concat_axis=0, tiled=True)
    picked = jnp.dot(pick, returned.reshape(slots, width), preferred_element_type=jnp.float32)
    weighted = jnp.sum(picked.reshape(tok_rows, TOP, width) * route_gates[:, :, None], axis=1)
    moe = weighted + swap_exp(weighted)
    return (mixed_rows + moe).astype(jnp.bfloat16)


def solution(mesh):
    placed = (
        P(("groups", "seq"), "exp"),
        P(("groups", "seq"), "exp"),
        P(("groups", "seq"), "exp"),
        P(None, "groups", "exp"),
        P("exp"),
        P("exp", None),
        P(("groups", "seq"), None),
        P(),
        P("seq", None, None, "exp"),
        P("seq", "exp", None),
        P(("groups", "seq"), None),
        P(("groups", "seq"), None),
    )
    return jax.shard_map(
        on_device, mesh=mesh, in_specs=placed, out_specs=P(("groups", "seq"), None), check_vma=False
    )
```

```python
import jax
import jax.numpy as jnp
from jax import lax
from jax.experimental import pallas as pl
from jax.experimental.pallas import tpu as pltpu
from jax.sharding import PartitionSpec as P

HEAD_DIM = 64
WINDOW = 128
TOP = 4


GLU_ALPHA = 1.702
EPSILON = 1e-05


def shifted(shard, axis, by):
    size = lax.axis_size(axis)
    pairs = [(i, i + by) for i in range(size) if 0 <= i + by < size]
    return lax.ppermute(shard, axis, pairs)


def swap_exp(x):
    size = lax.axis_size("exp")
    return lax.ppermute(x, "exp", [(i, (i + 1) % size) for i in range(size)])


def rms_normalize(mixed_rows, norm_gain):
    mean_square = jnp.mean(mixed_rows * mixed_rows, axis=-1, keepdims=True)
    return (mixed_rows * lax.rsqrt(mean_square + EPSILON) * norm_gain).astype(jnp.bfloat16)


def attend_block(queries, keys_all, values_all, sink_logits, block_rows, window_rows):
    kv_count = keys_all.shape[1] // HEAD_DIM
    group = queries.shape[1] // HEAD_DIM // kv_count
    query_block = queries.reshape(block_rows, kv_count, group, HEAD_DIM)
    key_block = keys_all.reshape(block_rows + window_rows, kv_count, HEAD_DIM)
    value_block = values_all.reshape(block_rows + window_rows, kv_count, HEAD_DIM)
    scores = jnp.einsum(
        "qhgd,khd->hgqk", query_block, key_block, preferred_element_type=jnp.float32
    ) * HEAD_DIM ** (-0.5)
    query_pos = jnp.arange(block_rows)[:, None]
    key_pos = jnp.arange(block_rows + window_rows)[None, :]
    allowed = (key_pos > query_pos) & (key_pos <= query_pos + window_rows)
    scores = jnp.where(allowed, scores, -jnp.inf)
    sink_table = sink_logits.reshape(kv_count, group)[:, :, None]
    largest = jnp.maximum(jnp.max(scores, axis=-1), sink_table)
    weights_exp = jnp.exp(scores - largest[..., None])
    denominator = jnp.exp(sink_table - largest) + jnp.sum(weights_exp, axis=-1)
    probs = (weights_exp / denominator[..., None]).astype(jnp.bfloat16)
    heads_out = jnp.einsum("hgqk,khd->qhgd", probs, value_block, preferred_element_type=jnp.float32)
    return heads_out.astype(jnp.bfloat16).reshape(block_rows, queries.shape[1])


def expert_hidden(rows, expert_in):
    gate_up = jnp.einsum("rd,kdf->krf", rows, expert_in, preferred_element_type=jnp.float32)
    gate_val = gate_up[0]
    up_val = gate_up[1]
    return ((up_val + 1.0) * gate_val * jax.nn.sigmoid(GLU_ALPHA * gate_val)).astype(jnp.bfloat16)


def attention_kernel(sink_ref, q_ref, pk_ref, k_ref, pv_ref, v_ref, o_ref):
    rows = q_ref.shape[0]
    prior = pk_ref.shape[0]
    span = 2 * WINDOW
    pair_cols = 2 * HEAD_DIM
    pairs = q_ref.shape[1] // pair_cols
    kv_count = k_ref.shape[1] // HEAD_DIM
    per_kv = pairs // kv_count
    keys_all = jnp.concatenate([pk_ref[...], k_ref[...]], axis=0)
    values_all = jnp.concatenate([pv_ref[...], v_ref[...]], axis=0)
    q_pos = lax.broadcasted_iota(jnp.int32, (WINDOW, span), 0)
    k_pos = lax.broadcasted_iota(jnp.int32, (WINDOW, span), 1)
    allowed = (k_pos > q_pos) & (k_pos <= q_pos + WINDOW)
    lane_half = lax.broadcasted_iota(jnp.int32, (span, pair_cols), 1) // HEAD_DIM
    for b in range(rows // WINDOW):
        first = b * WINDOW + prior - WINDOW
        key_win = keys_all[first : first + span]
        value_win = values_all[first : first + span]
        swapped_k = pltpu.roll(key_win, HEAD_DIM, 1)
        swapped_v = pltpu.roll(value_win, HEAD_DIM, 1)
        placed = {}
        for kv in range(kv_count):
            for a in range(2):
                src_k = key_win if (kv % 2) == a else swapped_k
                src_v = value_win if (kv % 2) == a else swapped_v
                placed[kv, a] = (
                    jnp.where(lane_half == a, src_k, jnp.zeros_like(src_k)),
                    jnp.where(lane_half == a, src_v, jnp.zeros_like(src_v)),
                )
        for j in range(pairs):
            kv = j // per_kv
            q_pair = q_ref[b * WINDOW : (b + 1) * WINDOW, j * pair_cols : (j + 1) * pair_cols]
            total = None
            for a in range(2):
                k_placed, v_placed = placed[kv, a]
                scores = lax.dot_general(
                    q_pair, k_placed, (((1,), (1,)), ((), ())), preferred_element_type=jnp.float32
                ) * HEAD_DIM ** (-0.5)
                scores = jnp.where(allowed, scores, -jnp.inf)
                sink = sink_ref[2 * j + a]
                largest = jnp.maximum(jnp.max(scores, axis=-1, keepdims=True), sink)
                weights_exp = jnp.exp(scores - largest)
                denominator = jnp.exp(sink - largest) + jnp.sum(weights_exp, axis=-1, keepdims=True)
                probs = (weights_exp * (1.0 / denominator)).astype(jnp.bfloat16)
                out = jnp.dot(probs, v_placed, preferred_element_type=jnp.float32)
                total = out if total is None else total + out
            o_ref[b * WINDOW : (b + 1) * WINDOW, j * pair_cols : (j + 1) * pair_cols] = total.astype(
                o_ref.dtype
            )


def attend_kernel(queries, prior_keys, key_rows, prior_values, values, sink_logits):
    rows, cols = queries.shape
    heads = cols // HEAD_DIM
    span = 2 * WINDOW
    cost = pl.CostEstimate(
        flops=2 * 2 * rows * span * 2 * HEAD_DIM * heads,
        transcendentals=rows * span * heads,
        bytes_accessed=2 * rows * cols * 2 + 2 * (rows + WINDOW) * key_rows.shape[1] * 2,
    )
    vmem = pl.BlockSpec(memory_space=pltpu.VMEM)
    return pl.pallas_call(
        attention_kernel,
        out_shape=jax.ShapeDtypeStruct((rows, cols), jnp.bfloat16),
        in_specs=[pl.BlockSpec(memory_space=pltpu.SMEM)] + [vmem] * 5,
        out_specs=vmem,
        cost_estimate=cost,
    )(sink_logits, queries, prior_keys, key_rows, prior_values, values)


def on_device(
    queries,
    key_rows,
    values,
    cached_rows,
    sink_logits,
    out_weight,
    residual,
    norm_gain,
    expert_in,
    expert_out,
    routes,
    route_gates,
):
    tok_rows = queries.shape[0]
    window_rows = WINDOW
    rim_rows = jnp.stack([key_rows[tok_rows - window_rows :], values[tok_rows - window_rows :]])
    received = shifted(rim_rows, "seq", 1)
    prior = jnp.where(lax.axis_index("seq") == 0, cached_rows, received)
    pieces = attend_kernel(queries, prior[0], key_rows, prior[1], values, sink_logits)
    partial_rows = jnp.dot(pieces, out_weight, preferred_element_type=jnp.float32)
    mixed_rows = residual.astype(jnp.float32) + (partial_rows + swap_exp(partial_rows))
    normed = rms_normalize(mixed_rows, norm_gain)

    experts = lax.axis_size("seq")
    width = normed.shape[1]
    capacity = 3 * tok_rows * TOP // (2 * experts)
    half = -(-capacity // 2)
    slots = experts * half
    core = lax.axis_index("exp")
    flat_experts = routes.reshape(-1)
    expert_hits = (flat_experts[:, None] == jnp.arange(experts, dtype=jnp.int32)[None, :]).astype(
        jnp.int32
    )
    slot_rank = jnp.sum(expert_hits * (jnp.cumsum(expert_hits, axis=0) - 1), axis=1)
    local_rank = slot_rank - core * half
    mine = (local_rank >= 0) & (local_rank < half)
    slot_id = jnp.where(mine, flat_experts * half + local_rank, -1)
    slot_iota = jnp.arange(slots, dtype=jnp.int32)
    pick = (slot_id[:, None] == slot_iota[None, :]).astype(jnp.bfloat16)
    select = jnp.max(pick.reshape(tok_rows, TOP, slots), axis=1).T
    outgoing = (
        jnp.dot(select, normed, preferred_element_type=jnp.float32)
        .astype(jnp.bfloat16)
        .reshape(experts, half, width)
    )
    slot_rows = lax.all_to_all(outgoing, "seq", split_axis=0, concat_axis=0, tiled=True)
    other_rows = swap_exp(slot_rows)
    own_hidden = expert_hidden(slot_rows.reshape(-1, width), expert_in[0])
    own_hidden, other_rows = lax.optimization_barrier((own_hidden, other_rows))
    other_hidden = expert_hidden(other_rows.reshape(-1, width), expert_in[0])
    their_part = swap_exp(
        jnp.dot(other_hidden, expert_out[0], preferred_element_type=jnp.float32)
        .astype(jnp.bfloat16)
        .reshape(experts, half, width)
    )
    own_part = (
        jnp.dot(own_hidden, expert_out[0], preferred_element_type=jnp.float32)
        .astype(jnp.bfloat16)
        .reshape(experts, half, width)
    )
    result = (own_part.astype(jnp.float32) + their_part.astype(jnp.float32)).astype(jnp.bfloat16)
    returned = lax.all_to_all(result, "seq", split_axis=0, concat_axis=0, tiled=True)
    picked = jnp.dot(pick, returned.reshape(slots, width), preferred_element_type=jnp.float32)
    weighted = jnp.sum(picked.reshape(tok_rows, TOP, width) * route_gates[:, :, None], axis=1)
    moe = weighted + swap_exp(weighted)
    return (mixed_rows + moe).astype(jnp.bfloat16)


def solution(mesh):
    placed = (
        P(("groups", "seq"), "exp"),
        P(("groups", "seq"), "exp"),
        P(("groups", "seq"), "exp"),
        P(None, "groups", "exp"),
        P("exp"),
        P("exp", None),
        P(("groups", "seq"), None),
        P(),
        P("seq", None, None, "exp"),
        P("seq", "exp", None),
        P(("groups", "seq"), None),
        P(("groups", "seq"), None),
    )
    return jax.shard_map(
        on_device, mesh=mesh, in_specs=placed, out_specs=P(("groups", "seq"), None), check_vma=False
    )
```

```python
import jax
import jax.numpy as jnp
from jax import lax
from jax.experimental import pallas as pl
from jax.experimental.pallas import tpu as pltpu
from jax.sharding import PartitionSpec as P

HEAD_DIM = 64
WINDOW = 128
TOP = 4


GLU_ALPHA = 1.702
EPSILON = 1e-05


def shifted(shard, axis, by):
    size = lax.axis_size(axis)
    pairs = [(i, i + by) for i in range(size) if 0 <= i + by < size]
    return lax.ppermute(shard, axis, pairs)


def swap_exp(x):
    size = lax.axis_size("exp")
    return lax.ppermute(x, "exp", [(i, (i + 1) % size) for i in range(size)])


def rms_normalize(mixed_rows, norm_gain):
    mean_square = jnp.mean(mixed_rows * mixed_rows, axis=-1, keepdims=True)
    return (mixed_rows * lax.rsqrt(mean_square + EPSILON) * norm_gain).astype(jnp.bfloat16)


def attend_block(queries, keys_all, values_all, sink_logits, block_rows, window_rows):
    kv_count = keys_all.shape[1] // HEAD_DIM
    group = queries.shape[1] // HEAD_DIM // kv_count
    query_block = queries.reshape(block_rows, kv_count, group, HEAD_DIM)
    key_block = keys_all.reshape(block_rows + window_rows, kv_count, HEAD_DIM)
    value_block = values_all.reshape(block_rows + window_rows, kv_count, HEAD_DIM)
    scores = jnp.einsum(
        "qhgd,khd->hgqk", query_block, key_block, preferred_element_type=jnp.float32
    ) * HEAD_DIM ** (-0.5)
    query_pos = jnp.arange(block_rows)[:, None]
    key_pos = jnp.arange(block_rows + window_rows)[None, :]
    allowed = (key_pos > query_pos) & (key_pos <= query_pos + window_rows)
    scores = jnp.where(allowed, scores, -jnp.inf)
    sink_table = sink_logits.reshape(kv_count, group)[:, :, None]
    largest = jnp.maximum(jnp.max(scores, axis=-1), sink_table)
    weights_exp = jnp.exp(scores - largest[..., None])
    denominator = jnp.exp(sink_table - largest) + jnp.sum(weights_exp, axis=-1)
    probs = (weights_exp / denominator[..., None]).astype(jnp.bfloat16)
    heads_out = jnp.einsum("hgqk,khd->qhgd", probs, value_block, preferred_element_type=jnp.float32)
    return heads_out.astype(jnp.bfloat16).reshape(block_rows, queries.shape[1])


def expert_hidden(rows, expert_in):
    gate_up = jnp.einsum("rd,kdf->krf", rows, expert_in, preferred_element_type=jnp.float32)
    gate_val = gate_up[0]
    up_val = gate_up[1]
    return ((up_val + 1.0) * gate_val * jax.nn.sigmoid(GLU_ALPHA * gate_val)).astype(jnp.bfloat16)


def attention_kernel(sink_ref, q_ref, pk_ref, k_ref, pv_ref, v_ref, o_ref):
    rows = q_ref.shape[0]
    prior = pk_ref.shape[0]
    span = 2 * WINDOW
    pair_cols = 2 * HEAD_DIM
    pairs = q_ref.shape[1] // pair_cols
    kv_count = k_ref.shape[1] // HEAD_DIM
    per_kv = pairs // kv_count
    keys_all = jnp.concatenate([pk_ref[...], k_ref[...]], axis=0)
    values_all = jnp.concatenate([pv_ref[...], v_ref[...]], axis=0)
    q_pos = lax.broadcasted_iota(jnp.int32, (WINDOW, span), 0)
    k_pos = lax.broadcasted_iota(jnp.int32, (WINDOW, span), 1)
    allowed = (k_pos > q_pos) & (k_pos <= q_pos + WINDOW)
    lane_half = lax.broadcasted_iota(jnp.int32, (span, pair_cols), 1) // HEAD_DIM
    for b in range(rows // WINDOW):
        first = b * WINDOW + prior - WINDOW
        key_win = keys_all[first : first + span]
        value_win = values_all[first : first + span]
        swapped_k = pltpu.roll(key_win, HEAD_DIM, 1)
        swapped_v = pltpu.roll(value_win, HEAD_DIM, 1)
        placed = {}
        for kv in range(kv_count):
            for a in range(2):
                src_k = key_win if (kv % 2) == a else swapped_k
                src_v = value_win if (kv % 2) == a else swapped_v
                placed[kv, a] = (
                    jnp.where(lane_half == a, src_k, jnp.zeros_like(src_k)),
                    jnp.where(lane_half == a, src_v, jnp.zeros_like(src_v)),
                )
        for j in range(pairs):
            kv = j // per_kv
            q_pair = q_ref[b * WINDOW : (b + 1) * WINDOW, j * pair_cols : (j + 1) * pair_cols]
            total = None
            for a in range(2):
                k_placed, v_placed = placed[kv, a]
                scores = lax.dot_general(
                    q_pair, k_placed, (((1,), (1,)), ((), ())), preferred_element_type=jnp.float32
                ) * HEAD_DIM ** (-0.5)
                scores = jnp.where(allowed, scores, -jnp.inf)
                sink = sink_ref[2 * j + a]
                largest = jnp.maximum(jnp.max(scores, axis=-1, keepdims=True), sink)
                weights_exp = jnp.exp(scores - largest)
                denominator = jnp.exp(sink - largest) + jnp.sum(weights_exp, axis=-1, keepdims=True)
                probs = (weights_exp * (1.0 / denominator)).astype(jnp.bfloat16)
                out = jnp.dot(probs, v_placed, preferred_element_type=jnp.float32)
                total = out if total is None else total + out
            o_ref[b * WINDOW : (b + 1) * WINDOW, j * pair_cols : (j + 1) * pair_cols] = total.astype(
                o_ref.dtype
            )


def attend_kernel(queries, prior_keys, key_rows, prior_values, values, sink_logits):
    rows, cols = queries.shape
    heads = cols // HEAD_DIM
    span = 2 * WINDOW
    cost = pl.CostEstimate(
        flops=2 * 2 * rows * span * 2 * HEAD_DIM * heads,
        transcendentals=rows * span * heads,
        bytes_accessed=2 * rows * cols * 2 + 2 * (rows + WINDOW) * key_rows.shape[1] * 2,
    )
    vmem = pl.BlockSpec(memory_space=pltpu.VMEM)
    return pl.pallas_call(
        attention_kernel,
        out_shape=jax.ShapeDtypeStruct((rows, cols), jnp.bfloat16),
        in_specs=[pl.BlockSpec(memory_space=pltpu.SMEM)] + [vmem] * 5,
        out_specs=vmem,
        cost_estimate=cost,
    )(sink_logits, queries, prior_keys, key_rows, prior_values, values)


def serve_rows(slot_rows, expert_in, expert_out):
    blocks, piece, width = slot_rows.shape
    other_rows = swap_exp(slot_rows)
    own_hidden = expert_hidden(slot_rows.reshape(-1, width), expert_in)
    own_hidden, other_rows = lax.optimization_barrier((own_hidden, other_rows))
    other_hidden = expert_hidden(other_rows.reshape(-1, width), expert_in)
    their_part = swap_exp(
        jnp.dot(other_hidden, expert_out, preferred_element_type=jnp.float32)
        .astype(jnp.bfloat16)
        .reshape(blocks, piece, width)
    )
    own_part = (
        jnp.dot(own_hidden, expert_out, preferred_element_type=jnp.float32)
        .astype(jnp.bfloat16)
        .reshape(blocks, piece, width)
    )
    return (own_part.astype(jnp.float32) + their_part.astype(jnp.float32)).astype(jnp.bfloat16)


def swap_half(x):
    return lax.ppermute(x, "half", [(0, 1), (1, 0)])


def core_rows(x, core, share):
    return lax.dynamic_slice_in_dim(x, core * share, share, 0)


def join_rows(mine, theirs, core):
    return jnp.where(core == 0, jnp.concatenate([mine, theirs], 0), jnp.concatenate([theirs, mine], 0))


def slot_ids(routes, core, half, first_expert, quads):
    experts = lax.axis_size("half") * quads
    flat = routes.reshape(-1)
    hits = (flat[:, None] == jnp.arange(experts, dtype=jnp.int32)[None, :]).astype(jnp.int32)
    rank = jnp.sum(hits * (jnp.cumsum(hits, axis=0) - 1), axis=1)
    local_rank = rank - core * half
    local_expert = flat - first_expert
    mine = (local_rank >= 0) & (local_rank < half) & (local_expert >= 0) & (local_expert < quads)
    return jnp.where(mine, local_expert * half + local_rank, -1)


def dispatch(normed, ids, slots, quads, half):
    tok_rows, width = normed.shape
    pick = (ids[:, None] == jnp.arange(slots, dtype=jnp.int32)[None, :]).astype(jnp.bfloat16)
    select = jnp.max(pick.reshape(tok_rows, TOP, slots), axis=1).T
    outgoing = (
        jnp.dot(select, normed, preferred_element_type=jnp.float32)
        .astype(jnp.bfloat16)
        .reshape(quads, half, width)
    )
    return pick, lax.all_to_all(outgoing, "quad", split_axis=0, concat_axis=0, tiled=True)


def combine(pick, returned, gates):
    tok_rows = gates.shape[0]
    slots, width = pick.shape[1], returned.shape[-1]
    picked = jnp.dot(pick, returned.reshape(slots, width), preferred_element_type=jnp.float32)
    return jnp.sum(picked.reshape(tok_rows, TOP, width) * gates[:, :, None], axis=1)


def on_device(
    queries,
    key_rows,
    values,
    cached_rows,
    sink_logits,
    out_weight,
    residual,
    norm_gain,
    expert_in,
    expert_out,
    routes,
    route_gates,
):
    tok_rows = queries.shape[0]
    window_rows = WINDOW
    quads = lax.axis_size("quad")
    side = lax.axis_index("half")
    seq_index = side * quads + lax.axis_index("quad")
    core = lax.axis_index("exp")
    rim_rows = jnp.stack([key_rows[tok_rows - window_rows :], values[tok_rows - window_rows :]])
    received = shifted(rim_rows, ("half", "quad"), 1)
    prior = jnp.where(seq_index == 0, cached_rows, received)
    pieces = attend_kernel(queries, prior[0], key_rows, prior[1], values, sink_logits)
    partial_rows = jnp.dot(pieces, out_weight, preferred_element_type=jnp.float32)
    mixed_rows = residual.astype(jnp.float32) + (partial_rows + swap_exp(partial_rows))
    normed = rms_normalize(mixed_rows, norm_gain)

    experts = lax.axis_size("half") * quads
    width = normed.shape[1]
    share = tok_rows // lax.axis_size("exp")
    capacity = 3 * tok_rows * TOP // (2 * experts)
    half = -(-capacity // 2)
    slots = quads * half
    first_expert = side * quads

    partner_part = swap_half(core_rows(normed, core, share))
    partner_routes = swap_half(routes)
    partner_gates = swap_half(route_gates)
    own_ids = slot_ids(routes, core, half, first_expert, quads)
    own_pick, own_arrived = dispatch(normed, own_ids, slots, quads, half)
    partner_normed = join_rows(partner_part, swap_exp(partner_part), core)
    partner_ids = slot_ids(partner_routes, core, half, first_expert, quads)
    partner_pick, partner_arrived = dispatch(partner_normed, partner_ids, slots, quads, half)

    served = serve_rows(
        jnp.concatenate([own_arrived, partner_arrived], axis=0), expert_in[0], expert_out[0]
    )
    own_back = lax.all_to_all(served[:quads], "quad", split_axis=0, concat_axis=0, tiled=True)
    partner_back = lax.all_to_all(served[quads:], "quad", split_axis=0, concat_axis=0, tiled=True)

    partner_sum = combine(partner_pick, partner_back, partner_gates)
    other_core = 1 - core
    partner_rows = core_rows(partner_sum, core, share) + swap_exp(
        core_rows(partner_sum, other_core, share)
    )
    from_partner = swap_half(partner_rows.astype(jnp.bfloat16))
    own_sum = combine(own_pick, own_back, route_gates)
    own_rows = core_rows(own_sum, core, share) + swap_exp(core_rows(own_sum, other_core, share))
    moe_rows = own_rows + from_partner.astype(jnp.float32)
    out_rows = (core_rows(mixed_rows, core, share) + moe_rows).astype(jnp.bfloat16)
    return join_rows(out_rows, swap_exp(out_rows), core)


def solution(mesh):
    groups, seq, exp = mesh.devices.shape
    fine = jax.sharding.Mesh(
        mesh.devices.reshape(groups, 2, seq // 2, exp), ("groups", "half", "quad", "exp")
    )
    rows = ("groups", "half", "quad")
    experts = ("half", "quad")
    placed = (
        P(rows, "exp"),
        P(rows, "exp"),
        P(rows, "exp"),
        P(None, "groups", "exp"),
        P("exp"),
        P("exp", None),
        P(rows, None),
        P(),
        P(experts, None, None, "exp"),
        P(experts, "exp", None),
        P(rows, None),
        P(rows, None),
    )
    return jax.shard_map(on_device, mesh=fine, in_specs=placed, out_specs=P(rows, None), check_vma=False)
```

```python
import jax
import jax.numpy as jnp
from jax import lax
from jax.experimental import pallas as pl
from jax.experimental.pallas import tpu as pltpu
from jax.sharding import PartitionSpec as P

HEAD_DIM = 64
WINDOW = 128
TOP = 4


GLU_ALPHA = 1.702
EPSILON = 1e-05


def shifted(shard, axis, by):
    size = lax.axis_size(axis)
    pairs = [(i, i + by) for i in range(size) if 0 <= i + by < size]
    return lax.ppermute(shard, axis, pairs)


def swap_exp(x):
    size = lax.axis_size("exp")
    return lax.ppermute(x, "exp", [(i, (i + 1) % size) for i in range(size)])


def rms_normalize(mixed_rows, norm_gain):
    mean_square = jnp.mean(mixed_rows * mixed_rows, axis=-1, keepdims=True)
    return (mixed_rows * lax.rsqrt(mean_square + EPSILON) * norm_gain).astype(jnp.bfloat16)


def attend_block(queries, keys_all, values_all, sink_logits, block_rows, window_rows):
    kv_count = keys_all.shape[1] // HEAD_DIM
    group = queries.shape[1] // HEAD_DIM // kv_count
    query_block = queries.reshape(block_rows, kv_count, group, HEAD_DIM)
    key_block = keys_all.reshape(block_rows + window_rows, kv_count, HEAD_DIM)
    value_block = values_all.reshape(block_rows + window_rows, kv_count, HEAD_DIM)
    scores = jnp.einsum(
        "qhgd,khd->hgqk", query_block, key_block, preferred_element_type=jnp.float32
    ) * HEAD_DIM ** (-0.5)
    query_pos = jnp.arange(block_rows)[:, None]
    key_pos = jnp.arange(block_rows + window_rows)[None, :]
    allowed = (key_pos > query_pos) & (key_pos <= query_pos + window_rows)
    scores = jnp.where(allowed, scores, -jnp.inf)
    sink_table = sink_logits.reshape(kv_count, group)[:, :, None]
    largest = jnp.maximum(jnp.max(scores, axis=-1), sink_table)
    weights_exp = jnp.exp(scores - largest[..., None])
    denominator = jnp.exp(sink_table - largest) + jnp.sum(weights_exp, axis=-1)
    probs = (weights_exp / denominator[..., None]).astype(jnp.bfloat16)
    heads_out = jnp.einsum("hgqk,khd->qhgd", probs, value_block, preferred_element_type=jnp.float32)
    return heads_out.astype(jnp.bfloat16).reshape(block_rows, queries.shape[1])


def expert_hidden(rows, expert_in):
    gate_up = jnp.einsum("rd,kdf->krf", rows, expert_in, preferred_element_type=jnp.float32)
    gate_val = gate_up[0]
    up_val = gate_up[1]
    return ((up_val + 1.0) * gate_val * jax.nn.sigmoid(GLU_ALPHA * gate_val)).astype(jnp.bfloat16)


def attention_kernel(sink_ref, q_ref, pk_ref, k_ref, pv_ref, v_ref, o_ref):
    rows = q_ref.shape[0]
    prior = pk_ref.shape[0]
    span = 2 * WINDOW
    pair_cols = 2 * HEAD_DIM
    pairs = q_ref.shape[1] // pair_cols
    kv_count = k_ref.shape[1] // HEAD_DIM
    per_kv = pairs // kv_count
    keys_all = jnp.concatenate([pk_ref[...], k_ref[...]], axis=0)
    values_all = jnp.concatenate([pv_ref[...], v_ref[...]], axis=0)
    q_pos = lax.broadcasted_iota(jnp.int32, (WINDOW, span), 0)
    k_pos = lax.broadcasted_iota(jnp.int32, (WINDOW, span), 1)
    allowed = (k_pos > q_pos) & (k_pos <= q_pos + WINDOW)
    lane_half = lax.broadcasted_iota(jnp.int32, (span, pair_cols), 1) // HEAD_DIM
    for b in range(rows // WINDOW):
        first = b * WINDOW + prior - WINDOW
        key_win = keys_all[first : first + span]
        value_win = values_all[first : first + span]
        swapped_k = pltpu.roll(key_win, HEAD_DIM, 1)
        swapped_v = pltpu.roll(value_win, HEAD_DIM, 1)
        placed = {}
        for kv in range(kv_count):
            for a in range(2):
                src_k = key_win if (kv % 2) == a else swapped_k
                src_v = value_win if (kv % 2) == a else swapped_v
                placed[kv, a] = (
                    jnp.where(lane_half == a, src_k, jnp.zeros_like(src_k)),
                    jnp.where(lane_half == a, src_v, jnp.zeros_like(src_v)),
                )
        for j in range(pairs):
            kv = j // per_kv
            q_pair = q_ref[b * WINDOW : (b + 1) * WINDOW, j * pair_cols : (j + 1) * pair_cols]
            total = None
            for a in range(2):
                k_placed, v_placed = placed[kv, a]
                scores = lax.dot_general(
                    q_pair, k_placed, (((1,), (1,)), ((), ())), preferred_element_type=jnp.float32
                ) * HEAD_DIM ** (-0.5)
                scores = jnp.where(allowed, scores, -jnp.inf)
                sink = sink_ref[2 * j + a]
                largest = jnp.maximum(jnp.max(scores, axis=-1, keepdims=True), sink)
                weights_exp = jnp.exp(scores - largest)
                denominator = jnp.exp(sink - largest) + jnp.sum(weights_exp, axis=-1, keepdims=True)
                probs = (weights_exp * (1.0 / denominator)).astype(jnp.bfloat16)
                out = jnp.dot(probs, v_placed, preferred_element_type=jnp.float32)
                total = out if total is None else total + out
            o_ref[b * WINDOW : (b + 1) * WINDOW, j * pair_cols : (j + 1) * pair_cols] = total.astype(
                o_ref.dtype
            )


def attend_kernel(queries, prior_keys, key_rows, prior_values, values, sink_logits):
    rows, cols = queries.shape
    heads = cols // HEAD_DIM
    span = 2 * WINDOW
    cost = pl.CostEstimate(
        flops=2 * 2 * rows * span * 2 * HEAD_DIM * heads,
        transcendentals=rows * span * heads,
        bytes_accessed=2 * rows * cols * 2 + 2 * (rows + WINDOW) * key_rows.shape[1] * 2,
    )
    vmem = pl.BlockSpec(memory_space=pltpu.VMEM)
    return pl.pallas_call(
        attention_kernel,
        out_shape=jax.ShapeDtypeStruct((rows, cols), jnp.bfloat16),
        in_specs=[pl.BlockSpec(memory_space=pltpu.SMEM)] + [vmem] * 5,
        out_specs=vmem,
        cost_estimate=cost,
    )(sink_logits, queries, prior_keys, key_rows, prior_values, values)


def on_device(
    queries,
    key_rows,
    values,
    cached_rows,
    sink_logits,
    out_weight,
    residual,
    norm_gain,
    expert_in,
    expert_out,
    routes,
    route_gates,
):
    tok_rows = queries.shape[0]
    window_rows = WINDOW
    rim_rows = jnp.stack([key_rows[tok_rows - window_rows :], values[tok_rows - window_rows :]])
    received = shifted(rim_rows, "seq", 1)
    prior = jnp.where(lax.axis_index("seq") == 0, cached_rows, received)
    pieces = attend_kernel(queries, prior[0], key_rows, prior[1], values, sink_logits)
    partial_rows = jnp.dot(pieces, out_weight, preferred_element_type=jnp.float32)
    mixed_rows = residual.astype(jnp.float32) + (partial_rows + swap_exp(partial_rows))
    normed = rms_normalize(mixed_rows, norm_gain)

    experts = lax.axis_size("seq")
    width = normed.shape[1]
    capacity = 3 * tok_rows * TOP // (2 * experts)
    half = -(-capacity // 2)
    slots = experts * half
    core = lax.axis_index("exp")
    flat_experts = routes.reshape(-1)
    route_hits = (routes[:, :, None] == jnp.arange(experts, dtype=jnp.int32)[None, None, :]).astype(
        jnp.float32
    )
    token_hits = jnp.sum(route_hits, axis=1)
    earlier = (
        jnp.arange(tok_rows, dtype=jnp.int32)[None, :] < jnp.arange(tok_rows, dtype=jnp.int32)[:, None]
    ).astype(jnp.bfloat16)
    before = jnp.dot(earlier, token_hits.astype(jnp.bfloat16), preferred_element_type=jnp.float32)
    slot_rank = jnp.sum(route_hits * before[:, None, :], axis=2).astype(jnp.int32).reshape(-1)
    local_rank = slot_rank - core * half
    mine = (local_rank >= 0) & (local_rank < half)
    slot_id = jnp.where(mine, flat_experts * half + local_rank, -1)
    slot_iota = jnp.arange(slots, dtype=jnp.int32)
    pick = (slot_id[:, None] == slot_iota[None, :]).astype(jnp.bfloat16)
    select = jnp.max(pick.reshape(tok_rows, TOP, slots), axis=1).T
    outgoing = (
        jnp.dot(select, normed, preferred_element_type=jnp.float32)
        .astype(jnp.bfloat16)
        .reshape(experts, half, width)
    )
    slot_rows = lax.all_to_all(outgoing, "seq", split_axis=0, concat_axis=0, tiled=True)
    other_rows = swap_exp(slot_rows)
    own_hidden = expert_hidden(slot_rows.reshape(-1, width), expert_in[0])
    own_hidden, other_rows = lax.optimization_barrier((own_hidden, other_rows))
    other_hidden = expert_hidden(other_rows.reshape(-1, width), expert_in[0])
    their_part = swap_exp(
        jnp.dot(other_hidden, expert_out[0], preferred_element_type=jnp.float32)
        .astype(jnp.bfloat16)
        .reshape(experts, half, width)
    )
    own_part = (
        jnp.dot(own_hidden, expert_out[0], preferred_element_type=jnp.float32)
        .astype(jnp.bfloat16)
        .reshape(experts, half, width)
    )
    result = (own_part.astype(jnp.float32) + their_part.astype(jnp.float32)).astype(jnp.bfloat16)
    returned = lax.all_to_all(result, "seq", split_axis=0, concat_axis=0, tiled=True)
    flat_returned = returned.reshape(slots, width)
    outs = []
    for rows in (slice(0, tok_rows // 2), slice(tok_rows // 2, tok_rows)):
        picked = jnp.dot(
            pick[rows.start * TOP : rows.stop * TOP], flat_returned, preferred_element_type=jnp.float32
        )
        weighted = jnp.sum(picked.reshape(-1, TOP, width) * route_gates[rows][:, :, None], axis=1)
        outs.append((weighted, swap_exp(weighted)))
    moe = jnp.concatenate([mine + theirs for mine, theirs in outs], axis=0)
    return (mixed_rows + moe).astype(jnp.bfloat16)


def solution(mesh):
    placed = (
        P(("groups", "seq"), "exp"),
        P(("groups", "seq"), "exp"),
        P(("groups", "seq"), "exp"),
        P(None, "groups", "exp"),
        P("exp"),
        P("exp", None),
        P(("groups", "seq"), None),
        P(),
        P("seq", None, None, "exp"),
        P("seq", "exp", None),
        P(("groups", "seq"), None),
        P(("groups", "seq"), None),
    )
    return jax.shard_map(
        on_device, mesh=mesh, in_specs=placed, out_specs=P(("groups", "seq"), None), check_vma=False
    )
```

```python
import jax
import jax.numpy as jnp
from jax import lax
from jax.experimental import pallas as pl
from jax.experimental.pallas import tpu as pltpu
from jax.sharding import PartitionSpec as P

HEAD_DIM = 64
WINDOW = 128
TOP = 4


GLU_ALPHA = 1.702
EPSILON = 1e-05


def shifted(shard, axis, by):
    size = lax.axis_size(axis)
    pairs = [(i, i + by) for i in range(size) if 0 <= i + by < size]
    return lax.ppermute(shard, axis, pairs)


def swap_exp(x):
    size = lax.axis_size("exp")
    return lax.ppermute(x, "exp", [(i, (i + 1) % size) for i in range(size)])


def rms_normalize(mixed_rows, norm_gain):
    mean_square = jnp.mean(mixed_rows * mixed_rows, axis=-1, keepdims=True)
    return (mixed_rows * lax.rsqrt(mean_square + EPSILON) * norm_gain).astype(jnp.bfloat16)


def attend_block(queries, keys_all, values_all, sink_logits, block_rows, window_rows):
    kv_count = keys_all.shape[1] // HEAD_DIM
    group = queries.shape[1] // HEAD_DIM // kv_count
    query_block = queries.reshape(block_rows, kv_count, group, HEAD_DIM)
    key_block = keys_all.reshape(block_rows + window_rows, kv_count, HEAD_DIM)
    value_block = values_all.reshape(block_rows + window_rows, kv_count, HEAD_DIM)
    scores = jnp.einsum(
        "qhgd,khd->hgqk", query_block, key_block, preferred_element_type=jnp.float32
    ) * HEAD_DIM ** (-0.5)
    query_pos = jnp.arange(block_rows)[:, None]
    key_pos = jnp.arange(block_rows + window_rows)[None, :]
    allowed = (key_pos > query_pos) & (key_pos <= query_pos + window_rows)
    scores = jnp.where(allowed, scores, -jnp.inf)
    sink_table = sink_logits.reshape(kv_count, group)[:, :, None]
    largest = jnp.maximum(jnp.max(scores, axis=-1), sink_table)
    weights_exp = jnp.exp(scores - largest[..., None])
    denominator = jnp.exp(sink_table - largest) + jnp.sum(weights_exp, axis=-1)
    probs = (weights_exp / denominator[..., None]).astype(jnp.bfloat16)
    heads_out = jnp.einsum("hgqk,khd->qhgd", probs, value_block, preferred_element_type=jnp.float32)
    return heads_out.astype(jnp.bfloat16).reshape(block_rows, queries.shape[1])


def expert_hidden(rows, expert_in):
    gate_up = jnp.einsum("rd,kdf->krf", rows, expert_in, preferred_element_type=jnp.float32)
    gate_val = gate_up[0]
    up_val = gate_up[1]
    return ((up_val + 1.0) * gate_val * jax.nn.sigmoid(GLU_ALPHA * gate_val)).astype(jnp.bfloat16)


def attention_kernel(sink_ref, q_ref, pk_ref, k_ref, pv_ref, v_ref, o_ref):
    rows = q_ref.shape[0]
    prior = pk_ref.shape[0]
    span = 2 * WINDOW
    pair_cols = 2 * HEAD_DIM
    pairs = q_ref.shape[1] // pair_cols
    kv_count = k_ref.shape[1] // HEAD_DIM
    per_kv = pairs // kv_count
    keys_all = jnp.concatenate([pk_ref[...], k_ref[...]], axis=0)
    values_all = jnp.concatenate([pv_ref[...], v_ref[...]], axis=0)
    q_pos = lax.broadcasted_iota(jnp.int32, (WINDOW, span), 0)
    k_pos = lax.broadcasted_iota(jnp.int32, (WINDOW, span), 1)
    allowed = (k_pos > q_pos) & (k_pos <= q_pos + WINDOW)
    lane_half = lax.broadcasted_iota(jnp.int32, (span, pair_cols), 1) // HEAD_DIM
    for b in range(rows // WINDOW):
        first = b * WINDOW + prior - WINDOW
        key_win = keys_all[first : first + span]
        value_win = values_all[first : first + span]
        swapped_k = pltpu.roll(key_win, HEAD_DIM, 1)
        swapped_v = pltpu.roll(value_win, HEAD_DIM, 1)
        placed = {}
        for kv in range(kv_count):
            for a in range(2):
                src_k = key_win if (kv % 2) == a else swapped_k
                src_v = value_win if (kv % 2) == a else swapped_v
                placed[kv, a] = (
                    jnp.where(lane_half == a, src_k, jnp.zeros_like(src_k)),
                    jnp.where(lane_half == a, src_v, jnp.zeros_like(src_v)),
                )
        for j in range(pairs):
            kv = j // per_kv
            q_pair = q_ref[b * WINDOW : (b + 1) * WINDOW, j * pair_cols : (j + 1) * pair_cols]
            total = None
            for a in range(2):
                k_placed, v_placed = placed[kv, a]
                scores = lax.dot_general(
                    q_pair, k_placed, (((1,), (1,)), ((), ())), preferred_element_type=jnp.float32
                ) * HEAD_DIM ** (-0.5)
                scores = jnp.where(allowed, scores, -jnp.inf)
                sink = sink_ref[2 * j + a]
                largest = jnp.maximum(jnp.max(scores, axis=-1, keepdims=True), sink)
                weights_exp = jnp.exp(scores - largest)
                denominator = jnp.exp(sink - largest) + jnp.sum(weights_exp, axis=-1, keepdims=True)
                probs = (weights_exp * (1.0 / denominator)).astype(jnp.bfloat16)
                out = jnp.dot(probs, v_placed, preferred_element_type=jnp.float32)
                total = out if total is None else total + out
            o_ref[b * WINDOW : (b + 1) * WINDOW, j * pair_cols : (j + 1) * pair_cols] = total.astype(
                o_ref.dtype
            )


def attend_kernel(queries, prior_keys, key_rows, prior_values, values, sink_logits):
    rows, cols = queries.shape
    heads = cols // HEAD_DIM
    span = 2 * WINDOW
    cost = pl.CostEstimate(
        flops=2 * 2 * rows * span * 2 * HEAD_DIM * heads,
        transcendentals=rows * span * heads,
        bytes_accessed=2 * rows * cols * 2 + 2 * (rows + WINDOW) * key_rows.shape[1] * 2,
    )
    vmem = pl.BlockSpec(memory_space=pltpu.VMEM)
    return pl.pallas_call(
        attention_kernel,
        out_shape=jax.ShapeDtypeStruct((rows, cols), jnp.bfloat16),
        in_specs=[pl.BlockSpec(memory_space=pltpu.SMEM)] + [vmem] * 5,
        out_specs=vmem,
        cost_estimate=cost,
    )(sink_logits, queries, prior_keys, key_rows, prior_values, values)


def on_device(
    queries,
    key_rows,
    values,
    cached_rows,
    sink_logits,
    out_weight,
    residual,
    norm_gain,
    expert_in,
    expert_out,
    routes,
    route_gates,
):
    tok_rows = queries.shape[0]
    window_rows = WINDOW
    rim_rows = jnp.stack([key_rows[tok_rows - window_rows :], values[tok_rows - window_rows :]])
    received = shifted(rim_rows, "seq", 1)
    prior = jnp.where(lax.axis_index("seq") == 0, cached_rows, received)
    pieces = attend_kernel(queries, prior[0], key_rows, prior[1], values, sink_logits)
    partial_rows = jnp.dot(pieces, out_weight, preferred_element_type=jnp.float32)
    mixed_rows = residual.astype(jnp.float32) + (partial_rows + swap_exp(partial_rows))
    normed = rms_normalize(mixed_rows, norm_gain)

    experts = lax.axis_size("seq")
    width = normed.shape[1]
    capacity = 3 * tok_rows * TOP // (2 * experts)
    half = -(-capacity // 2)
    slots = experts * half
    core = lax.axis_index("exp")
    flat_experts = routes.reshape(-1)
    expert_hits = (flat_experts[:, None] == jnp.arange(experts, dtype=jnp.int32)[None, :]).astype(
        jnp.int32
    )
    slot_rank = jnp.sum(expert_hits * (jnp.cumsum(expert_hits, axis=0) - 1), axis=1)
    local_rank = slot_rank - core * half
    mine = (local_rank >= 0) & (local_rank < half)
    slot_id = jnp.where(mine, flat_experts * half + local_rank, -1)
    slot_iota = jnp.arange(slots, dtype=jnp.int32)
    pick = (slot_id[:, None] == slot_iota[None, :]).astype(jnp.bfloat16)
    select = jnp.max(pick.reshape(tok_rows, TOP, slots), axis=1).T
    outgoing = (
        jnp.dot(select, normed, preferred_element_type=jnp.float32)
        .astype(jnp.bfloat16)
        .reshape(experts, half, width)
    )
    slot_rows = lax.all_to_all(outgoing, "seq", split_axis=0, concat_axis=0, tiled=True)
    other_rows = swap_exp(slot_rows)
    own_hidden = expert_hidden(slot_rows.reshape(-1, width), expert_in[0])
    own_hidden, other_rows = lax.optimization_barrier((own_hidden, other_rows))
    other_hidden = expert_hidden(other_rows.reshape(-1, width), expert_in[0])
    their_part = swap_exp(
        jnp.dot(other_hidden, expert_out[0], preferred_element_type=jnp.float32)
        .astype(jnp.bfloat16)
        .reshape(experts, half, width)
    )
    own_part = (
        jnp.dot(own_hidden, expert_out[0], preferred_element_type=jnp.float32)
        .astype(jnp.bfloat16)
        .reshape(experts, half, width)
    )
    result = (own_part.astype(jnp.float32) + their_part.astype(jnp.float32)).astype(jnp.bfloat16)
    returned = lax.all_to_all(result, "seq", split_axis=0, concat_axis=0, tiled=True)
    gate_table = jnp.sum(
        pick.reshape(tok_rows, TOP, slots).astype(jnp.float32) * route_gates[:, :, None], axis=1
    )
    gate_high = gate_table.astype(jnp.bfloat16)
    gate_low = (gate_table - gate_high.astype(jnp.float32)).astype(jnp.bfloat16)
    flat_returned = returned.reshape(slots, width)
    parts = []
    for rows in (slice(0, tok_rows // 2), slice(tok_rows // 2, tok_rows)):
        weighted = jnp.dot(
            gate_high[rows], flat_returned, preferred_element_type=jnp.float32
        ) + jnp.dot(gate_low[rows], flat_returned, preferred_element_type=jnp.float32)
        parts.append(weighted + swap_exp(weighted))
    moe = jnp.concatenate(parts, axis=0)
    return (mixed_rows + moe).astype(jnp.bfloat16)


def solution(mesh):
    placed = (
        P(("groups", "seq"), "exp"),
        P(("groups", "seq"), "exp"),
        P(("groups", "seq"), "exp"),
        P(None, "groups", "exp"),
        P("exp"),
        P("exp", None),
        P(("groups", "seq"), None),
        P(),
        P("seq", None, None, "exp"),
        P("seq", "exp", None),
        P(("groups", "seq"), None),
        P(("groups", "seq"), None),
    )
    return jax.shard_map(
        on_device, mesh=mesh, in_specs=placed, out_specs=P(("groups", "seq"), None), check_vma=False
    )
```

```python
import jax
import jax.numpy as jnp
from jax import lax
from jax.experimental import pallas as pl
from jax.experimental.pallas import tpu as pltpu
from jax.sharding import PartitionSpec as P

HEAD_DIM = 64
WINDOW = 128
TOP = 4


GLU_ALPHA = 1.702
EPSILON = 1e-05


def shifted(shard, axis, by):
    size = lax.axis_size(axis)
    pairs = [(i, i + by) for i in range(size) if 0 <= i + by < size]
    return lax.ppermute(shard, axis, pairs)


def swap_exp(x):
    size = lax.axis_size("exp")
    return lax.ppermute(x, "exp", [(i, (i + 1) % size) for i in range(size)])


def rms_normalize(mixed_rows, norm_gain):
    mean_square = jnp.mean(mixed_rows * mixed_rows, axis=-1, keepdims=True)
    return (mixed_rows * lax.rsqrt(mean_square + EPSILON) * norm_gain).astype(jnp.bfloat16)


def attend_block(queries, keys_all, values_all, sink_logits, block_rows, window_rows):
    kv_count = keys_all.shape[1] // HEAD_DIM
    group = queries.shape[1] // HEAD_DIM // kv_count
    query_block = queries.reshape(block_rows, kv_count, group, HEAD_DIM)
    key_block = keys_all.reshape(block_rows + window_rows, kv_count, HEAD_DIM)
    value_block = values_all.reshape(block_rows + window_rows, kv_count, HEAD_DIM)
    scores = jnp.einsum(
        "qhgd,khd->hgqk", query_block, key_block, preferred_element_type=jnp.float32
    ) * HEAD_DIM ** (-0.5)
    query_pos = jnp.arange(block_rows)[:, None]
    key_pos = jnp.arange(block_rows + window_rows)[None, :]
    allowed = (key_pos > query_pos) & (key_pos <= query_pos + window_rows)
    scores = jnp.where(allowed, scores, -jnp.inf)
    sink_table = sink_logits.reshape(kv_count, group)[:, :, None]
    largest = jnp.maximum(jnp.max(scores, axis=-1), sink_table)
    weights_exp = jnp.exp(scores - largest[..., None])
    denominator = jnp.exp(sink_table - largest) + jnp.sum(weights_exp, axis=-1)
    probs = (weights_exp / denominator[..., None]).astype(jnp.bfloat16)
    heads_out = jnp.einsum("hgqk,khd->qhgd", probs, value_block, preferred_element_type=jnp.float32)
    return heads_out.astype(jnp.bfloat16).reshape(block_rows, queries.shape[1])


def expert_hidden(rows, expert_in):
    gate_up = jnp.einsum("rd,kdf->krf", rows, expert_in, preferred_element_type=jnp.float32)
    gate_val = gate_up[0]
    up_val = gate_up[1]
    return ((up_val + 1.0) * gate_val * jax.nn.sigmoid(GLU_ALPHA * gate_val)).astype(jnp.bfloat16)


def attention_kernel(sink_ref, q_ref, pk_ref, k_ref, pv_ref, v_ref, o_ref):
    rows = q_ref.shape[0]
    prior = pk_ref.shape[0]
    span = 2 * WINDOW
    pair_cols = 2 * HEAD_DIM
    pairs = q_ref.shape[1] // pair_cols
    kv_count = k_ref.shape[1] // HEAD_DIM
    per_kv = pairs // kv_count
    keys_all = jnp.concatenate([pk_ref[...], k_ref[...]], axis=0)
    values_all = jnp.concatenate([pv_ref[...], v_ref[...]], axis=0)
    q_pos = lax.broadcasted_iota(jnp.int32, (WINDOW, span), 0)
    k_pos = lax.broadcasted_iota(jnp.int32, (WINDOW, span), 1)
    allowed = (k_pos > q_pos) & (k_pos <= q_pos + WINDOW)
    lane_half = lax.broadcasted_iota(jnp.int32, (span, pair_cols), 1) // HEAD_DIM
    for b in range(rows // WINDOW):
        first = b * WINDOW + prior - WINDOW
        key_win = keys_all[first : first + span]
        value_win = values_all[first : first + span]
        swapped_k = pltpu.roll(key_win, HEAD_DIM, 1)
        swapped_v = pltpu.roll(value_win, HEAD_DIM, 1)
        placed = {}
        for kv in range(kv_count):
            for a in range(2):
                src_k = key_win if (kv % 2) == a else swapped_k
                src_v = value_win if (kv % 2) == a else swapped_v
                placed[kv, a] = (
                    jnp.where(lane_half == a, src_k, jnp.zeros_like(src_k)),
                    jnp.where(lane_half == a, src_v, jnp.zeros_like(src_v)),
                )
        for j in range(pairs):
            kv = j // per_kv
            q_pair = q_ref[b * WINDOW : (b + 1) * WINDOW, j * pair_cols : (j + 1) * pair_cols]
            total = None
            for a in range(2):
                k_placed, v_placed = placed[kv, a]
                scores = lax.dot_general(
                    q_pair, k_placed, (((1,), (1,)), ((), ())), preferred_element_type=jnp.float32
                ) * HEAD_DIM ** (-0.5)
                scores = jnp.where(allowed, scores, -jnp.inf)
                sink = sink_ref[2 * j + a]
                largest = jnp.maximum(jnp.max(scores, axis=-1, keepdims=True), sink)
                weights_exp = jnp.exp(scores - largest)
                denominator = jnp.exp(sink - largest) + jnp.sum(weights_exp, axis=-1, keepdims=True)
                probs = (weights_exp * (1.0 / denominator)).astype(jnp.bfloat16)
                out = jnp.dot(probs, v_placed, preferred_element_type=jnp.float32)
                total = out if total is None else total + out
            o_ref[b * WINDOW : (b + 1) * WINDOW, j * pair_cols : (j + 1) * pair_cols] = total.astype(
                o_ref.dtype
            )


def attend_kernel(queries, prior_keys, key_rows, prior_values, values, sink_logits):
    rows, cols = queries.shape
    heads = cols // HEAD_DIM
    span = 2 * WINDOW
    cost = pl.CostEstimate(
        flops=2 * 2 * rows * span * 2 * HEAD_DIM * heads,
        transcendentals=rows * span * heads,
        bytes_accessed=2 * rows * cols * 2 + 2 * (rows + WINDOW) * key_rows.shape[1] * 2,
    )
    vmem = pl.BlockSpec(memory_space=pltpu.VMEM)
    return pl.pallas_call(
        attention_kernel,
        out_shape=jax.ShapeDtypeStruct((rows, cols), jnp.bfloat16),
        in_specs=[pl.BlockSpec(memory_space=pltpu.SMEM)] + [vmem] * 5,
        out_specs=vmem,
        cost_estimate=cost,
    )(sink_logits, queries, prior_keys, key_rows, prior_values, values)


def serve_rows(slot_rows, expert_in, expert_out):
    blocks, piece, width = slot_rows.shape
    other_rows = swap_exp(slot_rows)
    own_hidden = expert_hidden(slot_rows.reshape(-1, width), expert_in)
    own_hidden, other_rows = lax.optimization_barrier((own_hidden, other_rows))
    other_hidden = expert_hidden(other_rows.reshape(-1, width), expert_in)
    their_part = swap_exp(
        jnp.dot(other_hidden, expert_out, preferred_element_type=jnp.float32)
        .astype(jnp.bfloat16)
        .reshape(blocks, piece, width)
    )
    own_part = (
        jnp.dot(own_hidden, expert_out, preferred_element_type=jnp.float32)
        .astype(jnp.bfloat16)
        .reshape(blocks, piece, width)
    )
    return (own_part.astype(jnp.float32) + their_part.astype(jnp.float32)).astype(jnp.bfloat16)


def swap_half(x):
    return lax.ppermute(x, "half", [(0, 1), (1, 0)])


def core_rows(x, core, share):
    return lax.dynamic_slice_in_dim(x, core * share, share, 0)


def join_rows(mine, theirs, core):
    return jnp.where(core == 0, jnp.concatenate([mine, theirs], 0), jnp.concatenate([theirs, mine], 0))


def slot_ids(routes, core, half, first_expert, quads):
    experts = lax.axis_size("half") * quads
    flat = routes.reshape(-1)
    hits = (flat[:, None] == jnp.arange(experts, dtype=jnp.int32)[None, :]).astype(jnp.int32)
    rank = jnp.sum(hits * (jnp.cumsum(hits, axis=0) - 1), axis=1)
    local_rank = rank - core * half
    local_expert = flat - first_expert
    mine = (local_rank >= 0) & (local_rank < half) & (local_expert >= 0) & (local_expert < quads)
    return jnp.where(mine, local_expert * half + local_rank, -1)


def dispatch(normed, ids, slots, quads, half):
    tok_rows, width = normed.shape
    pick = (ids[:, None] == jnp.arange(slots, dtype=jnp.int32)[None, :]).astype(jnp.bfloat16)
    select = jnp.max(pick.reshape(tok_rows, TOP, slots), axis=1).T
    outgoing = (
        jnp.dot(select, normed, preferred_element_type=jnp.float32)
        .astype(jnp.bfloat16)
        .reshape(quads, half, width)
    )
    return pick, outgoing


def combine(pick, returned, gates):
    tok_rows = gates.shape[0]
    slots, width = pick.shape[1], returned.shape[-1]
    picked = jnp.dot(pick, returned.reshape(slots, width), preferred_element_type=jnp.float32)
    return jnp.sum(picked.reshape(tok_rows, TOP, width) * gates[:, :, None], axis=1)


def on_device(
    queries,
    key_rows,
    values,
    cached_rows,
    sink_logits,
    out_weight,
    residual,
    norm_gain,
    expert_in,
    expert_out,
    routes,
    route_gates,
):
    tok_rows = queries.shape[0]
    window_rows = WINDOW
    quads = lax.axis_size("quad")
    side = lax.axis_index("half")
    seq_index = side * quads + lax.axis_index("quad")
    core = lax.axis_index("exp")
    rim_rows = jnp.stack([key_rows[tok_rows - window_rows :], values[tok_rows - window_rows :]])
    received = shifted(rim_rows, ("half", "quad"), 1)
    prior = jnp.where(seq_index == 0, cached_rows, received)
    pieces = attend_kernel(queries, prior[0], key_rows, prior[1], values, sink_logits)
    partial_rows = jnp.dot(pieces, out_weight, preferred_element_type=jnp.float32)
    mixed_rows = residual.astype(jnp.float32) + (partial_rows + swap_exp(partial_rows))
    normed = rms_normalize(mixed_rows, norm_gain)

    experts = lax.axis_size("half") * quads
    width = normed.shape[1]
    share = tok_rows // lax.axis_size("exp")
    capacity = 3 * tok_rows * TOP // (2 * experts)
    half = -(-capacity // 2)
    slots = quads * half
    first_expert = side * quads

    partner_part = swap_half(core_rows(normed, core, share))
    partner_routes = swap_half(routes)
    partner_gates = swap_half(route_gates)
    partner_normed = join_rows(partner_part, swap_exp(partner_part), core)
    partner_ids = slot_ids(partner_routes, core, half, first_expert, quads)
    partner_pick, partner_out = dispatch(partner_normed, partner_ids, slots, quads, half)
    own_ids = slot_ids(routes, core, half, first_expert, quads)
    own_pick, own_out = dispatch(normed, own_ids, slots, quads, half)
    arrived = lax.all_to_all(
        jnp.concatenate([own_out, partner_out], axis=1), "quad", split_axis=0, concat_axis=0, tiled=True
    )
    served = serve_rows(arrived, expert_in[0], expert_out[0])
    back = lax.all_to_all(served, "quad", split_axis=0, concat_axis=0, tiled=True)
    own_back = back[:, :half]
    partner_back = back[:, half:]

    partner_sum = combine(partner_pick, partner_back, partner_gates)
    other_core = 1 - core
    partner_rows = core_rows(partner_sum, core, share) + swap_exp(
        core_rows(partner_sum, other_core, share)
    )
    from_partner = swap_half(partner_rows.astype(jnp.bfloat16))
    own_sum = combine(own_pick, own_back, route_gates)
    own_rows = core_rows(own_sum, core, share) + swap_exp(core_rows(own_sum, other_core, share))
    moe_rows = own_rows + from_partner.astype(jnp.float32)
    out_rows = (core_rows(mixed_rows, core, share) + moe_rows).astype(jnp.bfloat16)
    return join_rows(out_rows, swap_exp(out_rows), core)


def solution(mesh):
    groups, seq, exp = mesh.devices.shape
    fine = jax.sharding.Mesh(
        mesh.devices.reshape(groups, 2, seq // 2, exp), ("groups", "half", "quad", "exp")
    )
    rows = ("groups", "half", "quad")
    experts = ("half", "quad")
    placed = (
        P(rows, "exp"),
        P(rows, "exp"),
        P(rows, "exp"),
        P(None, "groups", "exp"),
        P("exp"),
        P("exp", None),
        P(rows, None),
        P(),
        P(experts, None, None, "exp"),
        P(experts, "exp", None),
        P(rows, None),
        P(rows, None),
    )
    return jax.shard_map(on_device, mesh=fine, in_specs=placed, out_specs=P(rows, None), check_vma=False)
```

```python
import jax
import jax.numpy as jnp
from jax import lax
from jax.experimental import pallas as pl
from jax.experimental.pallas import tpu as pltpu
from jax.sharding import PartitionSpec as P

HEAD_DIM = 64
WINDOW = 128
TOP = 4


GLU_ALPHA = 1.702
EPSILON = 1e-05


def shifted(shard, axis, by):
    size = lax.axis_size(axis)
    pairs = [(i, i + by) for i in range(size) if 0 <= i + by < size]
    return lax.ppermute(shard, axis, pairs)


def swap_exp(x):
    size = lax.axis_size("exp")
    return lax.ppermute(x, "exp", [(i, (i + 1) % size) for i in range(size)])


def rms_normalize(mixed_rows, norm_gain):
    mean_square = jnp.mean(mixed_rows * mixed_rows, axis=-1, keepdims=True)
    return (mixed_rows * lax.rsqrt(mean_square + EPSILON) * norm_gain).astype(jnp.bfloat16)


def attend_block(queries, keys_all, values_all, sink_logits, block_rows, window_rows):
    kv_count = keys_all.shape[1] // HEAD_DIM
    group = queries.shape[1] // HEAD_DIM // kv_count
    query_block = queries.reshape(block_rows, kv_count, group, HEAD_DIM)
    key_block = keys_all.reshape(block_rows + window_rows, kv_count, HEAD_DIM)
    value_block = values_all.reshape(block_rows + window_rows, kv_count, HEAD_DIM)
    scores = jnp.einsum(
        "qhgd,khd->hgqk", query_block, key_block, preferred_element_type=jnp.float32
    ) * HEAD_DIM ** (-0.5)
    query_pos = jnp.arange(block_rows)[:, None]
    key_pos = jnp.arange(block_rows + window_rows)[None, :]
    allowed = (key_pos > query_pos) & (key_pos <= query_pos + window_rows)
    scores = jnp.where(allowed, scores, -jnp.inf)
    sink_table = sink_logits.reshape(kv_count, group)[:, :, None]
    largest = jnp.maximum(jnp.max(scores, axis=-1), sink_table)
    weights_exp = jnp.exp(scores - largest[..., None])
    denominator = jnp.exp(sink_table - largest) + jnp.sum(weights_exp, axis=-1)
    probs = (weights_exp / denominator[..., None]).astype(jnp.bfloat16)
    heads_out = jnp.einsum("hgqk,khd->qhgd", probs, value_block, preferred_element_type=jnp.float32)
    return heads_out.astype(jnp.bfloat16).reshape(block_rows, queries.shape[1])


def expert_hidden(rows, expert_in):
    gate_up = jnp.einsum("rd,kdf->krf", rows, expert_in, preferred_element_type=jnp.float32)
    gate_val = gate_up[0]
    up_val = gate_up[1]
    return ((up_val + 1.0) * gate_val * jax.nn.sigmoid(GLU_ALPHA * gate_val)).astype(jnp.bfloat16)


def attention_kernel(sink_ref, q_ref, pk_ref, k_ref, pv_ref, v_ref, o_ref):
    rows = q_ref.shape[0]
    prior = pk_ref.shape[0]
    span = 2 * WINDOW
    pair_cols = 2 * HEAD_DIM
    pairs = q_ref.shape[1] // pair_cols
    kv_count = k_ref.shape[1] // HEAD_DIM
    per_kv = pairs // kv_count
    keys_all = jnp.concatenate([pk_ref[...], k_ref[...]], axis=0)
    values_all = jnp.concatenate([pv_ref[...], v_ref[...]], axis=0)
    q_pos = lax.broadcasted_iota(jnp.int32, (WINDOW, span), 0)
    k_pos = lax.broadcasted_iota(jnp.int32, (WINDOW, span), 1)
    allowed = (k_pos > q_pos) & (k_pos <= q_pos + WINDOW)
    lane_half = lax.broadcasted_iota(jnp.int32, (span, pair_cols), 1) // HEAD_DIM
    for b in range(rows // WINDOW):
        first = b * WINDOW + prior - WINDOW
        key_win = keys_all[first : first + span]
        value_win = values_all[first : first + span]
        swapped_k = pltpu.roll(key_win, HEAD_DIM, 1)
        swapped_v = pltpu.roll(value_win, HEAD_DIM, 1)
        placed = {}
        for kv in range(kv_count):
            for a in range(2):
                src_k = key_win if (kv % 2) == a else swapped_k
                src_v = value_win if (kv % 2) == a else swapped_v
                placed[kv, a] = (
                    jnp.where(lane_half == a, src_k, jnp.zeros_like(src_k)),
                    jnp.where(lane_half == a, src_v, jnp.zeros_like(src_v)),
                )
        for j in range(pairs):
            kv = j // per_kv
            q_pair = q_ref[b * WINDOW : (b + 1) * WINDOW, j * pair_cols : (j + 1) * pair_cols]
            total = None
            for a in range(2):
                k_placed, v_placed = placed[kv, a]
                scores = lax.dot_general(
                    q_pair, k_placed, (((1,), (1,)), ((), ())), preferred_element_type=jnp.float32
                ) * HEAD_DIM ** (-0.5)
                scores = jnp.where(allowed, scores, -jnp.inf)
                sink = sink_ref[2 * j + a]
                largest = jnp.maximum(jnp.max(scores, axis=-1, keepdims=True), sink)
                weights_exp = jnp.exp(scores - largest)
                denominator = jnp.exp(sink - largest) + jnp.sum(weights_exp, axis=-1, keepdims=True)
                probs = (weights_exp * (1.0 / denominator)).astype(jnp.bfloat16)
                out = jnp.dot(probs, v_placed, preferred_element_type=jnp.float32)
                total = out if total is None else total + out
            o_ref[b * WINDOW : (b + 1) * WINDOW, j * pair_cols : (j + 1) * pair_cols] = total.astype(
                o_ref.dtype
            )


def attend_kernel(queries, prior_keys, key_rows, prior_values, values, sink_logits):
    rows, cols = queries.shape
    heads = cols // HEAD_DIM
    span = 2 * WINDOW
    cost = pl.CostEstimate(
        flops=2 * 2 * rows * span * 2 * HEAD_DIM * heads,
        transcendentals=rows * span * heads,
        bytes_accessed=2 * rows * cols * 2 + 2 * (rows + WINDOW) * key_rows.shape[1] * 2,
    )
    vmem = pl.BlockSpec(memory_space=pltpu.VMEM)
    return pl.pallas_call(
        attention_kernel,
        out_shape=jax.ShapeDtypeStruct((rows, cols), jnp.bfloat16),
        in_specs=[pl.BlockSpec(memory_space=pltpu.SMEM)] + [vmem] * 5,
        out_specs=vmem,
        cost_estimate=cost,
    )(sink_logits, queries, prior_keys, key_rows, prior_values, values)


def serve_rows(slot_rows, expert_in, expert_out):
    blocks, piece, width = slot_rows.shape
    other_rows = swap_exp(slot_rows)
    own_hidden = expert_hidden(slot_rows.reshape(-1, width), expert_in)
    own_hidden, other_rows = lax.optimization_barrier((own_hidden, other_rows))
    other_hidden = expert_hidden(other_rows.reshape(-1, width), expert_in)
    their_part = swap_exp(
        jnp.dot(other_hidden, expert_out, preferred_element_type=jnp.float32)
        .astype(jnp.bfloat16)
        .reshape(blocks, piece, width)
    )
    own_part = (
        jnp.dot(own_hidden, expert_out, preferred_element_type=jnp.float32)
        .astype(jnp.bfloat16)
        .reshape(blocks, piece, width)
    )
    return (own_part.astype(jnp.float32) + their_part.astype(jnp.float32)).astype(jnp.bfloat16)


def swap_half(x):
    return lax.ppermute(x, "half", [(0, 1), (1, 0)])


def core_rows(x, core, share):
    return lax.dynamic_slice_in_dim(x, core * share, share, 0)


def join_rows(mine, theirs, core):
    return jnp.where(core == 0, jnp.concatenate([mine, theirs], 0), jnp.concatenate([theirs, mine], 0))


def slot_ids(routes, core, half, first_expert, quads):
    experts = lax.axis_size("half") * quads
    flat = routes.reshape(-1)
    hits = (flat[:, None] == jnp.arange(experts, dtype=jnp.int32)[None, :]).astype(jnp.int32)
    rank = jnp.sum(hits * (jnp.cumsum(hits, axis=0) - 1), axis=1)
    local_rank = rank - core * half
    local_expert = flat - first_expert
    mine = (local_rank >= 0) & (local_rank < half) & (local_expert >= 0) & (local_expert < quads)
    return jnp.where(mine, local_expert * half + local_rank, -1)


def half_slot_ids(routes, core, share, first_expert, quads):
    tok_rows = routes.shape[0]
    experts = lax.axis_size("half") * quads
    flat = routes.reshape(-1)
    token = jnp.arange(tok_rows * TOP, dtype=jnp.int32) // TOP
    in_half = (token // share) == core
    hits = ((flat[:, None] == jnp.arange(experts, dtype=jnp.int32)[None, :]) & in_half[:, None]).astype(
        jnp.int32
    )
    rank = jnp.sum(hits * (jnp.cumsum(hits, axis=0) - 1), axis=1)
    local_expert = flat - first_expert
    mine = in_half & (local_expert >= 0) & (local_expert < quads)
    return jnp.where(mine, local_expert * share + rank, -1)


def dispatch(normed, ids, slots, quads, half):
    tok_rows, width = normed.shape
    pick = (ids[:, None] == jnp.arange(slots, dtype=jnp.int32)[None, :]).astype(jnp.bfloat16)
    select = jnp.max(pick.reshape(tok_rows, TOP, slots), axis=1).T
    outgoing = (
        jnp.dot(select, normed, preferred_element_type=jnp.float32)
        .astype(jnp.bfloat16)
        .reshape(quads, half, width)
    )
    return pick, outgoing


def combine(pick, returned, gates):
    tok_rows = gates.shape[0]
    slots, width = pick.shape[1], returned.shape[-1]
    picked = jnp.dot(pick, returned.reshape(slots, width), preferred_element_type=jnp.float32)
    return jnp.sum(picked.reshape(tok_rows, TOP, width) * gates[:, :, None], axis=1)


def on_device(
    queries,
    key_rows,
    values,
    cached_rows,
    sink_logits,
    out_weight,
    residual,
    norm_gain,
    expert_in,
    expert_out,
    routes,
    route_gates,
):
    tok_rows = queries.shape[0]
    window_rows = WINDOW
    quads = lax.axis_size("quad")
    side = lax.axis_index("half")
    seq_index = side * quads + lax.axis_index("quad")
    core = lax.axis_index("exp")
    rim_rows = jnp.stack([key_rows[tok_rows - window_rows :], values[tok_rows - window_rows :]])
    received = shifted(rim_rows, ("half", "quad"), 1)
    prior = jnp.where(seq_index == 0, cached_rows, received)
    pieces = attend_kernel(queries, prior[0], key_rows, prior[1], values, sink_logits)
    partial_rows = jnp.dot(pieces, out_weight, preferred_element_type=jnp.float32)
    mixed_rows = residual.astype(jnp.float32) + (partial_rows + swap_exp(partial_rows))
    normed = rms_normalize(mixed_rows, norm_gain)

    experts = lax.axis_size("half") * quads
    width = normed.shape[1]
    share = tok_rows // lax.axis_size("exp")
    capacity = 3 * tok_rows * TOP // (2 * experts)
    half = -(-capacity // 2)
    slots = quads * half
    first_expert = side * quads

    own_rows_in = core_rows(normed, core, share)
    own_ids = slot_ids(routes, core, half, first_expert, quads)
    own_pick, own_out = dispatch(normed, own_ids, slots, quads, half)
    own_out, own_rows_in = lax.optimization_barrier((own_out, own_rows_in))
    partner_part = swap_half(own_rows_in)
    partner_routes = swap_half(routes)
    partner_gates = swap_half(route_gates)
    own_arrived = lax.all_to_all(own_out, "quad", split_axis=0, concat_axis=0, tiled=True)
    partner_ids = core_rows(
        half_slot_ids(partner_routes, core, share, first_expert, quads).reshape(tok_rows, TOP),
        core,
        share,
    ).reshape(-1)
    partner_pick, partner_out = dispatch(partner_part, partner_ids, quads * share, quads, share)
    partner_arrived = lax.all_to_all(partner_out, "quad", split_axis=0, concat_axis=0, tiled=True)
    served = serve_rows(
        jnp.concatenate([own_arrived, partner_arrived], axis=1), expert_in[0], expert_out[0]
    )
    partner_back = lax.all_to_all(served[:, half:], "quad", split_axis=0, concat_axis=0, tiled=True)
    partner_rows = combine(partner_pick, partner_back, core_rows(partner_gates, core, share))
    own_served, partner_msg = lax.optimization_barrier(
        (served[:, :half], partner_rows.astype(jnp.bfloat16))
    )
    from_partner = swap_half(partner_msg)
    own_back = lax.all_to_all(own_served, "quad", split_axis=0, concat_axis=0, tiled=True)
    own_sum = combine(own_pick, own_back, route_gates)
    other_core = 1 - core
    own_rows = core_rows(own_sum, core, share) + swap_exp(core_rows(own_sum, other_core, share))
    moe_rows = own_rows + from_partner.astype(jnp.float32)
    out_rows = (core_rows(mixed_rows, core, share) + moe_rows).astype(jnp.bfloat16)
    return join_rows(out_rows, swap_exp(out_rows), core)


def solution(mesh):
    groups, seq, exp = mesh.devices.shape
    fine = jax.sharding.Mesh(
        mesh.devices.reshape(groups, 2, seq // 2, exp), ("groups", "half", "quad", "exp")
    )
    rows = ("groups", "half", "quad")
    experts = ("half", "quad")
    placed = (
        P(rows, "exp"),
        P(rows, "exp"),
        P(rows, "exp"),
        P(None, "groups", "exp"),
        P("exp"),
        P("exp", None),
        P(rows, None),
        P(),
        P(experts, None, None, "exp"),
        P(experts, "exp", None),
        P(rows, None),
        P(rows, None),
    )
    return jax.shard_map(on_device, mesh=fine, in_specs=placed, out_specs=P(rows, None), check_vma=False)
```

```python
import jax
import jax.numpy as jnp
from jax import lax
from jax.experimental import pallas as pl
from jax.experimental.pallas import tpu as pltpu
from jax.sharding import PartitionSpec as P

HEAD_DIM = 64
WINDOW = 128
TOP = 4


GLU_ALPHA = 1.702
EPSILON = 1e-05


def shifted(shard, axis, by):
    size = lax.axis_size(axis)
    pairs = [(i, i + by) for i in range(size) if 0 <= i + by < size]
    return lax.ppermute(shard, axis, pairs)


def swap_exp(x):
    size = lax.axis_size("exp")
    return lax.ppermute(x, "exp", [(i, (i + 1) % size) for i in range(size)])


def rms_normalize(mixed_rows, norm_gain):
    mean_square = jnp.mean(mixed_rows * mixed_rows, axis=-1, keepdims=True)
    return (mixed_rows * lax.rsqrt(mean_square + EPSILON) * norm_gain).astype(jnp.bfloat16)


def attend_block(queries, keys_all, values_all, sink_logits, block_rows, window_rows):
    kv_count = keys_all.shape[1] // HEAD_DIM
    group = queries.shape[1] // HEAD_DIM // kv_count
    query_block = queries.reshape(block_rows, kv_count, group, HEAD_DIM)
    key_block = keys_all.reshape(block_rows + window_rows, kv_count, HEAD_DIM)
    value_block = values_all.reshape(block_rows + window_rows, kv_count, HEAD_DIM)
    scores = jnp.einsum(
        "qhgd,khd->hgqk", query_block, key_block, preferred_element_type=jnp.float32
    ) * HEAD_DIM ** (-0.5)
    query_pos = jnp.arange(block_rows)[:, None]
    key_pos = jnp.arange(block_rows + window_rows)[None, :]
    allowed = (key_pos > query_pos) & (key_pos <= query_pos + window_rows)
    scores = jnp.where(allowed, scores, -jnp.inf)
    sink_table = sink_logits.reshape(kv_count, group)[:, :, None]
    largest = jnp.maximum(jnp.max(scores, axis=-1), sink_table)
    weights_exp = jnp.exp(scores - largest[..., None])
    denominator = jnp.exp(sink_table - largest) + jnp.sum(weights_exp, axis=-1)
    probs = (weights_exp / denominator[..., None]).astype(jnp.bfloat16)
    heads_out = jnp.einsum("hgqk,khd->qhgd", probs, value_block, preferred_element_type=jnp.float32)
    return heads_out.astype(jnp.bfloat16).reshape(block_rows, queries.shape[1])


def expert_hidden(rows, expert_in):
    gate_up = jnp.einsum("rd,kdf->krf", rows, expert_in, preferred_element_type=jnp.float32)
    gate_val = gate_up[0]
    up_val = gate_up[1]
    return ((up_val + 1.0) * gate_val * jax.nn.sigmoid(GLU_ALPHA * gate_val)).astype(jnp.bfloat16)


def attention_kernel(sink_ref, q_ref, pk_ref, k_ref, pv_ref, v_ref, w_ref, o_ref, heads_ref):
    rows = q_ref.shape[0]
    prior = pk_ref.shape[0]
    span = 2 * WINDOW
    pair_cols = 2 * HEAD_DIM
    pairs = q_ref.shape[1] // pair_cols
    kv_count = k_ref.shape[1] // HEAD_DIM
    per_kv = pairs // kv_count
    keys_all = jnp.concatenate([pk_ref[...], k_ref[...]], axis=0)
    values_all = jnp.concatenate([pv_ref[...], v_ref[...]], axis=0)
    q_pos = lax.broadcasted_iota(jnp.int32, (WINDOW, span), 0)
    k_pos = lax.broadcasted_iota(jnp.int32, (WINDOW, span), 1)
    allowed = (k_pos > q_pos) & (k_pos <= q_pos + WINDOW)
    lane_half = lax.broadcasted_iota(jnp.int32, (span, pair_cols), 1) // HEAD_DIM
    for b in range(rows // WINDOW):
        first = b * WINDOW + prior - WINDOW
        key_win = keys_all[first : first + span]
        value_win = values_all[first : first + span]
        swapped_k = pltpu.roll(key_win, HEAD_DIM, 1)
        swapped_v = pltpu.roll(value_win, HEAD_DIM, 1)
        placed = {}
        for kv in range(kv_count):
            for a in range(2):
                src_k = key_win if (kv % 2) == a else swapped_k
                src_v = value_win if (kv % 2) == a else swapped_v
                placed[kv, a] = (
                    jnp.where(lane_half == a, src_k, jnp.zeros_like(src_k)),
                    jnp.where(lane_half == a, src_v, jnp.zeros_like(src_v)),
                )
        for j in range(pairs):
            kv = j // per_kv
            q_pair = q_ref[b * WINDOW : (b + 1) * WINDOW, j * pair_cols : (j + 1) * pair_cols]
            total = None
            for a in range(2):
                k_placed, v_placed = placed[kv, a]
                scores = lax.dot_general(
                    q_pair, k_placed, (((1,), (1,)), ((), ())), preferred_element_type=jnp.float32
                ) * HEAD_DIM ** (-0.5)
                scores = jnp.where(allowed, scores, -jnp.inf)
                sink = sink_ref[2 * j + a]
                largest = jnp.maximum(jnp.max(scores, axis=-1, keepdims=True), sink)
                weights_exp = jnp.exp(scores - largest)
                denominator = jnp.exp(sink - largest) + jnp.sum(weights_exp, axis=-1, keepdims=True)
                probs = (weights_exp * (1.0 / denominator)).astype(jnp.bfloat16)
                out = jnp.dot(probs, v_placed, preferred_element_type=jnp.float32)
                total = out if total is None else total + out
            heads_ref[b * WINDOW : (b + 1) * WINDOW, j * pair_cols : (j + 1) * pair_cols] = total.astype(
                heads_ref.dtype
            )
    o_ref[...] = jnp.dot(heads_ref[...], w_ref[...], preferred_element_type=jnp.float32)


def attend_kernel(queries, prior_keys, key_rows, prior_values, values, sink_logits, out_weight):
    rows, cols = queries.shape
    heads = cols // HEAD_DIM
    span = 2 * WINDOW
    width = out_weight.shape[1]
    cost = pl.CostEstimate(
        flops=2 * 2 * rows * span * 2 * HEAD_DIM * heads + 2 * rows * cols * width,
        transcendentals=rows * span * heads,
        bytes_accessed=rows * cols * 2 + out_weight.size * 2 + rows * width * 4
        + 2 * (rows + WINDOW) * key_rows.shape[1] * 2,
    )
    vmem = pl.BlockSpec(memory_space=pltpu.VMEM)
    return pl.pallas_call(
        attention_kernel,
        out_shape=jax.ShapeDtypeStruct((rows, width), jnp.float32),
        in_specs=[pl.BlockSpec(memory_space=pltpu.SMEM)] + [vmem] * 6,
        out_specs=vmem,
        scratch_shapes=[pltpu.VMEM((rows, cols), jnp.bfloat16)],
        cost_estimate=cost,
    )(sink_logits, queries, prior_keys, key_rows, prior_values, values, out_weight)


def on_device(
    queries,
    key_rows,
    values,
    cached_rows,
    sink_logits,
    out_weight,
    residual,
    norm_gain,
    expert_in,
    expert_out,
    routes,
    route_gates,
):
    tok_rows = queries.shape[0]
    window_rows = WINDOW
    rim_rows = jnp.stack([key_rows[tok_rows - window_rows :], values[tok_rows - window_rows :]])
    received = shifted(rim_rows, "seq", 1)
    prior = jnp.where(lax.axis_index("seq") == 0, cached_rows, received)
    partial_rows = attend_kernel(queries, prior[0], key_rows, prior[1], values, sink_logits, out_weight)
    mixed_rows = residual.astype(jnp.float32) + (partial_rows + swap_exp(partial_rows))
    normed = rms_normalize(mixed_rows, norm_gain)

    experts = lax.axis_size("seq")
    width = normed.shape[1]
    capacity = 3 * tok_rows * TOP // (2 * experts)
    half = -(-capacity // 2)
    slots = experts * half
    core = lax.axis_index("exp")
    flat_experts = routes.reshape(-1)
    expert_hits = (flat_experts[:, None] == jnp.arange(experts, dtype=jnp.int32)[None, :]).astype(
        jnp.int32
    )
    slot_rank = jnp.sum(expert_hits * (jnp.cumsum(expert_hits, axis=0) - 1), axis=1)
    local_rank = slot_rank - core * half
    mine = (local_rank >= 0) & (local_rank < half)
    slot_id = jnp.where(mine, flat_experts * half + local_rank, -1)
    slot_iota = jnp.arange(slots, dtype=jnp.int32)
    pick = (slot_id[:, None] == slot_iota[None, :]).astype(jnp.bfloat16)
    select = jnp.max(pick.reshape(tok_rows, TOP, slots), axis=1).T
    outgoing = (
        jnp.dot(select, normed, preferred_element_type=jnp.float32)
        .astype(jnp.bfloat16)
        .reshape(experts, half, width)
    )
    slot_rows = lax.all_to_all(outgoing, "seq", split_axis=0, concat_axis=0, tiled=True)
    other_rows = swap_exp(slot_rows)
    own_hidden = expert_hidden(slot_rows.reshape(-1, width), expert_in[0])
    own_hidden, other_rows = lax.optimization_barrier((own_hidden, other_rows))
    other_hidden = expert_hidden(other_rows.reshape(-1, width), expert_in[0])
    their_part = swap_exp(
        jnp.dot(other_hidden, expert_out[0], preferred_element_type=jnp.float32)
        .astype(jnp.bfloat16)
        .reshape(experts, half, width)
    )
    own_part = (
        jnp.dot(own_hidden, expert_out[0], preferred_element_type=jnp.float32)
        .astype(jnp.bfloat16)
        .reshape(experts, half, width)
    )
    result = (own_part.astype(jnp.float32) + their_part.astype(jnp.float32)).astype(jnp.bfloat16)
    returned = lax.all_to_all(result, "seq", split_axis=0, concat_axis=0, tiled=True)
    picked = jnp.dot(pick, returned.reshape(slots, width), preferred_element_type=jnp.float32)
    weighted = jnp.sum(picked.reshape(tok_rows, TOP, width) * route_gates[:, :, None], axis=1)
    moe = weighted + swap_exp(weighted)
    return (mixed_rows + moe).astype(jnp.bfloat16)


def solution(mesh):
    placed = (
        P(("groups", "seq"), "exp"),
        P(("groups", "seq"), "exp"),
        P(("groups", "seq"), "exp"),
        P(None, "groups", "exp"),
        P("exp"),
        P("exp", None),
        P(("groups", "seq"), None),
        P(),
        P("seq", None, None, "exp"),
        P("seq", "exp", None),
        P(("groups", "seq"), None),
        P(("groups", "seq"), None),
    )
    return jax.shard_map(
        on_device, mesh=mesh, in_specs=placed, out_specs=P(("groups", "seq"), None), check_vma=False
    )
```

```python
import jax
import jax.numpy as jnp
from jax import lax
from jax.experimental import pallas as pl
from jax.experimental.pallas import tpu as pltpu
from jax.sharding import PartitionSpec as P

HEAD_DIM = 64
WINDOW = 128
TOP = 4


GLU_ALPHA = 1.702
EPSILON = 1e-05


def shifted(shard, axis, by):
    size = lax.axis_size(axis)
    pairs = [(i, i + by) for i in range(size) if 0 <= i + by < size]
    return lax.ppermute(shard, axis, pairs)


def swap_exp(x):
    size = lax.axis_size("exp")
    return lax.ppermute(x, "exp", [(i, (i + 1) % size) for i in range(size)])


def rms_normalize(mixed_rows, norm_gain):
    mean_square = jnp.mean(mixed_rows * mixed_rows, axis=-1, keepdims=True)
    return (mixed_rows * lax.rsqrt(mean_square + EPSILON) * norm_gain).astype(jnp.bfloat16)


def attend_block(queries, keys_all, values_all, sink_logits, block_rows, window_rows):
    kv_count = keys_all.shape[1] // HEAD_DIM
    group = queries.shape[1] // HEAD_DIM // kv_count
    query_block = queries.reshape(block_rows, kv_count, group, HEAD_DIM)
    key_block = keys_all.reshape(block_rows + window_rows, kv_count, HEAD_DIM)
    value_block = values_all.reshape(block_rows + window_rows, kv_count, HEAD_DIM)
    scores = jnp.einsum(
        "qhgd,khd->hgqk", query_block, key_block, preferred_element_type=jnp.float32
    ) * HEAD_DIM ** (-0.5)
    query_pos = jnp.arange(block_rows)[:, None]
    key_pos = jnp.arange(block_rows + window_rows)[None, :]
    allowed = (key_pos > query_pos) & (key_pos <= query_pos + window_rows)
    scores = jnp.where(allowed, scores, -jnp.inf)
    sink_table = sink_logits.reshape(kv_count, group)[:, :, None]
    largest = jnp.maximum(jnp.max(scores, axis=-1), sink_table)
    weights_exp = jnp.exp(scores - largest[..., None])
    denominator = jnp.exp(sink_table - largest) + jnp.sum(weights_exp, axis=-1)
    probs = (weights_exp / denominator[..., None]).astype(jnp.bfloat16)
    heads_out = jnp.einsum("hgqk,khd->qhgd", probs, value_block, preferred_element_type=jnp.float32)
    return heads_out.astype(jnp.bfloat16).reshape(block_rows, queries.shape[1])


def expert_hidden(rows, expert_in):
    gate_up = jnp.einsum("rd,kdf->krf", rows, expert_in, preferred_element_type=jnp.float32)
    gate_val = gate_up[0]
    up_val = gate_up[1]
    return ((up_val + 1.0) * gate_val * jax.nn.sigmoid(GLU_ALPHA * gate_val)).astype(jnp.bfloat16)


def attention_kernel(sink_ref, q_ref, k_ref, v_ref, w_ref, *rest):
    o_ref, heads_ref = rest[-2], rest[-1]
    span = k_ref.shape[0]
    pair_cols = 2 * HEAD_DIM
    pairs = q_ref.shape[1] // pair_cols
    kv_count = k_ref.shape[1] // HEAD_DIM
    per_kv = pairs // kv_count
    q_pos = lax.broadcasted_iota(jnp.int32, (WINDOW, span), 0)
    k_pos = lax.broadcasted_iota(jnp.int32, (WINDOW, span), 1)
    allowed = (k_pos > q_pos) & (k_pos <= q_pos + WINDOW)
    lane_half = lax.broadcasted_iota(jnp.int32, (span, pair_cols), 1) // HEAD_DIM
    key_win = k_ref[...]
    value_win = v_ref[...]
    swapped_k = pltpu.roll(key_win, HEAD_DIM, 1)
    swapped_v = pltpu.roll(value_win, HEAD_DIM, 1)
    placed = {}
    for kv in range(kv_count):
        for a in range(2):
            src_k = key_win if (kv % 2) == a else swapped_k
            src_v = value_win if (kv % 2) == a else swapped_v
            placed[kv, a] = (
                jnp.where(lane_half == a, src_k, jnp.zeros_like(src_k)),
                jnp.where(lane_half == a, src_v, jnp.zeros_like(src_v)),
            )
    for j in range(pairs):
        kv = j // per_kv
        q_pair = q_ref[:, j * pair_cols : (j + 1) * pair_cols]
        total = None
        for a in range(2):
            k_placed, v_placed = placed[kv, a]
            scores = lax.dot_general(
                q_pair, k_placed, (((1,), (1,)), ((), ())), preferred_element_type=jnp.float32
            ) * HEAD_DIM ** (-0.5)
            scores = jnp.where(allowed, scores, -jnp.inf)
            sink = sink_ref[2 * j + a]
            largest = jnp.maximum(jnp.max(scores, axis=-1, keepdims=True), sink)
            weights_exp = jnp.exp(scores - largest)
            denominator = jnp.exp(sink - largest) + jnp.sum(weights_exp, axis=-1, keepdims=True)
            probs = (weights_exp * (1.0 / denominator)).astype(jnp.bfloat16)
            out = jnp.dot(probs, v_placed, preferred_element_type=jnp.float32)
            total = out if total is None else total + out
        heads_ref[:, j * pair_cols : (j + 1) * pair_cols] = total.astype(heads_ref.dtype)
    o_ref[...] = jnp.dot(heads_ref[...], w_ref[...], preferred_element_type=jnp.float32)


def attend_rows(block, queries, key_win, value_win, sink_logits, out_weight, into=None):
    rows, cols = queries.shape
    heads = cols // HEAD_DIM
    span = key_win.shape[0]
    width = out_weight.shape[1]
    cost = pl.CostEstimate(
        flops=2 * 2 * WINDOW * span * 2 * HEAD_DIM * heads + 2 * WINDOW * cols * width,
        transcendentals=WINDOW * span * heads,
        bytes_accessed=WINDOW * cols * 2 + out_weight.size * 2 + WINDOW * width * 4 + 2 * key_win.size * 2,
    )
    whole = lambda shape: pl.BlockSpec(shape, lambda i: (0, 0))
    in_specs = [
        pl.BlockSpec(memory_space=pltpu.SMEM),
        pl.BlockSpec((WINDOW, cols), lambda i: (block, 0)),
        whole(key_win.shape),
        whole(value_win.shape),
        whole(out_weight.shape),
    ]
    args = [sink_logits, queries, key_win, value_win, out_weight]
    aliases = {}
    if into is not None:
        in_specs.append(pl.BlockSpec(memory_space=pl.ANY))
        args.append(into)
        aliases = {len(args) - 1: 0}
    return pl.pallas_call(
        attention_kernel,
        out_shape=jax.ShapeDtypeStruct((rows, width), jnp.float32),
        in_specs=in_specs,
        out_specs=pl.BlockSpec((WINDOW, width), lambda i: (block, 0)),
        grid=(1,),
        scratch_shapes=[pltpu.VMEM((WINDOW, cols), jnp.bfloat16)],
        input_output_aliases=aliases,
        cost_estimate=cost,
    )(*args)


def attend_kernel(queries, prior_keys, key_rows, prior_values, values, sink_logits, out_weight):
    rows = queries.shape[0]
    blocks = rows // WINDOW
    result = None
    for block in range(blocks - 1, 0, -1):
        first = (block - 1) * WINDOW
        result = attend_rows(
            block,
            queries,
            key_rows[first : first + 2 * WINDOW],
            values[first : first + 2 * WINDOW],
            sink_logits,
            out_weight,
            result,
        )
    key_win = jnp.concatenate([prior_keys, key_rows[:WINDOW]], axis=0)
    value_win = jnp.concatenate([prior_values, values[:WINDOW]], axis=0)
    return attend_rows(0, queries, key_win, value_win, sink_logits, out_weight, result)


def on_device(
    queries,
    key_rows,
    values,
    cached_rows,
    sink_logits,
    out_weight,
    residual,
    norm_gain,
    expert_in,
    expert_out,
    routes,
    route_gates,
):
    tok_rows = queries.shape[0]
    window_rows = WINDOW
    rim_rows = jnp.stack([key_rows[tok_rows - window_rows :], values[tok_rows - window_rows :]])
    received = shifted(rim_rows, "seq", 1)
    prior = jnp.where(lax.axis_index("seq") == 0, cached_rows, received)
    partial_rows = attend_kernel(queries, prior[0], key_rows, prior[1], values, sink_logits, out_weight)
    mixed_rows = residual.astype(jnp.float32) + (partial_rows + swap_exp(partial_rows))
    normed = rms_normalize(mixed_rows, norm_gain)

    experts = lax.axis_size("seq")
    width = normed.shape[1]
    capacity = 3 * tok_rows * TOP // (2 * experts)
    half = -(-capacity // 2)
    slots = experts * half
    core = lax.axis_index("exp")
    flat_experts = routes.reshape(-1)
    expert_hits = (flat_experts[:, None] == jnp.arange(experts, dtype=jnp.int32)[None, :]).astype(
        jnp.int32
    )
    slot_rank = jnp.sum(expert_hits * (jnp.cumsum(expert_hits, axis=0) - 1), axis=1)
    local_rank = slot_rank - core * half
    mine = (local_rank >= 0) & (local_rank < half)
    slot_id = jnp.where(mine, flat_experts * half + local_rank, -1)
    slot_iota = jnp.arange(slots, dtype=jnp.int32)
    pick = (slot_id[:, None] == slot_iota[None, :]).astype(jnp.bfloat16)
    select = jnp.max(pick.reshape(tok_rows, TOP, slots), axis=1).T
    outgoing = (
        jnp.dot(select, normed, preferred_element_type=jnp.float32)
        .astype(jnp.bfloat16)
        .reshape(experts, half, width)
    )
    slot_rows = lax.all_to_all(outgoing, "seq", split_axis=0, concat_axis=0, tiled=True)
    other_rows = swap_exp(slot_rows)
    own_hidden = expert_hidden(slot_rows.reshape(-1, width), expert_in[0])
    own_hidden, other_rows = lax.optimization_barrier((own_hidden, other_rows))
    other_hidden = expert_hidden(other_rows.reshape(-1, width), expert_in[0])
    their_part = swap_exp(
        jnp.dot(other_hidden, expert_out[0], preferred_element_type=jnp.float32)
        .astype(jnp.bfloat16)
        .reshape(experts, half, width)
    )
    own_part = (
        jnp.dot(own_hidden, expert_out[0], preferred_element_type=jnp.float32)
        .astype(jnp.bfloat16)
        .reshape(experts, half, width)
    )
    result = (own_part.astype(jnp.float32) + their_part.astype(jnp.float32)).astype(jnp.bfloat16)
    returned = lax.all_to_all(result, "seq", split_axis=0, concat_axis=0, tiled=True)
    picked = jnp.dot(pick, returned.reshape(slots, width), preferred_element_type=jnp.float32)
    weighted = jnp.sum(picked.reshape(tok_rows, TOP, width) * route_gates[:, :, None], axis=1)
    moe = weighted + swap_exp(weighted)
    return (mixed_rows + moe).astype(jnp.bfloat16)


def solution(mesh):
    placed = (
        P(("groups", "seq"), "exp"),
        P(("groups", "seq"), "exp"),
        P(("groups", "seq"), "exp"),
        P(None, "groups", "exp"),
        P("exp"),
        P("exp", None),
        P(("groups", "seq"), None),
        P(),
        P("seq", None, None, "exp"),
        P("seq", "exp", None),
        P(("groups", "seq"), None),
        P(("groups", "seq"), None),
    )
    return jax.shard_map(
        on_device, mesh=mesh, in_specs=placed, out_specs=P(("groups", "seq"), None), check_vma=False
    )
```

```python
import jax
import jax.numpy as jnp
from jax import lax
from jax.experimental import pallas as pl
from jax.experimental.pallas import tpu as pltpu
from jax.sharding import PartitionSpec as P

HEAD_DIM = 64
WINDOW = 128
TOP = 4
SHIFT_LIMIT = 8


GLU_ALPHA = 1.702
EPSILON = 1e-05


def shifted(shard, axis, by):
    size = lax.axis_size(axis)
    pairs = [(i, i + by) for i in range(size) if 0 <= i + by < size]
    return lax.ppermute(shard, axis, pairs)


def swap_exp(x):
    size = lax.axis_size("exp")
    return lax.ppermute(x, "exp", [(i, (i + 1) % size) for i in range(size)])


def seq_all_to_all(blocks):
    return lax.all_to_all(blocks, "seq", split_axis=0, concat_axis=0, tiled=True)


def shift_exchange(blocks, sign):
    size = lax.axis_size("seq")
    out = [blocks[0]]
    for step in range(1, size):
        pairs = [(i, (i + sign * step) % size) for i in range(size)]
        out.append(lax.ppermute(blocks[step], "seq", pairs))
    return jnp.stack(out)


def rms_normalize(mixed_rows, norm_gain):
    mean_square = jnp.mean(mixed_rows * mixed_rows, axis=-1, keepdims=True)
    return (mixed_rows * lax.rsqrt(mean_square + EPSILON) * norm_gain).astype(jnp.bfloat16)


def attend_block(queries, keys_all, values_all, sink_logits, block_rows, window_rows):
    kv_count = keys_all.shape[1] // HEAD_DIM
    group = queries.shape[1] // HEAD_DIM // kv_count
    query_block = queries.reshape(block_rows, kv_count, group, HEAD_DIM)
    key_block = keys_all.reshape(block_rows + window_rows, kv_count, HEAD_DIM)
    value_block = values_all.reshape(block_rows + window_rows, kv_count, HEAD_DIM)
    scores = jnp.einsum(
        "qhgd,khd->hgqk", query_block, key_block, preferred_element_type=jnp.float32
    ) * HEAD_DIM ** (-0.5)
    query_pos = jnp.arange(block_rows)[:, None]
    key_pos = jnp.arange(block_rows + window_rows)[None, :]
    allowed = (key_pos > query_pos) & (key_pos <= query_pos + window_rows)
    scores = jnp.where(allowed, scores, -jnp.inf)
    sink_table = sink_logits.reshape(kv_count, group)[:, :, None]
    largest = jnp.maximum(jnp.max(scores, axis=-1), sink_table)
    weights_exp = jnp.exp(scores - largest[..., None])
    denominator = jnp.exp(sink_table - largest) + jnp.sum(weights_exp, axis=-1)
    probs = (weights_exp / denominator[..., None]).astype(jnp.bfloat16)
    heads_out = jnp.einsum("hgqk,khd->qhgd", probs, value_block, preferred_element_type=jnp.float32)
    return heads_out.astype(jnp.bfloat16).reshape(block_rows, queries.shape[1])


def expert_hidden(rows, expert_in):
    gate_up = jnp.einsum("rd,kdf->krf", rows, expert_in, preferred_element_type=jnp.float32)
    gate_val = gate_up[0]
    up_val = gate_up[1]
    return ((up_val + 1.0) * gate_val * jax.nn.sigmoid(GLU_ALPHA * gate_val)).astype(jnp.bfloat16)


def attention_kernel(sink_ref, q_ref, pk_ref, k_ref, pv_ref, v_ref, w_ref, o_ref, heads_ref):
    rows = q_ref.shape[0]
    prior = pk_ref.shape[0]
    span = 2 * WINDOW
    pair_cols = 2 * HEAD_DIM
    pairs = q_ref.shape[1] // pair_cols
    kv_count = k_ref.shape[1] // HEAD_DIM
    per_kv = pairs // kv_count
    keys_all = jnp.concatenate([pk_ref[...], k_ref[...]], axis=0)
    values_all = jnp.concatenate([pv_ref[...], v_ref[...]], axis=0)
    q_pos = lax.broadcasted_iota(jnp.int32, (WINDOW, span), 0)
    k_pos = lax.broadcasted_iota(jnp.int32, (WINDOW, span), 1)
    allowed = (k_pos > q_pos) & (k_pos <= q_pos + WINDOW)
    lane_half = lax.broadcasted_iota(jnp.int32, (span, pair_cols), 1) // HEAD_DIM
    for b in range(rows // WINDOW):
        first = b * WINDOW + prior - WINDOW
        key_win = keys_all[first : first + span]
        value_win = values_all[first : first + span]
        swapped_k = pltpu.roll(key_win, HEAD_DIM, 1)
        swapped_v = pltpu.roll(value_win, HEAD_DIM, 1)
        placed = {}
        for kv in range(kv_count):
            for a in range(2):
                src_k = key_win if (kv % 2) == a else swapped_k
                src_v = value_win if (kv % 2) == a else swapped_v
                placed[kv, a] = (
                    jnp.where(lane_half == a, src_k, jnp.zeros_like(src_k)),
                    jnp.where(lane_half == a, src_v, jnp.zeros_like(src_v)),
                )
        for j in range(pairs):
            kv = j // per_kv
            q_pair = q_ref[b * WINDOW : (b + 1) * WINDOW, j * pair_cols : (j + 1) * pair_cols]
            total = None
            for a in range(2):
                k_placed, v_placed = placed[kv, a]
                scores = lax.dot_general(
                    q_pair, k_placed, (((1,), (1,)), ((), ())), preferred_element_type=jnp.float32
                ) * HEAD_DIM ** (-0.5)
                scores = jnp.where(allowed, scores, -jnp.inf)
                sink = sink_ref[2 * j + a]
                largest = jnp.maximum(jnp.max(scores, axis=-1, keepdims=True), sink)
                weights_exp = jnp.exp(scores - largest)
                denominator = jnp.exp(sink - largest) + jnp.sum(weights_exp, axis=-1, keepdims=True)
                probs = (weights_exp * (1.0 / denominator)).astype(jnp.bfloat16)
                out = jnp.dot(probs, v_placed, preferred_element_type=jnp.float32)
                total = out if total is None else total + out
            heads_ref[b * WINDOW : (b + 1) * WINDOW, j * pair_cols : (j + 1) * pair_cols] = total.astype(
                heads_ref.dtype
            )
    o_ref[...] = jnp.dot(heads_ref[...], w_ref[...], preferred_element_type=jnp.float32)


def attend_kernel(queries, prior_keys, key_rows, prior_values, values, sink_logits, out_weight):
    rows, cols = queries.shape
    heads = cols // HEAD_DIM
    span = 2 * WINDOW
    width = out_weight.shape[1]
    cost = pl.CostEstimate(
        flops=2 * 2 * rows * span * 2 * HEAD_DIM * heads + 2 * rows * cols * width,
        transcendentals=rows * span * heads,
        bytes_accessed=rows * cols * 2 + out_weight.size * 2 + rows * width * 4
        + 2 * (rows + WINDOW) * key_rows.shape[1] * 2,
    )
    vmem = pl.BlockSpec(memory_space=pltpu.VMEM)
    return pl.pallas_call(
        attention_kernel,
        out_shape=jax.ShapeDtypeStruct((rows, width), jnp.float32),
        in_specs=[pl.BlockSpec(memory_space=pltpu.SMEM)] + [vmem] * 6,
        out_specs=vmem,
        scratch_shapes=[pltpu.VMEM((rows, cols), jnp.bfloat16)],
        cost_estimate=cost,
    )(sink_logits, queries, prior_keys, key_rows, prior_values, values, out_weight)


def on_device(
    queries,
    key_rows,
    values,
    cached_rows,
    sink_logits,
    out_weight,
    residual,
    norm_gain,
    expert_in,
    expert_out,
    routes,
    route_gates,
):
    tok_rows = queries.shape[0]
    window_rows = WINDOW
    rim_rows = jnp.stack([key_rows[tok_rows - window_rows :], values[tok_rows - window_rows :]])
    received = shifted(rim_rows, "seq", 1)
    prior = jnp.where(lax.axis_index("seq") == 0, cached_rows, received)
    partial_rows = attend_kernel(queries, prior[0], key_rows, prior[1], values, sink_logits, out_weight)
    mixed_rows = residual.astype(jnp.float32) + (partial_rows + swap_exp(partial_rows))
    normed = rms_normalize(mixed_rows, norm_gain)

    experts = lax.axis_size("seq")
    width = normed.shape[1]
    capacity = 3 * tok_rows * TOP // (2 * experts)
    half = -(-capacity // 2)
    slots = experts * half
    core = lax.axis_index("exp")
    flat_experts = routes.reshape(-1)
    expert_hits = (flat_experts[:, None] == jnp.arange(experts, dtype=jnp.int32)[None, :]).astype(
        jnp.int32
    )
    slot_rank = jnp.sum(expert_hits * (jnp.cumsum(expert_hits, axis=0) - 1), axis=1)
    local_rank = slot_rank - core * half
    mine = (local_rank >= 0) & (local_rank < half)
    by_shift = experts <= SHIFT_LIMIT
    offset = (flat_experts - lax.axis_index("seq")) % experts if by_shift else flat_experts
    slot_id = jnp.where(mine, offset * half + local_rank, -1)
    slot_iota = jnp.arange(slots, dtype=jnp.int32)
    pick = (slot_id[:, None] == slot_iota[None, :]).astype(jnp.bfloat16)
    select = jnp.max(pick.reshape(tok_rows, TOP, slots), axis=1).T
    outgoing = (
        jnp.dot(select, normed, preferred_element_type=jnp.float32)
        .astype(jnp.bfloat16)
        .reshape(experts, half, width)
    )
    slot_rows = shift_exchange(outgoing, 1) if by_shift else seq_all_to_all(outgoing)
    other_rows = swap_exp(slot_rows)
    own_hidden = expert_hidden(slot_rows.reshape(-1, width), expert_in[0])
    own_hidden, other_rows = lax.optimization_barrier((own_hidden, other_rows))
    other_hidden = expert_hidden(other_rows.reshape(-1, width), expert_in[0])
    their_part = swap_exp(
        jnp.dot(other_hidden, expert_out[0], preferred_element_type=jnp.float32)
        .astype(jnp.bfloat16)
        .reshape(experts, half, width)
    )
    own_part = (
        jnp.dot(own_hidden, expert_out[0], preferred_element_type=jnp.float32)
        .astype(jnp.bfloat16)
        .reshape(experts, half, width)
    )
    result = (own_part.astype(jnp.float32) + their_part.astype(jnp.float32)).astype(jnp.bfloat16)
    returned = shift_exchange(result, -1) if by_shift else seq_all_to_all(result)
    picked = jnp.dot(pick, returned.reshape(slots, width), preferred_element_type=jnp.float32)
    weighted = jnp.sum(picked.reshape(tok_rows, TOP, width) * route_gates[:, :, None], axis=1)
    moe = weighted + swap_exp(weighted)
    return (mixed_rows + moe).astype(jnp.bfloat16)


def solution(mesh):
    placed = (
        P(("groups", "seq"), "exp"),
        P(("groups", "seq"), "exp"),
        P(("groups", "seq"), "exp"),
        P(None, "groups", "exp"),
        P("exp"),
        P("exp", None),
        P(("groups", "seq"), None),
        P(),
        P("seq", None, None, "exp"),
        P("seq", "exp", None),
        P(("groups", "seq"), None),
        P(("groups", "seq"), None),
    )
    return jax.shard_map(
        on_device, mesh=mesh, in_specs=placed, out_specs=P(("groups", "seq"), None), check_vma=False
    )
```

```python
import jax
import jax.numpy as jnp
from jax import lax
from jax.experimental import pallas as pl
from jax.experimental.pallas import tpu as pltpu
from jax.sharding import PartitionSpec as P

HEAD_DIM = 64
WINDOW = 128
TOP = 4
SHIFT_LIMIT = 8


GLU_ALPHA = 1.702
EPSILON = 1e-05


def shifted(shard, axis, by):
    size = lax.axis_size(axis)
    pairs = [(i, i + by) for i in range(size) if 0 <= i + by < size]
    return lax.ppermute(shard, axis, pairs)


def swap_exp(x):
    size = lax.axis_size("exp")
    return lax.ppermute(x, "exp", [(i, (i + 1) % size) for i in range(size)])


def seq_all_to_all(blocks):
    return lax.all_to_all(blocks, "seq", split_axis=0, concat_axis=0, tiled=True)


def shift_exchange(blocks, sign):
    size = lax.axis_size("seq")
    out = {0: blocks[0]}
    steps = range(1, size) if sign > 0 else range(size - 1, 0, -1)
    for step in steps:
        pairs = [(i, (i + sign * step) % size) for i in range(size)]
        out[step] = lax.ppermute(blocks[step], "seq", pairs)
    return jnp.stack([out[step] for step in range(size)])


def rms_normalize(mixed_rows, norm_gain):
    mean_square = jnp.mean(mixed_rows * mixed_rows, axis=-1, keepdims=True)
    return (mixed_rows * lax.rsqrt(mean_square + EPSILON) * norm_gain).astype(jnp.bfloat16)


def attend_block(queries, keys_all, values_all, sink_logits, block_rows, window_rows):
    kv_count = keys_all.shape[1] // HEAD_DIM
    group = queries.shape[1] // HEAD_DIM // kv_count
    query_block = queries.reshape(block_rows, kv_count, group, HEAD_DIM)
    key_block = keys_all.reshape(block_rows + window_rows, kv_count, HEAD_DIM)
    value_block = values_all.reshape(block_rows + window_rows, kv_count, HEAD_DIM)
    scores = jnp.einsum(
        "qhgd,khd->hgqk", query_block, key_block, preferred_element_type=jnp.float32
    ) * HEAD_DIM ** (-0.5)
    query_pos = jnp.arange(block_rows)[:, None]
    key_pos = jnp.arange(block_rows + window_rows)[None, :]
    allowed = (key_pos > query_pos) & (key_pos <= query_pos + window_rows)
    scores = jnp.where(allowed, scores, -jnp.inf)
    sink_table = sink_logits.reshape(kv_count, group)[:, :, None]
    largest = jnp.maximum(jnp.max(scores, axis=-1), sink_table)
    weights_exp = jnp.exp(scores - largest[..., None])
    denominator = jnp.exp(sink_table - largest) + jnp.sum(weights_exp, axis=-1)
    probs = (weights_exp / denominator[..., None]).astype(jnp.bfloat16)
    heads_out = jnp.einsum("hgqk,khd->qhgd", probs, value_block, preferred_element_type=jnp.float32)
    return heads_out.astype(jnp.bfloat16).reshape(block_rows, queries.shape[1])


def expert_hidden(rows, expert_in):
    gate_up = jnp.einsum("rd,kdf->krf", rows, expert_in, preferred_element_type=jnp.float32)
    gate_val = gate_up[0]
    up_val = gate_up[1]
    return ((up_val + 1.0) * gate_val * jax.nn.sigmoid(GLU_ALPHA * gate_val)).astype(jnp.bfloat16)


def attention_kernel(sink_ref, q_ref, pk_ref, k_ref, pv_ref, v_ref, w_ref, o_ref, heads_ref):
    rows = q_ref.shape[0]
    prior = pk_ref.shape[0]
    span = 2 * WINDOW
    pair_cols = 2 * HEAD_DIM
    pairs = q_ref.shape[1] // pair_cols
    kv_count = k_ref.shape[1] // HEAD_DIM
    per_kv = pairs // kv_count
    keys_all = jnp.concatenate([pk_ref[...], k_ref[...]], axis=0)
    values_all = jnp.concatenate([pv_ref[...], v_ref[...]], axis=0)
    q_pos = lax.broadcasted_iota(jnp.int32, (WINDOW, span), 0)
    k_pos = lax.broadcasted_iota(jnp.int32, (WINDOW, span), 1)
    allowed = (k_pos > q_pos) & (k_pos <= q_pos + WINDOW)
    lane_half = lax.broadcasted_iota(jnp.int32, (span, pair_cols), 1) // HEAD_DIM
    for b in range(rows // WINDOW):
        first = b * WINDOW + prior - WINDOW
        key_win = keys_all[first : first + span]
        value_win = values_all[first : first + span]
        swapped_k = pltpu.roll(key_win, HEAD_DIM, 1)
        swapped_v = pltpu.roll(value_win, HEAD_DIM, 1)
        placed = {}
        for kv in range(kv_count):
            for a in range(2):
                src_k = key_win if (kv % 2) == a else swapped_k
                src_v = value_win if (kv % 2) == a else swapped_v
                placed[kv, a] = (
                    jnp.where(lane_half == a, src_k, jnp.zeros_like(src_k)),
                    jnp.where(lane_half == a, src_v, jnp.zeros_like(src_v)),
                )
        for j in range(pairs):
            kv = j // per_kv
            q_pair = q_ref[b * WINDOW : (b + 1) * WINDOW, j * pair_cols : (j + 1) * pair_cols]
            total = None
            for a in range(2):
                k_placed, v_placed = placed[kv, a]
                scores = lax.dot_general(
                    q_pair, k_placed, (((1,), (1,)), ((), ())), preferred_element_type=jnp.float32
                ) * HEAD_DIM ** (-0.5)
                scores = jnp.where(allowed, scores, -jnp.inf)
                sink = sink_ref[2 * j + a]
                largest = jnp.maximum(jnp.max(scores, axis=-1, keepdims=True), sink)
                weights_exp = jnp.exp(scores - largest)
                denominator = jnp.exp(sink - largest) + jnp.sum(weights_exp, axis=-1, keepdims=True)
                probs = (weights_exp * (1.0 / denominator)).astype(jnp.bfloat16)
                out = jnp.dot(probs, v_placed, preferred_element_type=jnp.float32)
                total = out if total is None else total + out
            heads_ref[b * WINDOW : (b + 1) * WINDOW, j * pair_cols : (j + 1) * pair_cols] = total.astype(
                heads_ref.dtype
            )
    o_ref[...] = jnp.dot(heads_ref[...], w_ref[...], preferred_element_type=jnp.float32)


def attend_kernel(queries, prior_keys, key_rows, prior_values, values, sink_logits, out_weight):
    rows, cols = queries.shape
    heads = cols // HEAD_DIM
    span = 2 * WINDOW
    width = out_weight.shape[1]
    cost = pl.CostEstimate(
        flops=2 * 2 * rows * span * 2 * HEAD_DIM * heads + 2 * rows * cols * width,
        transcendentals=rows * span * heads,
        bytes_accessed=rows * cols * 2 + out_weight.size * 2 + rows * width * 4
        + 2 * (rows + WINDOW) * key_rows.shape[1] * 2,
    )
    vmem = pl.BlockSpec(memory_space=pltpu.VMEM)
    return pl.pallas_call(
        attention_kernel,
        out_shape=jax.ShapeDtypeStruct((rows, width), jnp.float32),
        in_specs=[pl.BlockSpec(memory_space=pltpu.SMEM)] + [vmem] * 6,
        out_specs=vmem,
        scratch_shapes=[pltpu.VMEM((rows, cols), jnp.bfloat16)],
        cost_estimate=cost,
    )(sink_logits, queries, prior_keys, key_rows, prior_values, values, out_weight)


def on_device(
    queries,
    key_rows,
    values,
    cached_rows,
    sink_logits,
    out_weight,
    residual,
    norm_gain,
    expert_in,
    expert_out,
    routes,
    route_gates,
):
    tok_rows = queries.shape[0]
    window_rows = WINDOW
    rim_rows = jnp.stack([key_rows[tok_rows - window_rows :], values[tok_rows - window_rows :]])
    received = shifted(rim_rows, "seq", 1)
    prior = jnp.where(lax.axis_index("seq") == 0, cached_rows, received)
    partial_rows = attend_kernel(queries, prior[0], key_rows, prior[1], values, sink_logits, out_weight)
    mixed_rows = residual.astype(jnp.float32) + (partial_rows + swap_exp(partial_rows))
    normed = rms_normalize(mixed_rows, norm_gain)

    experts = lax.axis_size("seq")
    width = normed.shape[1]
    capacity = 3 * tok_rows * TOP // (2 * experts)
    half = -(-capacity // 2)
    slots = experts * half
    core = lax.axis_index("exp")
    flat_experts = routes.reshape(-1)
    expert_hits = (flat_experts[:, None] == jnp.arange(experts, dtype=jnp.int32)[None, :]).astype(
        jnp.int32
    )
    slot_rank = jnp.sum(expert_hits * (jnp.cumsum(expert_hits, axis=0) - 1), axis=1)
    local_rank = slot_rank - core * half
    mine = (local_rank >= 0) & (local_rank < half)
    by_shift = experts <= SHIFT_LIMIT
    offset = (flat_experts - lax.axis_index("seq")) % experts if by_shift else flat_experts
    slot_id = jnp.where(mine, offset * half + local_rank, -1)
    slot_iota = jnp.arange(slots, dtype=jnp.int32)
    pick = (slot_id[:, None] == slot_iota[None, :]).astype(jnp.bfloat16)
    select = jnp.max(pick.reshape(tok_rows, TOP, slots), axis=1).T
    outgoing = (
        jnp.dot(select, normed, preferred_element_type=jnp.float32)
        .astype(jnp.bfloat16)
        .reshape(experts, half, width)
    )
    slot_rows = shift_exchange(outgoing, 1) if by_shift else seq_all_to_all(outgoing)
    other_rows = swap_exp(slot_rows)
    own_hidden = expert_hidden(slot_rows.reshape(-1, width), expert_in[0])
    own_hidden, other_rows = lax.optimization_barrier((own_hidden, other_rows))
    other_hidden = expert_hidden(other_rows.reshape(-1, width), expert_in[0])
    their_part = swap_exp(
        jnp.dot(other_hidden, expert_out[0], preferred_element_type=jnp.float32)
        .astype(jnp.bfloat16)
        .reshape(experts, half, width)
    )
    own_part = (
        jnp.dot(own_hidden, expert_out[0], preferred_element_type=jnp.float32)
        .astype(jnp.bfloat16)
        .reshape(experts, half, width)
    )
    result = (own_part.astype(jnp.float32) + their_part.astype(jnp.float32)).astype(jnp.bfloat16)
    returned = shift_exchange(result, -1) if by_shift else seq_all_to_all(result)
    picked = jnp.dot(pick, returned.reshape(slots, width), preferred_element_type=jnp.float32)
    weighted = jnp.sum(picked.reshape(tok_rows, TOP, width) * route_gates[:, :, None], axis=1)
    moe = weighted + swap_exp(weighted)
    return (mixed_rows + moe).astype(jnp.bfloat16)


def solution(mesh):
    placed = (
        P(("groups", "seq"), "exp"),
        P(("groups", "seq"), "exp"),
        P(("groups", "seq"), "exp"),
        P(None, "groups", "exp"),
        P("exp"),
        P("exp", None),
        P(("groups", "seq"), None),
        P(),
        P("seq", None, None, "exp"),
        P("seq", "exp", None),
        P(("groups", "seq"), None),
        P(("groups", "seq"), None),
    )
    return jax.shard_map(
        on_device, mesh=mesh, in_specs=placed, out_specs=P(("groups", "seq"), None), check_vma=False
    )
```

```python
import jax
import jax.numpy as jnp
from jax import lax
from jax.experimental import pallas as pl
from jax.experimental.pallas import tpu as pltpu
from jax.sharding import PartitionSpec as P

HEAD_DIM = 64
WINDOW = 128
TOP = 4
SHIFT_LIMIT = 8


GLU_ALPHA = 1.702
EPSILON = 1e-05


def shifted(shard, axis, by):
    size = lax.axis_size(axis)
    pairs = [(i, i + by) for i in range(size) if 0 <= i + by < size]
    return lax.ppermute(shard, axis, pairs)


def swap_exp(x):
    size = lax.axis_size("exp")
    return lax.ppermute(x, "exp", [(i, (i + 1) % size) for i in range(size)])


def seq_all_to_all(blocks):
    return lax.all_to_all(blocks, "seq", split_axis=0, concat_axis=0, tiled=True)


def shift_exchange(blocks, sign):
    size = lax.axis_size("seq")
    out = [blocks[0]]
    for step in range(1, size):
        pairs = [(i, (i + sign * step) % size) for i in range(size)]
        out.append(lax.ppermute(blocks[step], "seq", pairs))
    return jnp.stack(out)


def rms_normalize(mixed_rows, norm_gain):
    mean_square = jnp.mean(mixed_rows * mixed_rows, axis=-1, keepdims=True)
    return (mixed_rows * lax.rsqrt(mean_square + EPSILON) * norm_gain).astype(jnp.bfloat16)


def attend_block(queries, keys_all, values_all, sink_logits, block_rows, window_rows):
    kv_count = keys_all.shape[1] // HEAD_DIM
    group = queries.shape[1] // HEAD_DIM // kv_count
    query_block = queries.reshape(block_rows, kv_count, group, HEAD_DIM)
    key_block = keys_all.reshape(block_rows + window_rows, kv_count, HEAD_DIM)
    value_block = values_all.reshape(block_rows + window_rows, kv_count, HEAD_DIM)
    scores = jnp.einsum(
        "qhgd,khd->hgqk", query_block, key_block, preferred_element_type=jnp.float32
    ) * HEAD_DIM ** (-0.5)
    query_pos = jnp.arange(block_rows)[:, None]
    key_pos = jnp.arange(block_rows + window_rows)[None, :]
    allowed = (key_pos > query_pos) & (key_pos <= query_pos + window_rows)
    scores = jnp.where(allowed, scores, -jnp.inf)
    sink_table = sink_logits.reshape(kv_count, group)[:, :, None]
    largest = jnp.maximum(jnp.max(scores, axis=-1), sink_table)
    weights_exp = jnp.exp(scores - largest[..., None])
    denominator = jnp.exp(sink_table - largest) + jnp.sum(weights_exp, axis=-1)
    probs = (weights_exp / denominator[..., None]).astype(jnp.bfloat16)
    heads_out = jnp.einsum("hgqk,khd->qhgd", probs, value_block, preferred_element_type=jnp.float32)
    return heads_out.astype(jnp.bfloat16).reshape(block_rows, queries.shape[1])


def expert_hidden(rows, expert_in):
    gate_up = jnp.einsum("rd,kdf->krf", rows, expert_in, preferred_element_type=jnp.float32)
    gate_val = gate_up[0]
    up_val = gate_up[1]
    return ((up_val + 1.0) * gate_val * jax.nn.sigmoid(GLU_ALPHA * gate_val)).astype(jnp.bfloat16)


def attention_kernel(sink_ref, q_ref, pk_ref, k_ref, pv_ref, v_ref, w_ref, o_ref, heads_ref):
    rows = q_ref.shape[0]
    prior = pk_ref.shape[0]
    span = 2 * WINDOW
    pair_cols = 2 * HEAD_DIM
    pairs = q_ref.shape[1] // pair_cols
    kv_count = k_ref.shape[1] // HEAD_DIM
    per_kv = pairs // kv_count
    keys_all = jnp.concatenate([pk_ref[...], k_ref[...]], axis=0)
    values_all = jnp.concatenate([pv_ref[...], v_ref[...]], axis=0)
    q_pos = lax.broadcasted_iota(jnp.int32, (WINDOW, span), 0)
    k_pos = lax.broadcasted_iota(jnp.int32, (WINDOW, span), 1)
    allowed = (k_pos > q_pos) & (k_pos <= q_pos + WINDOW)
    lane_half = lax.broadcasted_iota(jnp.int32, (span, pair_cols), 1) // HEAD_DIM
    for b in range(rows // WINDOW):
        first = b * WINDOW + prior - WINDOW
        key_win = keys_all[first : first + span]
        value_win = values_all[first : first + span]
        swapped_k = pltpu.roll(key_win, HEAD_DIM, 1)
        swapped_v = pltpu.roll(value_win, HEAD_DIM, 1)
        placed = {}
        for kv in range(kv_count):
            for a in range(2):
                src_k = key_win if (kv % 2) == a else swapped_k
                src_v = value_win if (kv % 2) == a else swapped_v
                placed[kv, a] = (
                    jnp.where(lane_half == a, src_k, jnp.zeros_like(src_k)),
                    jnp.where(lane_half == a, src_v, jnp.zeros_like(src_v)),
                )
        for j in range(pairs):
            kv = j // per_kv
            q_pair = q_ref[b * WINDOW : (b + 1) * WINDOW, j * pair_cols : (j + 1) * pair_cols]
            total = None
            for a in range(2):
                k_placed, v_placed = placed[kv, a]
                scores = lax.dot_general(
                    q_pair, k_placed, (((1,), (1,)), ((), ())), preferred_element_type=jnp.float32
                ) * HEAD_DIM ** (-0.5)
                scores = jnp.where(allowed, scores, -jnp.inf)
                sink = sink_ref[2 * j + a]
                largest = jnp.maximum(jnp.max(scores, axis=-1, keepdims=True), sink)
                weights_exp = jnp.exp(scores - largest)
                denominator = jnp.exp(sink - largest) + jnp.sum(weights_exp, axis=-1, keepdims=True)
                probs = (weights_exp * (1.0 / denominator)).astype(jnp.bfloat16)
                out = jnp.dot(probs, v_placed, preferred_element_type=jnp.float32)
                total = out if total is None else total + out
            heads_ref[b * WINDOW : (b + 1) * WINDOW, j * pair_cols : (j + 1) * pair_cols] = total.astype(
                heads_ref.dtype
            )
    o_ref[...] = jnp.dot(heads_ref[...], w_ref[...], preferred_element_type=jnp.float32)


def attend_kernel(queries, prior_keys, key_rows, prior_values, values, sink_logits, out_weight):
    rows, cols = queries.shape
    heads = cols // HEAD_DIM
    span = 2 * WINDOW
    width = out_weight.shape[1]
    cost = pl.CostEstimate(
        flops=2 * 2 * rows * span * 2 * HEAD_DIM * heads + 2 * rows * cols * width,
        transcendentals=rows * span * heads,
        bytes_accessed=rows * cols * 2 + out_weight.size * 2 + rows * width * 4
        + 2 * (rows + WINDOW) * key_rows.shape[1] * 2,
    )
    vmem = pl.BlockSpec(memory_space=pltpu.VMEM)
    return pl.pallas_call(
        attention_kernel,
        out_shape=jax.ShapeDtypeStruct((rows, width), jnp.float32),
        in_specs=[pl.BlockSpec(memory_space=pltpu.SMEM)] + [vmem] * 6,
        out_specs=vmem,
        scratch_shapes=[pltpu.VMEM((rows, cols), jnp.bfloat16)],
        cost_estimate=cost,
    )(sink_logits, queries, prior_keys, key_rows, prior_values, values, out_weight)


def on_device(
    queries,
    key_rows,
    values,
    cached_rows,
    sink_logits,
    out_weight,
    residual,
    norm_gain,
    expert_in,
    expert_out,
    routes,
    route_gates,
):
    tok_rows = queries.shape[0]
    window_rows = WINDOW
    rim_rows = jnp.stack([key_rows[tok_rows - window_rows :], values[tok_rows - window_rows :]])
    received = shifted(rim_rows, "seq", 1)
    prior = jnp.where(lax.axis_index("seq") == 0, cached_rows, received)
    partial_rows = attend_kernel(queries, prior[0], key_rows, prior[1], values, sink_logits, out_weight)
    mixed_rows = residual.astype(jnp.float32) + (partial_rows + swap_exp(partial_rows))
    normed = rms_normalize(mixed_rows, norm_gain)

    experts = lax.axis_size("seq")
    width = normed.shape[1]
    capacity = 3 * tok_rows * TOP // (2 * experts)
    half = -(-capacity // 2)
    slots = experts * half
    core = lax.axis_index("exp")
    flat_experts = routes.reshape(-1)
    expert_hits = (flat_experts[:, None] == jnp.arange(experts, dtype=jnp.int32)[None, :]).astype(
        jnp.int32
    )
    slot_rank = jnp.sum(expert_hits * (jnp.cumsum(expert_hits, axis=0) - 1), axis=1)
    local_rank = slot_rank - core * half
    mine = (local_rank >= 0) & (local_rank < half)
    by_shift = experts <= SHIFT_LIMIT
    offset = (flat_experts - lax.axis_index("seq")) % experts if by_shift else flat_experts
    slot_id = jnp.where(mine, offset * half + local_rank, -1)
    slot_iota = jnp.arange(slots, dtype=jnp.int32)
    pick = (slot_id[:, None] == slot_iota[None, :]).astype(jnp.bfloat16)
    select = jnp.max(pick.reshape(tok_rows, TOP, slots), axis=1).T
    outgoing = (
        jnp.dot(select, normed, preferred_element_type=jnp.float32)
        .astype(jnp.bfloat16)
        .reshape(experts, half, width)
    )
    slot_rows = shift_exchange(outgoing, 1) if by_shift else seq_all_to_all(outgoing)
    other_rows = swap_exp(slot_rows)
    own_hidden = expert_hidden(slot_rows.reshape(-1, width), expert_in[0])
    own_hidden, other_rows = lax.optimization_barrier((own_hidden, other_rows))
    other_hidden = expert_hidden(other_rows.reshape(-1, width), expert_in[0])
    their_part = swap_exp(
        jnp.dot(other_hidden, expert_out[0], preferred_element_type=jnp.float32)
        .astype(jnp.bfloat16)
        .reshape(experts, half, width)
    )
    own_part = (
        jnp.dot(own_hidden, expert_out[0], preferred_element_type=jnp.float32)
        .astype(jnp.bfloat16)
        .reshape(experts, half, width)
    )
    result = (own_part.astype(jnp.float32) + their_part.astype(jnp.float32)).astype(jnp.bfloat16)
    returned = shift_exchange(result, -1) if by_shift else seq_all_to_all(result)
    picked = jnp.dot(pick, returned.reshape(slots, width), preferred_element_type=jnp.float32)
    weighted = jnp.sum(picked.reshape(tok_rows, TOP, width) * route_gates[:, :, None], axis=1)
    rounded = weighted.astype(jnp.bfloat16)
    moe = rounded.astype(jnp.float32) + swap_exp(rounded).astype(jnp.float32)
    return (mixed_rows + moe).astype(jnp.bfloat16)


def solution(mesh):
    placed = (
        P(("groups", "seq"), "exp"),
        P(("groups", "seq"), "exp"),
        P(("groups", "seq"), "exp"),
        P(None, "groups", "exp"),
        P("exp"),
        P("exp", None),
        P(("groups", "seq"), None),
        P(),
        P("seq", None, None, "exp"),
        P("seq", "exp", None),
        P(("groups", "seq"), None),
        P(("groups", "seq"), None),
    )
    return jax.shard_map(
        on_device, mesh=mesh, in_specs=placed, out_specs=P(("groups", "seq"), None), check_vma=False
    )
```

```python
import jax
import jax.numpy as jnp
from jax import lax
from jax.experimental import pallas as pl
from jax.experimental.pallas import tpu as pltpu
from jax.sharding import PartitionSpec as P

HEAD_DIM = 64
WINDOW = 128
TOP = 4
SHIFT_LIMIT = 8


GLU_ALPHA = 1.702
EPSILON = 1e-05


def shifted(shard, axis, by):
    size = lax.axis_size(axis)
    pairs = [(i, i + by) for i in range(size) if 0 <= i + by < size]
    return lax.ppermute(shard, axis, pairs)


def swap_exp(x):
    size = lax.axis_size("exp")
    return lax.ppermute(x, "exp", [(i, (i + 1) % size) for i in range(size)])


def seq_all_to_all(blocks):
    return lax.all_to_all(blocks, "seq", split_axis=0, concat_axis=0, tiled=True)


def shift_exchange(blocks, sign):
    size = lax.axis_size("seq")
    out = [blocks[0]]
    for step in range(1, size):
        pairs = [(i, (i + sign * step) % size) for i in range(size)]
        out.append(lax.ppermute(blocks[step], "seq", pairs))
    return jnp.stack(out)


def rms_normalize(mixed_rows, norm_gain):
    mean_square = jnp.mean(mixed_rows * mixed_rows, axis=-1, keepdims=True)
    return (mixed_rows * lax.rsqrt(mean_square + EPSILON) * norm_gain).astype(jnp.bfloat16)


def attend_block(queries, keys_all, values_all, sink_logits, block_rows, window_rows):
    kv_count = keys_all.shape[1] // HEAD_DIM
    group = queries.shape[1] // HEAD_DIM // kv_count
    query_block = queries.reshape(block_rows, kv_count, group, HEAD_DIM)
    key_block = keys_all.reshape(block_rows + window_rows, kv_count, HEAD_DIM)
    value_block = values_all.reshape(block_rows + window_rows, kv_count, HEAD_DIM)
    scores = jnp.einsum(
        "qhgd,khd->hgqk", query_block, key_block, preferred_element_type=jnp.float32
    ) * HEAD_DIM ** (-0.5)
    query_pos = jnp.arange(block_rows)[:, None]
    key_pos = jnp.arange(block_rows + window_rows)[None, :]
    allowed = (key_pos > query_pos) & (key_pos <= query_pos + window_rows)
    scores = jnp.where(allowed, scores, -jnp.inf)
    sink_table = sink_logits.reshape(kv_count, group)[:, :, None]
    largest = jnp.maximum(jnp.max(scores, axis=-1), sink_table)
    weights_exp = jnp.exp(scores - largest[..., None])
    denominator = jnp.exp(sink_table - largest) + jnp.sum(weights_exp, axis=-1)
    probs = (weights_exp / denominator[..., None]).astype(jnp.bfloat16)
    heads_out = jnp.einsum("hgqk,khd->qhgd", probs, value_block, preferred_element_type=jnp.float32)
    return heads_out.astype(jnp.bfloat16).reshape(block_rows, queries.shape[1])


def expert_hidden(rows, expert_in):
    gate_up = jnp.einsum("rd,kdf->krf", rows, expert_in, preferred_element_type=jnp.float32)
    gate_val = gate_up[0]
    up_val = gate_up[1]
    return ((up_val + 1.0) * gate_val * jax.nn.sigmoid(GLU_ALPHA * gate_val)).astype(jnp.bfloat16)


def attention_kernel(sink_ref, first_ref, q_ref, cached_ref, recv_ref, k_ref, v_ref, w_ref, o_ref, heads_ref):
    rows = q_ref.shape[0]
    prior = cached_ref.shape[1]
    span = 2 * WINDOW
    pair_cols = 2 * HEAD_DIM
    pairs = q_ref.shape[1] // pair_cols
    kv_count = k_ref.shape[1] // HEAD_DIM
    per_kv = pairs // kv_count
    first = first_ref[0] == 1
    prior_keys = jnp.where(first, cached_ref[0], recv_ref[0])
    prior_values = jnp.where(first, cached_ref[1], recv_ref[1])
    keys_all = jnp.concatenate([prior_keys, k_ref[...]], axis=0)
    values_all = jnp.concatenate([prior_values, v_ref[...]], axis=0)
    q_pos = lax.broadcasted_iota(jnp.int32, (WINDOW, span), 0)
    k_pos = lax.broadcasted_iota(jnp.int32, (WINDOW, span), 1)
    allowed = (k_pos > q_pos) & (k_pos <= q_pos + WINDOW)
    lane_half = lax.broadcasted_iota(jnp.int32, (span, pair_cols), 1) // HEAD_DIM
    for b in range(rows // WINDOW):
        first = b * WINDOW + prior - WINDOW
        key_win = keys_all[first : first + span]
        value_win = values_all[first : first + span]
        swapped_k = pltpu.roll(key_win, HEAD_DIM, 1)
        swapped_v = pltpu.roll(value_win, HEAD_DIM, 1)
        placed = {}
        for kv in range(kv_count):
            for a in range(2):
                src_k = key_win if (kv % 2) == a else swapped_k
                src_v = value_win if (kv % 2) == a else swapped_v
                placed[kv, a] = (
                    jnp.where(lane_half == a, src_k, jnp.zeros_like(src_k)),
                    jnp.where(lane_half == a, src_v, jnp.zeros_like(src_v)),
                )
        for j in range(pairs):
            kv = j // per_kv
            q_pair = q_ref[b * WINDOW : (b + 1) * WINDOW, j * pair_cols : (j + 1) * pair_cols]
            total = None
            for a in range(2):
                k_placed, v_placed = placed[kv, a]
                scores = lax.dot_general(
                    q_pair, k_placed, (((1,), (1,)), ((), ())), preferred_element_type=jnp.float32
                ) * HEAD_DIM ** (-0.5)
                scores = jnp.where(allowed, scores, -jnp.inf)
                sink = sink_ref[2 * j + a]
                largest = jnp.maximum(jnp.max(scores, axis=-1, keepdims=True), sink)
                weights_exp = jnp.exp(scores - largest)
                denominator = jnp.exp(sink - largest) + jnp.sum(weights_exp, axis=-1, keepdims=True)
                probs = (weights_exp * (1.0 / denominator)).astype(jnp.bfloat16)
                out = jnp.dot(probs, v_placed, preferred_element_type=jnp.float32)
                total = out if total is None else total + out
            heads_ref[b * WINDOW : (b + 1) * WINDOW, j * pair_cols : (j + 1) * pair_cols] = total.astype(
                heads_ref.dtype
            )
    o_ref[...] = jnp.dot(heads_ref[...], w_ref[...], preferred_element_type=jnp.float32)


def attend_kernel(queries, first_block, cached_rows, received, key_rows, values, sink_logits, out_weight):
    rows, cols = queries.shape
    heads = cols // HEAD_DIM
    span = 2 * WINDOW
    width = out_weight.shape[1]
    cost = pl.CostEstimate(
        flops=2 * 2 * rows * span * 2 * HEAD_DIM * heads + 2 * rows * cols * width,
        transcendentals=rows * span * heads,
        bytes_accessed=rows * cols * 2 + out_weight.size * 2 + rows * width * 4
        + 2 * (rows + WINDOW) * key_rows.shape[1] * 2,
    )
    vmem = pl.BlockSpec(memory_space=pltpu.VMEM)
    return pl.pallas_call(
        attention_kernel,
        out_shape=jax.ShapeDtypeStruct((rows, width), jnp.float32),
        in_specs=[pl.BlockSpec(memory_space=pltpu.SMEM)] * 2 + [vmem] * 6,
        out_specs=vmem,
        scratch_shapes=[pltpu.VMEM((rows, cols), jnp.bfloat16)],
        cost_estimate=cost,
    )(sink_logits, first_block, queries, cached_rows, received, key_rows, values, out_weight)


def on_device(
    queries,
    key_rows,
    values,
    cached_rows,
    sink_logits,
    out_weight,
    residual,
    norm_gain,
    expert_in,
    expert_out,
    routes,
    route_gates,
):
    tok_rows = queries.shape[0]
    window_rows = WINDOW
    rim_rows = jnp.stack([key_rows[tok_rows - window_rows :], values[tok_rows - window_rows :]])
    received = shifted(rim_rows, "seq", 1)
    first_block = (lax.axis_index("seq") == 0).astype(jnp.int32).reshape(1)
    partial_rows = attend_kernel(
        queries, first_block, cached_rows, received, key_rows, values, sink_logits, out_weight
    )
    mixed_rows = residual.astype(jnp.float32) + (partial_rows + swap_exp(partial_rows))
    normed = rms_normalize(mixed_rows, norm_gain)

    experts = lax.axis_size("seq")
    width = normed.shape[1]
    capacity = 3 * tok_rows * TOP // (2 * experts)
    half = -(-capacity // 2)
    slots = experts * half
    core = lax.axis_index("exp")
    flat_experts = routes.reshape(-1)
    expert_hits = (flat_experts[:, None] == jnp.arange(experts, dtype=jnp.int32)[None, :]).astype(
        jnp.int32
    )
    slot_rank = jnp.sum(expert_hits * (jnp.cumsum(expert_hits, axis=0) - 1), axis=1)
    local_rank = slot_rank - core * half
    mine = (local_rank >= 0) & (local_rank < half)
    by_shift = experts <= SHIFT_LIMIT
    offset = (flat_experts - lax.axis_index("seq")) % experts if by_shift else flat_experts
    slot_id = jnp.where(mine, offset * half + local_rank, -1)
    slot_iota = jnp.arange(slots, dtype=jnp.int32)
    pick = (slot_id[:, None] == slot_iota[None, :]).astype(jnp.bfloat16)
    select = jnp.max(pick.reshape(tok_rows, TOP, slots), axis=1).T
    outgoing = (
        jnp.dot(select, normed, preferred_element_type=jnp.float32)
        .astype(jnp.bfloat16)
        .reshape(experts, half, width)
    )
    slot_rows = shift_exchange(outgoing, 1) if by_shift else seq_all_to_all(outgoing)
    other_rows = swap_exp(slot_rows)
    own_hidden = expert_hidden(slot_rows.reshape(-1, width), expert_in[0])
    own_hidden, other_rows = lax.optimization_barrier((own_hidden, other_rows))
    other_hidden = expert_hidden(other_rows.reshape(-1, width), expert_in[0])
    their_part = swap_exp(
        jnp.dot(other_hidden, expert_out[0], preferred_element_type=jnp.float32)
        .astype(jnp.bfloat16)
        .reshape(experts, half, width)
    )
    own_part = (
        jnp.dot(own_hidden, expert_out[0], preferred_element_type=jnp.float32)
        .astype(jnp.bfloat16)
        .reshape(experts, half, width)
    )
    result = (own_part.astype(jnp.float32) + their_part.astype(jnp.float32)).astype(jnp.bfloat16)
    returned = shift_exchange(result, -1) if by_shift else seq_all_to_all(result)
    picked = jnp.dot(pick, returned.reshape(slots, width), preferred_element_type=jnp.float32)
    weighted = jnp.sum(picked.reshape(tok_rows, TOP, width) * route_gates[:, :, None], axis=1)
    rounded = weighted.astype(jnp.bfloat16)
    moe = rounded.astype(jnp.float32) + swap_exp(rounded).astype(jnp.float32)
    return (mixed_rows + moe).astype(jnp.bfloat16)


def solution(mesh):
    placed = (
        P(("groups", "seq"), "exp"),
        P(("groups", "seq"), "exp"),
        P(("groups", "seq"), "exp"),
        P(None, "groups", "exp"),
        P("exp"),
        P("exp", None),
        P(("groups", "seq"), None),
        P(),
        P("seq", None, None, "exp"),
        P("seq", "exp", None),
        P(("groups", "seq"), None),
        P(("groups", "seq"), None),
    )
    return jax.shard_map(
        on_device, mesh=mesh, in_specs=placed, out_specs=P(("groups", "seq"), None), check_vma=False
    )
```

```python
import jax
import jax.numpy as jnp
from jax import lax
from jax.experimental import pallas as pl
from jax.experimental.pallas import tpu as pltpu
from jax.sharding import PartitionSpec as P

HEAD_DIM = 64
WINDOW = 128
TOP = 4
SHIFT_LIMIT = 8


GLU_ALPHA = 1.702
EPSILON = 1e-05


def shifted(shard, axis, by):
    size = lax.axis_size(axis)
    pairs = [(i, i + by) for i in range(size) if 0 <= i + by < size]
    return lax.ppermute(shard, axis, pairs)


def swap_exp(x):
    size = lax.axis_size("exp")
    return lax.ppermute(x, "exp", [(i, (i + 1) % size) for i in range(size)])


def seq_all_to_all(blocks):
    return lax.all_to_all(blocks, "seq", split_axis=0, concat_axis=0, tiled=True)


def return_exchange(blocks):
    size = lax.axis_size("seq")
    me = lax.axis_index("seq")
    out = [lax.dynamic_index_in_dim(blocks, me, 0, keepdims=False)]
    for step in range(1, size):
        pairs = [(i, (i - step) % size) for i in range(size)]
        source = lax.dynamic_index_in_dim(blocks, (me - step) % size, 0, keepdims=False)
        out.append(lax.ppermute(source, "seq", pairs))
    return jnp.stack(out)


def shift_exchange(blocks, sign):
    size = lax.axis_size("seq")
    out = [blocks[0]]
    for step in range(1, size):
        pairs = [(i, (i + sign * step) % size) for i in range(size)]
        out.append(lax.ppermute(blocks[step], "seq", pairs))
    return jnp.stack(out)


def rms_normalize(mixed_rows, norm_gain):
    mean_square = jnp.mean(mixed_rows * mixed_rows, axis=-1, keepdims=True)
    return (mixed_rows * lax.rsqrt(mean_square + EPSILON) * norm_gain).astype(jnp.bfloat16)


def attend_block(queries, keys_all, values_all, sink_logits, block_rows, window_rows):
    kv_count = keys_all.shape[1] // HEAD_DIM
    group = queries.shape[1] // HEAD_DIM // kv_count
    query_block = queries.reshape(block_rows, kv_count, group, HEAD_DIM)
    key_block = keys_all.reshape(block_rows + window_rows, kv_count, HEAD_DIM)
    value_block = values_all.reshape(block_rows + window_rows, kv_count, HEAD_DIM)
    scores = jnp.einsum(
        "qhgd,khd->hgqk", query_block, key_block, preferred_element_type=jnp.float32
    ) * HEAD_DIM ** (-0.5)
    query_pos = jnp.arange(block_rows)[:, None]
    key_pos = jnp.arange(block_rows + window_rows)[None, :]
    allowed = (key_pos > query_pos) & (key_pos <= query_pos + window_rows)
    scores = jnp.where(allowed, scores, -jnp.inf)
    sink_table = sink_logits.reshape(kv_count, group)[:, :, None]
    largest = jnp.maximum(jnp.max(scores, axis=-1), sink_table)
    weights_exp = jnp.exp(scores - largest[..., None])
    denominator = jnp.exp(sink_table - largest) + jnp.sum(weights_exp, axis=-1)
    probs = (weights_exp / denominator[..., None]).astype(jnp.bfloat16)
    heads_out = jnp.einsum("hgqk,khd->qhgd", probs, value_block, preferred_element_type=jnp.float32)
    return heads_out.astype(jnp.bfloat16).reshape(block_rows, queries.shape[1])


def expert_hidden(rows, expert_in):
    gate_up = jnp.einsum("rd,kdf->krf", rows, expert_in, preferred_element_type=jnp.float32)
    gate_val = gate_up[0]
    up_val = gate_up[1]
    return ((up_val + 1.0) * gate_val * jax.nn.sigmoid(GLU_ALPHA * gate_val)).astype(jnp.bfloat16)


def attention_kernel(sink_ref, first_ref, q_ref, cached_ref, recv_ref, k_ref, v_ref, w_ref, o_ref, heads_ref):
    rows = q_ref.shape[0]
    prior = cached_ref.shape[1]
    span = 2 * WINDOW
    pair_cols = 2 * HEAD_DIM
    pairs = q_ref.shape[1] // pair_cols
    kv_count = k_ref.shape[1] // HEAD_DIM
    per_kv = pairs // kv_count
    first = first_ref[0] == 1
    prior_keys = jnp.where(first, cached_ref[0], recv_ref[0])
    prior_values = jnp.where(first, cached_ref[1], recv_ref[1])
    keys_all = jnp.concatenate([prior_keys, k_ref[...]], axis=0)
    values_all = jnp.concatenate([prior_values, v_ref[...]], axis=0)
    q_pos = lax.broadcasted_iota(jnp.int32, (WINDOW, span), 0)
    k_pos = lax.broadcasted_iota(jnp.int32, (WINDOW, span), 1)
    allowed = (k_pos > q_pos) & (k_pos <= q_pos + WINDOW)
    lane_half = lax.broadcasted_iota(jnp.int32, (span, pair_cols), 1) // HEAD_DIM
    for b in range(rows // WINDOW):
        first = b * WINDOW + prior - WINDOW
        key_win = keys_all[first : first + span]
        value_win = values_all[first : first + span]
        swapped_k = pltpu.roll(key_win, HEAD_DIM, 1)
        swapped_v = pltpu.roll(value_win, HEAD_DIM, 1)
        placed = {}
        for kv in range(kv_count):
            for a in range(2):
                src_k = key_win if (kv % 2) == a else swapped_k
                src_v = value_win if (kv % 2) == a else swapped_v
                placed[kv, a] = (
                    jnp.where(lane_half == a, src_k, jnp.zeros_like(src_k)),
                    jnp.where(lane_half == a, src_v, jnp.zeros_like(src_v)),
                )
        for j in range(pairs):
            kv = j // per_kv
            q_pair = q_ref[b * WINDOW : (b + 1) * WINDOW, j * pair_cols : (j + 1) * pair_cols]
            total = None
            for a in range(2):
                k_placed, v_placed = placed[kv, a]
                scores = lax.dot_general(
                    q_pair, k_placed, (((1,), (1,)), ((), ())), preferred_element_type=jnp.float32
                ) * HEAD_DIM ** (-0.5)
                scores = jnp.where(allowed, scores, -jnp.inf)
                sink = sink_ref[2 * j + a]
                largest = jnp.maximum(jnp.max(scores, axis=-1, keepdims=True), sink)
                weights_exp = jnp.exp(scores - largest)
                denominator = jnp.exp(sink - largest) + jnp.sum(weights_exp, axis=-1, keepdims=True)
                probs = (weights_exp * (1.0 / denominator)).astype(jnp.bfloat16)
                out = jnp.dot(probs, v_placed, preferred_element_type=jnp.float32)
                total = out if total is None else total + out
            heads_ref[b * WINDOW : (b + 1) * WINDOW, j * pair_cols : (j + 1) * pair_cols] = total.astype(
                heads_ref.dtype
            )
    o_ref[...] = jnp.dot(heads_ref[...], w_ref[...], preferred_element_type=jnp.float32)


def attend_kernel(queries, first_block, cached_rows, received, key_rows, values, sink_logits, out_weight):
    rows, cols = queries.shape
    heads = cols // HEAD_DIM
    span = 2 * WINDOW
    width = out_weight.shape[1]
    cost = pl.CostEstimate(
        flops=2 * 2 * rows * span * 2 * HEAD_DIM * heads + 2 * rows * cols * width,
        transcendentals=rows * span * heads,
        bytes_accessed=rows * cols * 2 + out_weight.size * 2 + rows * width * 4
        + 2 * (rows + WINDOW) * key_rows.shape[1] * 2,
    )
    vmem = pl.BlockSpec(memory_space=pltpu.VMEM)
    return pl.pallas_call(
        attention_kernel,
        out_shape=jax.ShapeDtypeStruct((rows, width), jnp.float32),
        in_specs=[pl.BlockSpec(memory_space=pltpu.SMEM)] * 2 + [vmem] * 6,
        out_specs=vmem,
        scratch_shapes=[pltpu.VMEM((rows, cols), jnp.bfloat16)],
        cost_estimate=cost,
    )(sink_logits, first_block, queries, cached_rows, received, key_rows, values, out_weight)


def on_device(
    queries,
    key_rows,
    values,
    cached_rows,
    sink_logits,
    out_weight,
    residual,
    norm_gain,
    expert_in,
    expert_out,
    routes,
    route_gates,
):
    tok_rows = queries.shape[0]
    window_rows = WINDOW
    rim_rows = jnp.stack([key_rows[tok_rows - window_rows :], values[tok_rows - window_rows :]])
    received = shifted(rim_rows, "seq", 1)
    first_block = (lax.axis_index("seq") == 0).astype(jnp.int32).reshape(1)
    partial_rows = attend_kernel(
        queries, first_block, cached_rows, received, key_rows, values, sink_logits, out_weight
    )
    mixed_rows = residual.astype(jnp.float32) + (partial_rows + swap_exp(partial_rows))
    normed = rms_normalize(mixed_rows, norm_gain)

    experts = lax.axis_size("seq")
    width = normed.shape[1]
    capacity = 3 * tok_rows * TOP // (2 * experts)
    half = -(-capacity // 2)
    slots = experts * half
    core = lax.axis_index("exp")
    flat_experts = routes.reshape(-1)
    expert_hits = (flat_experts[:, None] == jnp.arange(experts, dtype=jnp.int32)[None, :]).astype(
        jnp.int32
    )
    slot_rank = jnp.sum(expert_hits * (jnp.cumsum(expert_hits, axis=0) - 1), axis=1)
    local_rank = slot_rank - core * half
    mine = (local_rank >= 0) & (local_rank < half)
    by_shift = experts <= SHIFT_LIMIT
    offset = (flat_experts - lax.axis_index("seq")) % experts if by_shift else flat_experts
    slot_id = jnp.where(mine, flat_experts * half + local_rank, -1)
    back_id = jnp.where(mine, offset * half + local_rank, -1)
    slot_iota = jnp.arange(slots, dtype=jnp.int32)
    pick = (slot_id[:, None] == slot_iota[None, :]).astype(jnp.bfloat16)
    back_pick = (back_id[:, None] == slot_iota[None, :]).astype(jnp.bfloat16)
    select = jnp.max(pick.reshape(tok_rows, TOP, slots), axis=1).T
    outgoing = (
        jnp.dot(select, normed, preferred_element_type=jnp.float32)
        .astype(jnp.bfloat16)
        .reshape(experts, half, width)
    )
    slot_rows = seq_all_to_all(outgoing)
    other_rows = swap_exp(slot_rows)
    own_hidden = expert_hidden(slot_rows.reshape(-1, width), expert_in[0])
    own_hidden, other_rows = lax.optimization_barrier((own_hidden, other_rows))
    other_hidden = expert_hidden(other_rows.reshape(-1, width), expert_in[0])
    their_part = swap_exp(
        jnp.dot(other_hidden, expert_out[0], preferred_element_type=jnp.float32)
        .astype(jnp.bfloat16)
        .reshape(experts, half, width)
    )
    own_part = (
        jnp.dot(own_hidden, expert_out[0], preferred_element_type=jnp.float32)
        .astype(jnp.bfloat16)
        .reshape(experts, half, width)
    )
    result = (own_part.astype(jnp.float32) + their_part.astype(jnp.float32)).astype(jnp.bfloat16)
    returned = return_exchange(result) if by_shift else seq_all_to_all(result)
    picked = jnp.dot(back_pick, returned.reshape(slots, width), preferred_element_type=jnp.float32)
    weighted = jnp.sum(picked.reshape(tok_rows, TOP, width) * route_gates[:, :, None], axis=1)
    rounded = weighted.astype(jnp.bfloat16)
    moe = rounded.astype(jnp.float32) + swap_exp(rounded).astype(jnp.float32)
    return (mixed_rows + moe).astype(jnp.bfloat16)


def solution(mesh):
    placed = (
        P(("groups", "seq"), "exp"),
        P(("groups", "seq"), "exp"),
        P(("groups", "seq"), "exp"),
        P(None, "groups", "exp"),
        P("exp"),
        P("exp", None),
        P(("groups", "seq"), None),
        P(),
        P("seq", None, None, "exp"),
        P("seq", "exp", None),
        P(("groups", "seq"), None),
        P(("groups", "seq"), None),
    )
    return jax.shard_map(
        on_device, mesh=mesh, in_specs=placed, out_specs=P(("groups", "seq"), None), check_vma=False
    )
```

```python
import jax
import jax.numpy as jnp
from jax import lax
from jax.experimental import pallas as pl
from jax.experimental.pallas import tpu as pltpu
from jax.sharding import PartitionSpec as P

HEAD_DIM = 64
WINDOW = 128
TOP = 4
SHIFT_LIMIT = 8


GLU_ALPHA = 1.702
EPSILON = 1e-05


def shifted(shard, axis, by):
    size = lax.axis_size(axis)
    pairs = [(i, i + by) for i in range(size) if 0 <= i + by < size]
    return lax.ppermute(shard, axis, pairs)


def swap_exp(x):
    size = lax.axis_size("exp")
    return lax.ppermute(x, "exp", [(i, (i + 1) % size) for i in range(size)])


def seq_all_to_all(blocks):
    return lax.all_to_all(blocks, "seq", split_axis=0, concat_axis=0, tiled=True)


def shift_exchange(blocks, sign):
    size = lax.axis_size("seq")
    out = [blocks[0]]
    for step in range(1, size):
        pairs = [(i, (i + sign * step) % size) for i in range(size)]
        out.append(lax.ppermute(blocks[step], "seq", pairs))
    return jnp.stack(out)


def rms_normalize(mixed_rows, norm_gain):
    mean_square = jnp.mean(mixed_rows * mixed_rows, axis=-1, keepdims=True)
    return (mixed_rows * lax.rsqrt(mean_square + EPSILON) * norm_gain).astype(jnp.bfloat16)


def attend_block(queries, keys_all, values_all, sink_logits, block_rows, window_rows):
    kv_count = keys_all.shape[1] // HEAD_DIM
    group = queries.shape[1] // HEAD_DIM // kv_count
    query_block = queries.reshape(block_rows, kv_count, group, HEAD_DIM)
    key_block = keys_all.reshape(block_rows + window_rows, kv_count, HEAD_DIM)
    value_block = values_all.reshape(block_rows + window_rows, kv_count, HEAD_DIM)
    scores = jnp.einsum(
        "qhgd,khd->hgqk", query_block, key_block, preferred_element_type=jnp.float32
    ) * HEAD_DIM ** (-0.5)
    query_pos = jnp.arange(block_rows)[:, None]
    key_pos = jnp.arange(block_rows + window_rows)[None, :]
    allowed = (key_pos > query_pos) & (key_pos <= query_pos + window_rows)
    scores = jnp.where(allowed, scores, -jnp.inf)
    sink_table = sink_logits.reshape(kv_count, group)[:, :, None]
    largest = jnp.maximum(jnp.max(scores, axis=-1), sink_table)
    weights_exp = jnp.exp(scores - largest[..., None])
    denominator = jnp.exp(sink_table - largest) + jnp.sum(weights_exp, axis=-1)
    probs = (weights_exp / denominator[..., None]).astype(jnp.bfloat16)
    heads_out = jnp.einsum("hgqk,khd->qhgd", probs, value_block, preferred_element_type=jnp.float32)
    return heads_out.astype(jnp.bfloat16).reshape(block_rows, queries.shape[1])


def expert_hidden(rows, expert_in):
    gate_up = jnp.einsum("rd,kdf->krf", rows, expert_in, preferred_element_type=jnp.float32)
    gate_val = gate_up[0]
    up_val = gate_up[1]
    return ((up_val + 1.0) * gate_val * jax.nn.sigmoid(GLU_ALPHA * gate_val)).astype(jnp.bfloat16)


def attention_kernel(sink_ref, first_ref, q_ref, cached_ref, recv_ref, k_ref, v_ref, w_ref, o_ref, heads_ref):
    rows = q_ref.shape[0]
    prior = cached_ref.shape[1]
    span = 2 * WINDOW
    pair_cols = 2 * HEAD_DIM
    pairs = q_ref.shape[1] // pair_cols
    kv_count = k_ref.shape[1] // HEAD_DIM
    per_kv = pairs // kv_count
    first = first_ref[0] == 1
    prior_keys = jnp.where(first, cached_ref[0], recv_ref[0])
    prior_values = jnp.where(first, cached_ref[1], recv_ref[1])
    keys_all = jnp.concatenate([prior_keys, k_ref[...]], axis=0)
    values_all = jnp.concatenate([prior_values, v_ref[...]], axis=0)
    q_pos = lax.broadcasted_iota(jnp.int32, (WINDOW, span), 0)
    k_pos = lax.broadcasted_iota(jnp.int32, (WINDOW, span), 1)
    allowed = (k_pos > q_pos) & (k_pos <= q_pos + WINDOW)
    lane_half = lax.broadcasted_iota(jnp.int32, (span, pair_cols), 1) // HEAD_DIM
    for b in range(rows // WINDOW):
        first = b * WINDOW + prior - WINDOW
        key_win = keys_all[first : first + span]
        value_win = values_all[first : first + span]
        swapped_k = pltpu.roll(key_win, HEAD_DIM, 1)
        swapped_v = pltpu.roll(value_win, HEAD_DIM, 1)
        placed = {}
        for kv in range(kv_count):
            for a in range(2):
                src_k = key_win if (kv % 2) == a else swapped_k
                src_v = value_win if (kv % 2) == a else swapped_v
                placed[kv, a] = (
                    jnp.where(lane_half == a, src_k, jnp.zeros_like(src_k)),
                    jnp.where(lane_half == a, src_v, jnp.zeros_like(src_v)),
                )
        for j in range(pairs):
            kv = j // per_kv
            q_pair = q_ref[b * WINDOW : (b + 1) * WINDOW, j * pair_cols : (j + 1) * pair_cols]
            total = None
            for a in range(2):
                k_placed, v_placed = placed[kv, a]
                scores = lax.dot_general(
                    q_pair, k_placed, (((1,), (1,)), ((), ())), preferred_element_type=jnp.float32
                ) * HEAD_DIM ** (-0.5)
                scores = jnp.where(allowed, scores, -jnp.inf)
                sink = sink_ref[2 * j + a]
                largest = jnp.maximum(jnp.max(scores, axis=-1, keepdims=True), sink)
                weights_exp = jnp.exp(scores - largest)
                denominator = jnp.exp(sink - largest) + jnp.sum(weights_exp, axis=-1, keepdims=True)
                probs = (weights_exp * (1.0 / denominator)).astype(jnp.bfloat16)
                out = jnp.dot(probs, v_placed, preferred_element_type=jnp.float32)
                total = out if total is None else total + out
            heads_ref[b * WINDOW : (b + 1) * WINDOW, j * pair_cols : (j + 1) * pair_cols] = total.astype(
                heads_ref.dtype
            )
    o_ref[...] = jnp.dot(heads_ref[...], w_ref[...], preferred_element_type=jnp.float32)


def attend_kernel(queries, first_block, cached_rows, received, key_rows, values, sink_logits, out_weight):
    rows, cols = queries.shape
    heads = cols // HEAD_DIM
    span = 2 * WINDOW
    width = out_weight.shape[1]
    cost = pl.CostEstimate(
        flops=2 * 2 * rows * span * 2 * HEAD_DIM * heads + 2 * rows * cols * width,
        transcendentals=rows * span * heads,
        bytes_accessed=rows * cols * 2 + out_weight.size * 2 + rows * width * 4
        + 2 * (rows + WINDOW) * key_rows.shape[1] * 2,
    )
    vmem = pl.BlockSpec(memory_space=pltpu.VMEM)
    return pl.pallas_call(
        attention_kernel,
        out_shape=jax.ShapeDtypeStruct((rows, width), jnp.float32),
        in_specs=[pl.BlockSpec(memory_space=pltpu.SMEM)] * 2 + [vmem] * 6,
        out_specs=vmem,
        scratch_shapes=[pltpu.VMEM((rows, cols), jnp.bfloat16)],
        cost_estimate=cost,
    )(sink_logits, first_block, queries, cached_rows, received, key_rows, values, out_weight)


def on_device(
    queries,
    key_rows,
    values,
    cached_rows,
    sink_logits,
    out_weight,
    residual,
    norm_gain,
    expert_in,
    expert_out,
    routes,
    route_gates,
):
    tok_rows = queries.shape[0]
    window_rows = WINDOW
    rim_rows = jnp.stack([key_rows[tok_rows - window_rows :], values[tok_rows - window_rows :]])
    received = shifted(rim_rows, "seq", 1)
    first_block = (lax.axis_index("seq") == 0).astype(jnp.int32).reshape(1)
    partial_rows = attend_kernel(
        queries, first_block, cached_rows, received, key_rows, values, sink_logits, out_weight
    )
    mixed_rows = residual.astype(jnp.float32) + (partial_rows + swap_exp(partial_rows))
    normed = rms_normalize(mixed_rows, norm_gain)

    experts = lax.axis_size("seq")
    width = normed.shape[1]
    capacity = 3 * tok_rows * TOP // (2 * experts)
    half = -(-capacity // 2)
    slots = experts * half
    core = lax.axis_index("exp")
    flat_experts = routes.reshape(-1)
    expert_hits = (flat_experts[:, None] == jnp.arange(experts, dtype=jnp.int32)[None, :]).astype(
        jnp.int32
    )
    slot_rank = jnp.sum(expert_hits * (jnp.cumsum(expert_hits, axis=0) - 1), axis=1)
    local_rank = slot_rank - core * half
    mine = (local_rank >= 0) & (local_rank < half)
    by_shift = experts <= SHIFT_LIMIT
    offset = (flat_experts - lax.axis_index("seq")) % experts if by_shift else flat_experts
    slot_id = jnp.where(mine, offset * half + local_rank, -1)
    slot_iota = jnp.arange(slots, dtype=jnp.int32)
    pick = (slot_id[:, None] == slot_iota[None, :]).astype(jnp.bfloat16)
    select = jnp.max(pick.reshape(tok_rows, TOP, slots), axis=1).T
    outgoing = (
        jnp.dot(select, normed, preferred_element_type=jnp.float32)
        .astype(jnp.bfloat16)
        .reshape(experts, half, width)
    )
    slot_rows = shift_exchange(outgoing, 1) if by_shift else seq_all_to_all(outgoing)
    other_rows = swap_exp(slot_rows)
    own_hidden = expert_hidden(slot_rows.reshape(-1, width), expert_in[0])
    own_hidden, other_rows = lax.optimization_barrier((own_hidden, other_rows))
    other_hidden = expert_hidden(other_rows.reshape(-1, width), expert_in[0])
    their_part = swap_exp(
        jnp.dot(other_hidden, expert_out[0], preferred_element_type=jnp.float32)
        .astype(jnp.bfloat16)
        .reshape(experts, half, width)
    )
    own_part = (
        jnp.dot(own_hidden, expert_out[0], preferred_element_type=jnp.float32)
        .astype(jnp.bfloat16)
        .reshape(experts, half, width)
    )
    result = (own_part.astype(jnp.float32) + their_part.astype(jnp.float32)).astype(jnp.bfloat16)
    returned = shift_exchange(result, -1) if by_shift else seq_all_to_all(result)
    gate_table = jnp.sum(
        pick.reshape(tok_rows, TOP, slots).astype(jnp.float32) * route_gates[:, :, None], axis=1
    )
    gate_high = gate_table.astype(jnp.bfloat16)
    gate_low = (gate_table - gate_high.astype(jnp.float32)).astype(jnp.bfloat16)
    flat_returned = returned.reshape(slots, width)
    weighted = jnp.dot(gate_high, flat_returned, preferred_element_type=jnp.float32) + jnp.dot(
        gate_low, flat_returned, preferred_element_type=jnp.float32
    )
    rounded = weighted.astype(jnp.bfloat16)
    moe = rounded.astype(jnp.float32) + swap_exp(rounded).astype(jnp.float32)
    return (mixed_rows + moe).astype(jnp.bfloat16)


def solution(mesh):
    placed = (
        P(("groups", "seq"), "exp"),
        P(("groups", "seq"), "exp"),
        P(("groups", "seq"), "exp"),
        P(None, "groups", "exp"),
        P("exp"),
        P("exp", None),
        P(("groups", "seq"), None),
        P(),
        P("seq", None, None, "exp"),
        P("seq", "exp", None),
        P(("groups", "seq"), None),
        P(("groups", "seq"), None),
    )
    return jax.shard_map(
        on_device, mesh=mesh, in_specs=placed, out_specs=P(("groups", "seq"), None), check_vma=False
    )
```

```python
import jax
import jax.numpy as jnp
from jax import lax
from jax.experimental import pallas as pl
from jax.experimental.pallas import tpu as pltpu
from jax.sharding import PartitionSpec as P

HEAD_DIM = 64
WINDOW = 128
TOP = 4
SHIFT_LIMIT = 8


GLU_ALPHA = 1.702
EPSILON = 1e-05


def shifted(shard, axis, by):
    size = lax.axis_size(axis)
    pairs = [(i, i + by) for i in range(size) if 0 <= i + by < size]
    return lax.ppermute(shard, axis, pairs)


def swap_exp(x):
    size = lax.axis_size("exp")
    return lax.ppermute(x, "exp", [(i, (i + 1) % size) for i in range(size)])


def seq_all_to_all(blocks):
    return lax.all_to_all(blocks, "seq", split_axis=0, concat_axis=0, tiled=True)


def shift_exchange(blocks, sign):
    size = lax.axis_size("seq")
    out = [blocks[0]]
    for step in range(1, size):
        pairs = [(i, (i + sign * step) % size) for i in range(size)]
        out.append(lax.ppermute(blocks[step], "seq", pairs))
    return jnp.stack(out)


def rms_normalize(mixed_rows, norm_gain):
    mean_square = jnp.mean(mixed_rows * mixed_rows, axis=-1, keepdims=True)
    return (mixed_rows * lax.rsqrt(mean_square + EPSILON) * norm_gain).astype(jnp.bfloat16)


def attend_block(queries, keys_all, values_all, sink_logits, block_rows, window_rows):
    kv_count = keys_all.shape[1] // HEAD_DIM
    group = queries.shape[1] // HEAD_DIM // kv_count
    query_block = queries.reshape(block_rows, kv_count, group, HEAD_DIM)
    key_block = keys_all.reshape(block_rows + window_rows, kv_count, HEAD_DIM)
    value_block = values_all.reshape(block_rows + window_rows, kv_count, HEAD_DIM)
    scores = jnp.einsum(
        "qhgd,khd->hgqk", query_block, key_block, preferred_element_type=jnp.float32
    ) * HEAD_DIM ** (-0.5)
    query_pos = jnp.arange(block_rows)[:, None]
    key_pos = jnp.arange(block_rows + window_rows)[None, :]
    allowed = (key_pos > query_pos) & (key_pos <= query_pos + window_rows)
    scores = jnp.where(allowed, scores, -jnp.inf)
    sink_table = sink_logits.reshape(kv_count, group)[:, :, None]
    largest = jnp.maximum(jnp.max(scores, axis=-1), sink_table)
    weights_exp = jnp.exp(scores - largest[..., None])
    denominator = jnp.exp(sink_table - largest) + jnp.sum(weights_exp, axis=-1)
    probs = (weights_exp / denominator[..., None]).astype(jnp.bfloat16)
    heads_out = jnp.einsum("hgqk,khd->qhgd", probs, value_block, preferred_element_type=jnp.float32)
    return heads_out.astype(jnp.bfloat16).reshape(block_rows, queries.shape[1])


def expert_hidden(rows, expert_in):
    gate_up = jnp.einsum("rd,kdf->krf", rows, expert_in, preferred_element_type=jnp.float32)
    gate_val = gate_up[0]
    up_val = gate_up[1]
    return ((up_val + 1.0) * gate_val * jax.nn.sigmoid(GLU_ALPHA * gate_val)).astype(jnp.bfloat16)


def attention_kernel(sink_ref, first_ref, q_ref, cached_ref, recv_ref, k_ref, v_ref, w_ref, o_ref, heads_ref):
    rows = q_ref.shape[0]
    prior = cached_ref.shape[1]
    span = 2 * WINDOW
    pair_cols = 2 * HEAD_DIM
    pairs = q_ref.shape[1] // pair_cols
    kv_count = k_ref.shape[1] // HEAD_DIM
    per_kv = pairs // kv_count
    first = first_ref[0] == 1
    prior_keys = jnp.where(first, cached_ref[0], recv_ref[0])
    prior_values = jnp.where(first, cached_ref[1], recv_ref[1])
    keys_all = jnp.concatenate([prior_keys, k_ref[...]], axis=0)
    values_all = jnp.concatenate([prior_values, v_ref[...]], axis=0)
    q_pos = lax.broadcasted_iota(jnp.int32, (WINDOW, span), 0)
    k_pos = lax.broadcasted_iota(jnp.int32, (WINDOW, span), 1)
    allowed = (k_pos > q_pos) & (k_pos <= q_pos + WINDOW)
    lane_half = lax.broadcasted_iota(jnp.int32, (span, pair_cols), 1) // HEAD_DIM
    for b in range(rows // WINDOW):
        first = b * WINDOW + prior - WINDOW
        key_win = keys_all[first : first + span]
        value_win = values_all[first : first + span]
        swapped_k = pltpu.roll(key_win, HEAD_DIM, 1)
        swapped_v = pltpu.roll(value_win, HEAD_DIM, 1)
        placed = {}
        for kv in range(kv_count):
            for a in range(2):
                src_k = key_win if (kv % 2) == a else swapped_k
                src_v = value_win if (kv % 2) == a else swapped_v
                placed[kv, a] = (
                    jnp.where(lane_half == a, src_k, jnp.zeros_like(src_k)),
                    jnp.where(lane_half == a, src_v, jnp.zeros_like(src_v)),
                )
        for j in range(pairs):
            kv = j // per_kv
            q_pair = q_ref[b * WINDOW : (b + 1) * WINDOW, j * pair_cols : (j + 1) * pair_cols] * HEAD_DIM ** (
                -0.5
            )
            total = None
            for a in range(2):
                k_placed, v_placed = placed[kv, a]
                scores = lax.dot_general(
                    q_pair, k_placed, (((1,), (1,)), ((), ())), preferred_element_type=jnp.float32
                )
                scores = jnp.where(allowed, scores, -jnp.inf)
                sink = sink_ref[2 * j + a]
                largest = jnp.maximum(jnp.max(scores, axis=-1, keepdims=True), sink)
                weights_exp = jnp.exp(scores - largest)
                denominator = jnp.exp(sink - largest) + jnp.sum(weights_exp, axis=-1, keepdims=True)
                probs = (weights_exp * (1.0 / denominator)).astype(jnp.bfloat16)
                out = jnp.dot(probs, v_placed, preferred_element_type=jnp.float32)
                total = out if total is None else total + out
            heads_ref[b * WINDOW : (b + 1) * WINDOW, j * pair_cols : (j + 1) * pair_cols] = total.astype(
                heads_ref.dtype
            )
    o_ref[...] = jnp.dot(heads_ref[...], w_ref[...], preferred_element_type=jnp.float32)


def attend_kernel(queries, first_block, cached_rows, received, key_rows, values, sink_logits, out_weight):
    rows, cols = queries.shape
    heads = cols // HEAD_DIM
    span = 2 * WINDOW
    width = out_weight.shape[1]
    cost = pl.CostEstimate(
        flops=2 * 2 * rows * span * 2 * HEAD_DIM * heads + 2 * rows * cols * width,
        transcendentals=rows * span * heads,
        bytes_accessed=rows * cols * 2 + out_weight.size * 2 + rows * width * 4
        + 2 * (rows + WINDOW) * key_rows.shape[1] * 2,
    )
    vmem = pl.BlockSpec(memory_space=pltpu.VMEM)
    return pl.pallas_call(
        attention_kernel,
        out_shape=jax.ShapeDtypeStruct((rows, width), jnp.float32),
        in_specs=[pl.BlockSpec(memory_space=pltpu.SMEM)] * 2 + [vmem] * 6,
        out_specs=vmem,
        scratch_shapes=[pltpu.VMEM((rows, cols), jnp.bfloat16)],
        cost_estimate=cost,
    )(sink_logits, first_block, queries, cached_rows, received, key_rows, values, out_weight)


def on_device(
    queries,
    key_rows,
    values,
    cached_rows,
    sink_logits,
    out_weight,
    residual,
    norm_gain,
    expert_in,
    expert_out,
    routes,
    route_gates,
):
    tok_rows = queries.shape[0]
    window_rows = WINDOW
    rim_rows = jnp.stack([key_rows[tok_rows - window_rows :], values[tok_rows - window_rows :]])
    received = shifted(rim_rows, "seq", 1)
    first_block = (lax.axis_index("seq") == 0).astype(jnp.int32).reshape(1)
    partial_rows = attend_kernel(
        queries, first_block, cached_rows, received, key_rows, values, sink_logits, out_weight
    )
    mixed_rows = residual.astype(jnp.float32) + (partial_rows + swap_exp(partial_rows))
    normed = rms_normalize(mixed_rows, norm_gain)

    experts = lax.axis_size("seq")
    width = normed.shape[1]
    capacity = 3 * tok_rows * TOP // (2 * experts)
    half = -(-capacity // 2)
    slots = experts * half
    core = lax.axis_index("exp")
    flat_experts = routes.reshape(-1)
    expert_hits = (flat_experts[:, None] == jnp.arange(experts, dtype=jnp.int32)[None, :]).astype(
        jnp.int32
    )
    slot_rank = jnp.sum(expert_hits * (jnp.cumsum(expert_hits, axis=0) - 1), axis=1)
    local_rank = slot_rank - core * half
    mine = (local_rank >= 0) & (local_rank < half)
    by_shift = experts <= SHIFT_LIMIT
    offset = (flat_experts - lax.axis_index("seq")) % experts if by_shift else flat_experts
    slot_id = jnp.where(mine, offset * half + local_rank, -1)
    slot_iota = jnp.arange(slots, dtype=jnp.int32)
    pick = (slot_id[:, None] == slot_iota[None, :]).astype(jnp.bfloat16)
    select = jnp.max(pick.reshape(tok_rows, TOP, slots), axis=1).T
    outgoing = (
        jnp.dot(select, normed, preferred_element_type=jnp.float32)
        .astype(jnp.bfloat16)
        .reshape(experts, half, width)
    )
    slot_rows = shift_exchange(outgoing, 1) if by_shift else seq_all_to_all(outgoing)
    other_rows = swap_exp(slot_rows)
    own_hidden = expert_hidden(slot_rows.reshape(-1, width), expert_in[0])
    own_hidden, other_rows = lax.optimization_barrier((own_hidden, other_rows))
    other_hidden = expert_hidden(other_rows.reshape(-1, width), expert_in[0])
    their_part = swap_exp(
        jnp.dot(other_hidden, expert_out[0], preferred_element_type=jnp.float32)
        .astype(jnp.bfloat16)
        .reshape(experts, half, width)
    )
    own_part = (
        jnp.dot(own_hidden, expert_out[0], preferred_element_type=jnp.float32)
        .astype(jnp.bfloat16)
        .reshape(experts, half, width)
    )
    result = (own_part.astype(jnp.float32) + their_part.astype(jnp.float32)).astype(jnp.bfloat16)
    returned = shift_exchange(result, -1) if by_shift else seq_all_to_all(result)
    gate_table = jnp.sum(
        pick.reshape(tok_rows, TOP, slots).astype(jnp.float32) * route_gates[:, :, None], axis=1
    )
    gate_high = gate_table.astype(jnp.bfloat16)
    gate_low = (gate_table - gate_high.astype(jnp.float32)).astype(jnp.bfloat16)
    flat_returned = returned.reshape(slots, width)
    weighted = jnp.dot(gate_high, flat_returned, preferred_element_type=jnp.float32) + jnp.dot(
        gate_low, flat_returned, preferred_element_type=jnp.float32
    )
    rounded = weighted.astype(jnp.bfloat16)
    moe = rounded.astype(jnp.float32) + swap_exp(rounded).astype(jnp.float32)
    return (mixed_rows + moe).astype(jnp.bfloat16)


def solution(mesh):
    placed = (
        P(("groups", "seq"), "exp"),
        P(("groups", "seq"), "exp"),
        P(("groups", "seq"), "exp"),
        P(None, "groups", "exp"),
        P("exp"),
        P("exp", None),
        P(("groups", "seq"), None),
        P(),
        P("seq", None, None, "exp"),
        P("seq", "exp", None),
        P(("groups", "seq"), None),
        P(("groups", "seq"), None),
    )
    return jax.shard_map(
        on_device, mesh=mesh, in_specs=placed, out_specs=P(("groups", "seq"), None), check_vma=False
    )
```

```python
import jax
import jax.numpy as jnp
from jax import lax
from jax.experimental import pallas as pl
from jax.experimental.pallas import tpu as pltpu
from jax.sharding import PartitionSpec as P

HEAD_DIM = 64
WINDOW = 128
TOP = 4
SHIFT_LIMIT = 8


GLU_ALPHA = 1.702
EPSILON = 1e-05


def shifted(shard, axis, by):
    size = lax.axis_size(axis)
    pairs = [(i, i + by) for i in range(size) if 0 <= i + by < size]
    return lax.ppermute(shard, axis, pairs)


def swap_exp(x):
    size = lax.axis_size("exp")
    return lax.ppermute(x, "exp", [(i, (i + 1) % size) for i in range(size)])


def seq_all_to_all(blocks):
    return lax.all_to_all(blocks, "seq", split_axis=0, concat_axis=0, tiled=True)


def shift_exchange(blocks, sign):
    size = lax.axis_size("seq")
    out = [blocks[0]]
    for step in range(1, size):
        pairs = [(i, (i + sign * step) % size) for i in range(size)]
        out.append(lax.ppermute(blocks[step], "seq", pairs))
    return jnp.stack(out)


def rms_normalize(mixed_rows, norm_gain):
    mean_square = jnp.mean(mixed_rows * mixed_rows, axis=-1, keepdims=True)
    return (mixed_rows * lax.rsqrt(mean_square + EPSILON) * norm_gain).astype(jnp.bfloat16)


def attend_block(queries, keys_all, values_all, sink_logits, block_rows, window_rows):
    kv_count = keys_all.shape[1] // HEAD_DIM
    group = queries.shape[1] // HEAD_DIM // kv_count
    query_block = queries.reshape(block_rows, kv_count, group, HEAD_DIM)
    key_block = keys_all.reshape(block_rows + window_rows, kv_count, HEAD_DIM)
    value_block = values_all.reshape(block_rows + window_rows, kv_count, HEAD_DIM)
    scores = jnp.einsum(
        "qhgd,khd->hgqk", query_block, key_block, preferred_element_type=jnp.float32
    ) * HEAD_DIM ** (-0.5)
    query_pos = jnp.arange(block_rows)[:, None]
    key_pos = jnp.arange(block_rows + window_rows)[None, :]
    allowed = (key_pos > query_pos) & (key_pos <= query_pos + window_rows)
    scores = jnp.where(allowed, scores, -jnp.inf)
    sink_table = sink_logits.reshape(kv_count, group)[:, :, None]
    largest = jnp.maximum(jnp.max(scores, axis=-1), sink_table)
    weights_exp = jnp.exp(scores - largest[..., None])
    denominator = jnp.exp(sink_table - largest) + jnp.sum(weights_exp, axis=-1)
    probs = (weights_exp / denominator[..., None]).astype(jnp.bfloat16)
    heads_out = jnp.einsum("hgqk,khd->qhgd", probs, value_block, preferred_element_type=jnp.float32)
    return heads_out.astype(jnp.bfloat16).reshape(block_rows, queries.shape[1])


def expert_hidden(rows, expert_in):
    gate_up = jnp.einsum("rd,kdf->krf", rows, expert_in, preferred_element_type=jnp.float32)
    gate_val = gate_up[0]
    up_val = gate_up[1]
    return ((up_val + 1.0) * gate_val * jax.nn.sigmoid(GLU_ALPHA * gate_val)).astype(jnp.bfloat16)


def attention_kernel(
    sink_ref, first_ref, q_ref, cached_ref, recv_k_ref, recv_v_ref, k_ref, v_ref, w_ref, o_ref, heads_ref
):
    rows = q_ref.shape[0]
    prior = cached_ref.shape[1]
    span = 2 * WINDOW
    pair_cols = 2 * HEAD_DIM
    pairs = q_ref.shape[1] // pair_cols
    kv_count = k_ref.shape[1] // HEAD_DIM
    per_kv = pairs // kv_count
    first = first_ref[0] == 1
    prior_keys = jnp.where(first, cached_ref[0], recv_k_ref[...])
    prior_values = jnp.where(first, cached_ref[1], recv_v_ref[...])
    keys_all = jnp.concatenate([prior_keys, k_ref[...]], axis=0)
    values_all = jnp.concatenate([prior_values, v_ref[...]], axis=0)
    q_pos = lax.broadcasted_iota(jnp.int32, (WINDOW, span), 0)
    k_pos = lax.broadcasted_iota(jnp.int32, (WINDOW, span), 1)
    allowed = (k_pos > q_pos) & (k_pos <= q_pos + WINDOW)
    lane_half = lax.broadcasted_iota(jnp.int32, (span, pair_cols), 1) // HEAD_DIM
    for b in range(rows // WINDOW):
        first = b * WINDOW + prior - WINDOW
        key_win = keys_all[first : first + span]
        value_win = values_all[first : first + span]
        swapped_k = pltpu.roll(key_win, HEAD_DIM, 1)
        swapped_v = pltpu.roll(value_win, HEAD_DIM, 1)
        placed = {}
        for kv in range(kv_count):
            for a in range(2):
                src_k = key_win if (kv % 2) == a else swapped_k
                src_v = value_win if (kv % 2) == a else swapped_v
                placed[kv, a] = (
                    jnp.where(lane_half == a, src_k, jnp.zeros_like(src_k)),
                    jnp.where(lane_half == a, src_v, jnp.zeros_like(src_v)),
                )
        for j in range(pairs):
            kv = j // per_kv
            q_pair = q_ref[b * WINDOW : (b + 1) * WINDOW, j * pair_cols : (j + 1) * pair_cols] * HEAD_DIM ** (
                -0.5
            )
            total = None
            for a in range(2):
                k_placed, v_placed = placed[kv, a]
                scores = lax.dot_general(
                    q_pair, k_placed, (((1,), (1,)), ((), ())), preferred_element_type=jnp.float32
                )
                scores = jnp.where(allowed, scores, -jnp.inf)
                sink = sink_ref[2 * j + a]
                largest = jnp.maximum(jnp.max(scores, axis=-1, keepdims=True), sink)
                weights_exp = jnp.exp(scores - largest)
                denominator = jnp.exp(sink - largest) + jnp.sum(weights_exp, axis=-1, keepdims=True)
                probs = (weights_exp * (1.0 / denominator)).astype(jnp.bfloat16)
                out = jnp.dot(probs, v_placed, preferred_element_type=jnp.float32)
                total = out if total is None else total + out
            heads_ref[b * WINDOW : (b + 1) * WINDOW, j * pair_cols : (j + 1) * pair_cols] = total.astype(
                heads_ref.dtype
            )
    o_ref[...] = jnp.dot(heads_ref[...], w_ref[...], preferred_element_type=jnp.float32)


def attend_kernel(queries, first_block, cached_rows, received, key_rows, values, sink_logits, out_weight):
    rows, cols = queries.shape
    heads = cols // HEAD_DIM
    span = 2 * WINDOW
    width = out_weight.shape[1]
    cost = pl.CostEstimate(
        flops=2 * 2 * rows * span * 2 * HEAD_DIM * heads + 2 * rows * cols * width,
        transcendentals=rows * span * heads,
        bytes_accessed=rows * cols * 2 + out_weight.size * 2 + rows * width * 4
        + 2 * (rows + WINDOW) * key_rows.shape[1] * 2,
    )
    vmem = pl.BlockSpec(memory_space=pltpu.VMEM)
    return pl.pallas_call(
        attention_kernel,
        out_shape=jax.ShapeDtypeStruct((rows, width), jnp.float32),
        in_specs=[pl.BlockSpec(memory_space=pltpu.SMEM)] * 2 + [vmem] * 7,
        out_specs=vmem,
        scratch_shapes=[pltpu.VMEM((rows, cols), jnp.bfloat16)],
        cost_estimate=cost,
    )(sink_logits, first_block, queries, cached_rows, *received, key_rows, values, out_weight)


def on_device(
    queries,
    key_rows,
    values,
    cached_rows,
    sink_logits,
    out_weight,
    residual,
    norm_gain,
    expert_in,
    expert_out,
    routes,
    route_gates,
):
    tok_rows = queries.shape[0]
    window_rows = WINDOW
    received = [shifted(rows[tok_rows - window_rows :], "seq", 1) for rows in (key_rows, values)]
    first_block = (lax.axis_index("seq") == 0).astype(jnp.int32).reshape(1)
    partial_rows = attend_kernel(
        queries, first_block, cached_rows, received, key_rows, values, sink_logits, out_weight
    )
    mixed_rows = residual.astype(jnp.float32) + (partial_rows + swap_exp(partial_rows))
    normed = rms_normalize(mixed_rows, norm_gain)

    experts = lax.axis_size("seq")
    width = normed.shape[1]
    capacity = 3 * tok_rows * TOP // (2 * experts)
    half = -(-capacity // 2)
    slots = experts * half
    core = lax.axis_index("exp")
    flat_experts = routes.reshape(-1)
    expert_hits = (flat_experts[:, None] == jnp.arange(experts, dtype=jnp.int32)[None, :]).astype(
        jnp.int32
    )
    slot_rank = jnp.sum(expert_hits * (jnp.cumsum(expert_hits, axis=0) - 1), axis=1)
    local_rank = slot_rank - core * half
    mine = (local_rank >= 0) & (local_rank < half)
    by_shift = experts <= SHIFT_LIMIT
    offset = (flat_experts - lax.axis_index("seq")) % experts if by_shift else flat_experts
    slot_id = jnp.where(mine, offset * half + local_rank, -1)
    slot_iota = jnp.arange(slots, dtype=jnp.int32)
    pick = (slot_id[:, None] == slot_iota[None, :]).astype(jnp.bfloat16)
    select = jnp.max(pick.reshape(tok_rows, TOP, slots), axis=1).T
    outgoing = (
        jnp.dot(select, normed, preferred_element_type=jnp.float32)
        .astype(jnp.bfloat16)
        .reshape(experts, half, width)
    )
    slot_rows = shift_exchange(outgoing, 1) if by_shift else seq_all_to_all(outgoing)
    other_rows = swap_exp(slot_rows)
    own_hidden = expert_hidden(slot_rows.reshape(-1, width), expert_in[0])
    own_hidden, other_rows = lax.optimization_barrier((own_hidden, other_rows))
    other_hidden = expert_hidden(other_rows.reshape(-1, width), expert_in[0])
    their_part = swap_exp(
        jnp.dot(other_hidden, expert_out[0], preferred_element_type=jnp.float32)
        .astype(jnp.bfloat16)
        .reshape(experts, half, width)
    )
    own_part = (
        jnp.dot(own_hidden, expert_out[0], preferred_element_type=jnp.float32)
        .astype(jnp.bfloat16)
        .reshape(experts, half, width)
    )
    result = (own_part.astype(jnp.float32) + their_part.astype(jnp.float32)).astype(jnp.bfloat16)
    returned = shift_exchange(result, -1) if by_shift else seq_all_to_all(result)
    gate_table = jnp.sum(
        pick.reshape(tok_rows, TOP, slots).astype(jnp.float32) * route_gates[:, :, None], axis=1
    )
    gate_high = gate_table.astype(jnp.bfloat16)
    gate_low = (gate_table - gate_high.astype(jnp.float32)).astype(jnp.bfloat16)
    flat_returned = returned.reshape(slots, width)
    weighted = jnp.dot(gate_high, flat_returned, preferred_element_type=jnp.float32) + jnp.dot(
        gate_low, flat_returned, preferred_element_type=jnp.float32
    )
    rounded = weighted.astype(jnp.bfloat16)
    moe = rounded.astype(jnp.float32) + swap_exp(rounded).astype(jnp.float32)
    return (mixed_rows + moe).astype(jnp.bfloat16)


def solution(mesh):
    placed = (
        P(("groups", "seq"), "exp"),
        P(("groups", "seq"), "exp"),
        P(("groups", "seq"), "exp"),
        P(None, "groups", "exp"),
        P("exp"),
        P("exp", None),
        P(("groups", "seq"), None),
        P(),
        P("seq", None, None, "exp"),
        P("seq", "exp", None),
        P(("groups", "seq"), None),
        P(("groups", "seq"), None),
    )
    return jax.shard_map(
        on_device, mesh=mesh, in_specs=placed, out_specs=P(("groups", "seq"), None), check_vma=False
    )
```
